128 devices in a mesh: pipe: 8 (over z, core), ctx: 16 (over y, x).
Axes of the slice: x: 4, y: 4, z: 4, core: 2. Of those that a mesh axis runs over, the one named last changes fastest.
Arguments:
- grad_in: bfloat16 [8, 4096, 8192], P('pipe', 'ctx'), may hold values from -6 to 6
- query: bfloat16 [8, 4096, 512], P('pipe', 'ctx'), may hold values from -8 to 8
- keyval: bfloat16 [8, 4096, 256], P('pipe', 'ctx'), may hold values from -8 to 8
- w_qkv: bfloat16 [8, 8192, 768], P('pipe', 'ctx'), may hold values from -0.0625 to 0.0625
- w_out: bfloat16 [8, 8192, 512], P('pipe', 'ctx'), may hold values from -0.25 to 0.25
- doc_lengths: int32 [8, 8], P('pipe'), may hold values from 1 to 2048, 4096 in all within a row
- order: int32 [8, 32], P('pipe'), may hold values from 0 to 31, as said below
Outputs:
- passed_grad: bfloat16 [8, 4096, 8192], P('pipe', 'ctx')
The draws below stay inside these ranges and needn't reach their ends.
Inputs may be any that keep to these rules, and one draw needn't show every extreme that they name: Each row of order is a permutation of 0 to 31; entry d * 2 + k (device d's stored slot k, k < 2) names one of the sequence blocks e * 2 to e * 2 + 1 of device e = (d + k * 8) mod 16. `doc_lengths`: each row sums to 4096 and its largest entry is 2048.
All inputs are finite; a program needn't handle non-finite values.
Results may differ from the reference program's by a relative error of at most 0.015.
Values may be sent and summed in bfloat16 or wider, within the bound.
No kernel may reach another device: no remote copies, remote signals or barrier semaphores. Data moves between devices by JAX's collectives and lax.ppermute only.
A program may use at most 128 MiB of HBM per device.

```python
import math
import jax
import jax.numpy as jnp
import numpy as np
from jax import lax

D = 8192
HD = 128
GROUP = 4
DOCS = 8
SECTIONS = 8
SEQ = 4096
BLOCKS_DEV = 2
NBLK = 32
DOC_MOST = 2048


def stored_rows(key):
    base_key = jax.random.fold_in(key, 17)
    subkeys = jax.random.split(base_key, 3)
    query_shape = (SECTIONS, SEQ, GROUP, HD)
    array_shape = (SECTIONS, SEQ, HD)
    queries = jnp.clip(jax.random.normal(subkeys[0], query_shape, jnp.float32), -4.0, 4.0)
    key_rows = jnp.clip(jax.random.normal(subkeys[1], array_shape, jnp.float32), -4.0, 4.0)
    values = jnp.clip(jax.random.normal(subkeys[2], array_shape, jnp.float32), -4.0, 4.0)
    return (queries.reshape(SECTIONS, SEQ, GROUP * HD), jnp.concatenate([key_rows, values], axis=2))


def draw_query(key, part):
    return stored_rows(key)[0].astype(jnp.bfloat16)


def draw_keyval(key, part):
    return stored_rows(key)[1].astype(jnp.bfloat16)


def local_permutation(block_key):
    return jax.random.permutation(block_key, BLOCKS_DEV)


def draw_order(key, part):
    base_key = jax.random.fold_in(key, 29)
    devices = NBLK // BLOCKS_DEV

    def one_section(section_key):
        local_order = jax.vmap(local_permutation)(jax.random.split(section_key, devices)).astype(jnp.int32)
        owner_ids = jnp.arange(devices, dtype=jnp.int32)[:, None]
        slot_ids = jnp.arange(BLOCKS_DEV, dtype=jnp.int32)[None, :]
        offsets = slot_ids * devices // BLOCKS_DEV
        holder = (owner_ids - offsets) % devices
        slot_index = (holder * BLOCKS_DEV + slot_ids).reshape(-1)
        block_ids = (owner_ids * BLOCKS_DEV + local_order).reshape(-1)
        return jnp.zeros((NBLK,), jnp.int32).at[slot_index].set(block_ids)
    return jax.vmap(one_section)(jax.random.split(base_key, SECTIONS)).astype(jnp.int32)


def block_scale(key, dims, pieces, least, largest):
    def one(position, blocks):
        draws = jax.random.uniform(jax.random.fold_in(jax.random.fold_in(key, 6), position), (blocks,), jnp.float32, least / len(pieces), largest / len(pieces))
        return jnp.repeat(jnp.exp(draws), dims[position] // blocks).reshape((-1,) + (1,) * (len(dims) - position - 1))

    gain = one(*pieces[0])
    for cut in pieces[1:]:
        gain = gain * one(*cut)
    return gain


def profile(count, total, most, slope):
    loads = [(1 << 20) // math.isqrt(rank ** slope) + 1 for rank in range(2, count + 1)]
    surplus, holding = total - most - (count - 1), [1] * (count - 1)
    while surplus > 0:
        free = [i for i in range(count - 1) if holding[i] < most]
        mass, left = sum([loads[i] for i in free]), surplus
        for i in free:
            addition = min(most - holding[i], max(1, left * loads[i] // mass), surplus)
            holding[i] = holding[i] + addition
            surplus = surplus - addition
    return np.array([most] + holding)


def ragged(own_key, amount, total, reach, skew):
    if amount == 2:
        one = jax.random.randint(own_key, (), max(1, total - reach), min(reach, total - 1) + 1)
        return jnp.stack([one, total - one])
    tallies = jnp.asarray(profile(amount, total, reach, skew), jnp.int32)
    pairs = (amount - 1) // 2
    source_of, receiver = tallies[1:1 + 2 * pairs:2], tallies[2:2 + 2 * pairs:2]
    room = jnp.minimum(source_of - 1, reach - receiver)
    shifted = jax.random.randint(jax.random.fold_in(own_key, 1), (pairs,), 0, 1 << 20) % (room + 1)
    tallies = tallies.at[1:1 + 2 * pairs:2].set(source_of - shifted).at[2:2 + 2 * pairs:2].set(receiver + shifted)
    return tallies[jax.random.permutation(jax.random.fold_in(own_key, 2), amount)]


def noise(stream_key, dims, width, bound, cuts=(), kind=jnp.bfloat16):
    entries = jax.random.normal(stream_key, dims, jnp.float32) * width
    if len(cuts) > 0:
        entries = block_scale(stream_key, dims, cuts, -0.22, 0.18) * entries
    return jnp.clip(entries, min=-bound, max=bound).astype(kind)


def setup_inputs(seed: int = 0) -> dict:
    key_of = jax.random.split(jax.random.key(seed), 8)
    return {
        "grad_in": noise(key_of[0], (SECTIONS, SEQ, D), 1.0, 6.0, ((0, 8), (1, 16))),
        "query": draw_query(jax.random.fold_in(key_of[7], 71), 0),
        "keyval": draw_keyval(jax.random.fold_in(key_of[7], 71), 0),
        "w_qkv": noise(key_of[3], (SECTIONS, D, (GROUP + 2) * HD), D ** -0.5, 0.0625, ((0, 8), (1, 16))),
        "w_out": noise(key_of[4], (SECTIONS, D, GROUP * HD), (GROUP * HD) ** -0.5, 0.25, ((0, 8), (1, 16))),
        "doc_lengths": jax.vmap(lambda own: ragged(own, DOCS, SEQ, DOC_MOST, 2))(jax.random.split(key_of[5], SECTIONS)).reshape((SECTIONS, DOCS)).astype(jnp.int32),
        "order": draw_order(jax.random.fold_in(key_of[7], 71), 0),
    }


ROPE_BASE = 500000.0

def rope_tables(positions, head_dim):
    half_width = head_dim // 2
    inv_freq = ROPE_BASE ** (-(jnp.arange(half_width, dtype=jnp.float32) * 2.0 / head_dim))
    angles = positions.astype(jnp.float32)[:, None] * inv_freq[None, :]
    angles = jnp.concatenate([angles, angles], axis=1)
    return (jnp.cos(angles), jnp.sin(angles))

def unrotate(gradient, positions):
    cosine, sine_table = rope_tables(positions, gradient.shape[1])
    half_width = gradient.shape[1] // 2
    turned = jnp.concatenate([-gradient[:, half_width:], gradient[:, :half_width]], axis=1)
    return gradient * cosine - turned * sine_table

def doc_ids(positions, lengths):
    doc_ends = jnp.cumsum(lengths)[:-1]
    return lax.optimization_barrier(jnp.sum((positions[:, None] >= doc_ends[None, :]).astype(jnp.int32), axis=1))

def section_backward(arrays):
    section_grad_in, stored_query, stored_keyval, in_weight, out_weight, lengths, block_order = arrays
    seq_len = section_grad_in.shape[0]
    head_dim = stored_keyval.shape[1] // 2
    group = stored_query.shape[1] // head_dim
    block_count = block_order.shape[0]
    block_rows = seq_len // block_count
    inverse = jnp.argsort(block_order).astype(jnp.int32)
    queries = stored_query.reshape(block_count, block_rows, group * head_dim)[inverse].reshape(seq_len, group * head_dim)
    pairs = stored_keyval.reshape(block_count, block_rows, 2 * head_dim)[inverse].reshape(seq_len, 2 * head_dim)
    key_rows = pairs[:, :head_dim]
    value_rows = pairs[:, head_dim:]
    value_wide = value_rows.astype(jnp.float32)
    out_grad = jnp.dot(section_grad_in, out_weight, preferred_element_type=jnp.float32).astype(jnp.bfloat16)
    flat_query = queries.reshape(seq_len * group, head_dim)
    flat_grad = out_grad.reshape(seq_len * group, head_dim)
    positions = jnp.arange(seq_len, dtype=jnp.int32)
    doc_table = doc_ids(positions, lengths)
    flat_pos = jnp.repeat(positions, group)
    flat_doc = jnp.repeat(doc_table, group)
    query_block = math.gcd(seq_len * group, 512)
    score_scale = 1.0 / math.sqrt(head_dim)

    def one_block(carried, block_index):
        start_row = block_index * query_block
        query_rows = lax.dynamic_slice_in_dim(flat_query, start_row, query_block)
        grad_rows = lax.dynamic_slice_in_dim(flat_grad, start_row, query_block)
        query_pos = lax.dynamic_slice_in_dim(flat_pos, start_row, query_block)
        query_doc = lax.dynamic_slice_in_dim(flat_doc, start_row, query_block)
        visible = (query_doc[:, None] == doc_table[None, :]) & (positions[None, :] <= query_pos[:, None])
        scores = jnp.dot(query_rows, key_rows.T, preferred_element_type=jnp.float32) * score_scale
        row_top = lax.optimization_barrier(jnp.max(jnp.where(visible, scores, -jnp.inf), axis=1))
        row_total = lax.optimization_barrier(jnp.sum(jnp.where(visible, jnp.exp(scores - row_top[:, None]), 0.0), axis=1))
        log_total = row_top + jnp.log(row_total)
        attn_prob = jnp.where(visible, jnp.exp(scores - log_total[:, None]), 0.0)
        attn_out = jnp.dot(attn_prob, value_wide, precision=lax.Precision.HIGHEST)
        row_delta = lax.optimization_barrier(jnp.sum(grad_rows.astype(jnp.float32) * attn_out, axis=1))
        prob_grad = jnp.dot(grad_rows, value_rows.T, preferred_element_type=jnp.float32)
        score_grad = (score_scale * attn_prob * (prob_grad - row_delta[:, None])).astype(jnp.bfloat16)
        prob16 = attn_prob.astype(jnp.bfloat16)
        query_grad = jnp.dot(score_grad, key_rows, preferred_element_type=jnp.float32)
        key_sum = carried[0] + jnp.dot(score_grad.T, query_rows, preferred_element_type=jnp.float32)
        value_sum = carried[1] + jnp.dot(prob16.T, grad_rows, preferred_element_type=jnp.float32)
        return ((key_sum, value_sum), query_grad)
    empty_sum = jnp.zeros((seq_len, head_dim), jnp.float32)
    steps_count = seq_len * group // query_block
    (key_sum, value_sum), query_grad = lax.scan(one_block, (empty_sum, empty_sum), jnp.arange(steps_count, dtype=jnp.int32))
    query_grad = query_grad.reshape(seq_len * group, head_dim)
    query_part = unrotate(query_grad, flat_pos).reshape(seq_len, group * head_dim)
    qkv_grad = jnp.concatenate([query_part, unrotate(key_sum, positions), value_sum], axis=1).astype(jnp.bfloat16)
    combined = section_grad_in.astype(jnp.float32) + lax.dot_general(qkv_grad, in_weight, (((1,), (1,)), ((), ())), preferred_element_type=jnp.float32)
    return combined.astype(jnp.bfloat16)

def reference(grad_in, query, keyval, w_qkv, w_out, doc_lengths, order):
    section_grads = lax.map(section_backward, (grad_in, query, keyval, w_qkv, w_out, doc_lengths, order))
    return jnp.concatenate([section_grads[1:], jnp.zeros_like(section_grads[:1])], axis=0)
```

```python
import math

import jax
import jax.numpy as jnp
from jax import lax
from jax.sharding import PartitionSpec as P

BLOCK = 128


ROPE_BASE = 500000.0
MASKED = -1e30


def passed_along(value, axis, steps):
    count = lax.axis_size(axis)
    pairs = [(source, (source + steps) % count) for source in range(count)]
    return lax.ppermute(value, axis, pairs)


def passed_along_2(value, axis, by):
    size = lax.axis_size(axis)
    pairs = [(i, i + by) for i in range(size) if 0 <= i + by < size]
    return lax.ppermute(value, axis, pairs)


def gathered_rows(value, axis):
    count = lax.axis_size(axis)
    spread = jnp.broadcast_to(value[None], (count,) + value.shape)
    return lax.all_to_all(spread, axis, 0, 0, tiled=False).reshape((-1,) + value.shape[1:])


def summed_rows(value, axis):
    count = lax.axis_size(axis)
    pieces = lax.all_to_all(value.reshape((count, -1) + value.shape[1:]), axis, 0, 0, tiled=False)
    return jnp.sum(pieces.astype(jnp.float32), axis=0)


def rope_tables(positions, head_dim):
    half_width = head_dim // 2
    inv_freq = ROPE_BASE ** (-(jnp.arange(half_width, dtype=jnp.float32) * 2.0 / head_dim))
    angles = positions.astype(jnp.float32)[:, None] * inv_freq[None, :]
    angles = jnp.concatenate([angles, angles], axis=1)
    return (jnp.cos(angles), jnp.sin(angles))


def unrotate(gradient, positions):
    cosine, sine_table = rope_tables(positions, gradient.shape[1])
    half_width = gradient.shape[1] // 2
    turned = jnp.concatenate([-gradient[:, half_width:], gradient[:, :half_width]], axis=1)
    return gradient * cosine - turned * sine_table


def doc_ids(positions, lengths):
    doc_ends = jnp.cumsum(lengths)[:-1]
    return jnp.sum((positions[:, None] >= doc_ends[None, :]).astype(jnp.int32), axis=1)


def seq_to_stored(rows, block_order, device, ctx_size, per_device):
    width = rows.shape[1]
    first_block = device * per_device
    blocks = rows.reshape(per_device, BLOCK, width)
    pieces = []
    for slot_k in range(per_device):
        offset = slot_k * ctx_size // per_device
        slot_at = (device - offset) % ctx_size * per_device + slot_k
        local_index = block_order[slot_at] - first_block
        chosen = lax.dynamic_index_in_dim(blocks, local_index, 0, keepdims=False)
        if slot_k > 0:
            chosen = passed_along(chosen, "ctx", -offset)
        pieces.append(chosen)
    return jnp.concatenate(pieces, axis=0)


def stored_to_seq(rows, block_order, device, ctx_size, per_device):
    width = rows.shape[1]
    first_block = device * per_device
    blocks = rows.reshape(per_device, BLOCK, width)
    pieces = []
    local_ids = []
    for slot_k in range(per_device):
        offset = slot_k * ctx_size // per_device
        piece = blocks[slot_k]
        if slot_k > 0:
            piece = passed_along(piece, "ctx", offset)
        pieces.append(piece)
        sender_slot = (device - offset) % ctx_size * per_device + slot_k
        local_ids.append(block_order[sender_slot] - first_block)
    stacked = jnp.stack(pieces)
    index_list = jnp.stack(local_ids)
    choose = (jnp.arange(per_device, dtype=jnp.int32)[:, None] == index_list[None, :]).astype(
        rows.dtype
    )
    placed = jnp.einsum("pk,kbw->pbw", choose, stacked, preferred_element_type=jnp.float32)
    return placed.astype(rows.dtype).reshape(-1, width)


def contract_rows(left_rows, right_rows):
    return lax.dot_general(
        left_rows, right_rows, (((0,), (0,)), ((), ())), preferred_element_type=jnp.float32
    )


def contract_cols(left_rows, right_rows):
    return lax.dot_general(
        left_rows, right_rows, (((1,), (1,)), ((), ())), preferred_element_type=jnp.float32
    )


def block_scores(query_rows, key_rows, query_pos, query_doc, key_pos, key_doc, score_scale):
    scores = contract_cols(query_rows, key_rows) * score_scale
    visible = (query_doc[:, None] == key_doc[None, :]) & (key_pos[None, :] <= query_pos[:, None])
    return (scores, visible)


def body(grad_in, query, keyval, w_qkv, w_out, doc_lengths, order):
    section_grad_in = grad_in[0]
    stored_query = query[0]
    stored_keyval = keyval[0]
    in_weight = w_qkv[0]
    out_weight = w_out[0]
    lengths = doc_lengths[0]
    block_order = order[0]
    ctx_size = lax.axis_size("ctx")
    device = lax.axis_index("ctx")
    local_rows = section_grad_in.shape[0]
    head_dim = stored_keyval.shape[1] // 2
    group = stored_query.shape[1] // head_dim
    per_device = local_rows // BLOCK
    block_count = block_order.shape[0]
    seq_len = local_rows * ctx_size
    first_row = device * local_rows
    score_scale = 1.0 / math.sqrt(head_dim)
    key_block = math.gcd(seq_len, 512)
    key_steps = seq_len // key_block
    within = jnp.arange(BLOCK, dtype=jnp.int32)
    next_grad_in = passed_along_2(section_grad_in, "pipe", -1)
    next_weight = lax.all_gather(passed_along_2(in_weight, "pipe", -1), "ctx", axis=0, tiled=True)
    out_grad = jnp.dot(
        section_grad_in,
        lax.all_gather(out_weight, "ctx", axis=0, tiled=True),
        preferred_element_type=jnp.float32,
    ).astype(jnp.bfloat16)
    local_out_grad = seq_to_stored(out_grad, block_order, device, ctx_size, per_device)
    query_positions = (block_order[:, None] * BLOCK + within[None, :]).reshape(-1)
    gathered = gathered_rows(stored_keyval, "ctx")
    slot_ids = jnp.arange(block_count, dtype=jnp.int32)
    inverse = jnp.sum(
        jnp.where(block_order[None, :] == slot_ids[:, None], slot_ids[None, :], 0), axis=1
    )
    all_keyval = gathered.reshape(block_count, BLOCK, 2 * head_dim)[inverse].reshape(
        seq_len, 2 * head_dim
    )
    key_positions = jnp.arange(seq_len, dtype=jnp.int32)
    key_docs = doc_ids(key_positions, lengths)
    query_pos = lax.dynamic_slice_in_dim(query_positions, first_row, local_rows)
    query_doc = doc_ids(query_pos, lengths)
    flat_rows = local_rows * group
    flat_query = stored_query.reshape(flat_rows, head_dim)
    flat_grad = local_out_grad.reshape(flat_rows, head_dim)
    flat_pos = jnp.repeat(query_pos, group)
    flat_doc = jnp.repeat(query_doc, group)
    key_blocks = (
        all_keyval.reshape(key_steps, key_block, 2 * head_dim),
        key_positions.reshape(key_steps, key_block),
        key_docs.reshape(key_steps, key_block),
    )

    def running_total(carried, current):
        row_top, row_total, weighted = carried
        pair_rows, key_pos, key_doc = current
        scores, visible = block_scores(
            flat_query, pair_rows[:, :head_dim], flat_pos, flat_doc, key_pos, key_doc, score_scale
        )
        new_top = jnp.maximum(row_top, jnp.max(jnp.where(visible, scores, MASKED), axis=1))
        rescale = jnp.exp(row_top - new_top)
        weights = jnp.where(visible, jnp.exp(scores - new_top[:, None]), 0.0)
        row_total = row_total * rescale + jnp.sum(weights, axis=1)
        value_wide = pair_rows[:, head_dim:].astype(jnp.float32)
        weighted = weighted * rescale[:, None] + jnp.dot(
            weights, value_wide, precision=lax.Precision.HIGHEST
        )
        return ((new_top, row_total, weighted), None)

    start_top = jnp.full((flat_rows,), MASKED, jnp.float32)
    start_carry = (
        start_top,
        jnp.zeros((flat_rows,), jnp.float32),
        jnp.zeros((flat_rows, head_dim), jnp.float32),
    )
    (row_top, row_total, weighted), unused = lax.scan(running_total, start_carry, key_blocks)
    log_total = row_top + jnp.log(row_total)
    attn_out = weighted / row_total[:, None]
    row_delta = jnp.sum(flat_grad.astype(jnp.float32) * attn_out, axis=1)

    def grad_step(summed, current):
        pair_rows, key_pos, key_doc = current
        scores, visible = block_scores(
            flat_query, pair_rows[:, :head_dim], flat_pos, flat_doc, key_pos, key_doc, score_scale
        )
        attn_prob = jnp.where(visible, jnp.exp(scores - log_total[:, None]), 0.0)
        prob_grad = contract_cols(flat_grad, pair_rows[:, head_dim:])
        score_grad = (score_scale * attn_prob * (prob_grad - row_delta[:, None])).astype(
            jnp.bfloat16
        )
        summed = summed + jnp.dot(
            score_grad, pair_rows[:, :head_dim], preferred_element_type=jnp.float32
        )
        key_term = contract_rows(score_grad, flat_query)
        value_term = contract_rows(attn_prob.astype(jnp.bfloat16), flat_grad)
        return (summed, jnp.concatenate([key_term, value_term], axis=1))

    query_grad_rot, key_terms = lax.scan(
        grad_step, jnp.zeros((flat_rows, head_dim), jnp.float32), key_blocks
    )
    own_positions = first_row + jnp.arange(local_rows, dtype=jnp.int32)
    keyval_grad = summed_rows(
        key_terms.reshape(seq_len, 2 * head_dim).astype(jnp.bfloat16), "ctx"
    )
    query_grad = (
        unrotate(query_grad_rot, flat_pos)
        .reshape(local_rows, group * head_dim)
        .astype(jnp.bfloat16)
    )
    query_grad = stored_to_seq(query_grad, block_order, device, ctx_size, per_device)
    key_grad = unrotate(keyval_grad[:, :head_dim], own_positions).astype(jnp.bfloat16)
    value_grad = keyval_grad[:, head_dim:].astype(jnp.bfloat16)
    qkv_grad = jnp.concatenate([query_grad, key_grad, value_grad], axis=1)
    next_qkv_grad = passed_along_2(qkv_grad, "pipe", -1)
    projected = contract_cols(next_qkv_grad, next_weight)
    passed = (next_grad_in.astype(jnp.float32) + projected).astype(jnp.bfloat16)
    return passed[None]


def solution(mesh):
    return jax.shard_map(
        body,
        mesh=mesh,
        in_specs=(
            P("pipe", "ctx", None),
            P("pipe", "ctx", None),
            P("pipe", "ctx", None),
            P("pipe", "ctx", None),
            P("pipe", "ctx", None),
            P("pipe", None),
            P("pipe", None),
        ),
        out_specs=P("pipe", "ctx", None),
        check_vma=False,
    )
```

```python
import math

import jax
import jax.numpy as jnp
from jax import lax
from jax.sharding import PartitionSpec as P

BLOCK = 128


ROPE_BASE = 500000.0
MASKED = -1e30


def passed_along(value, axis, steps):
    count = lax.axis_size(axis)
    pairs = [(source, (source + steps) % count) for source in range(count)]
    return lax.ppermute(value, axis, pairs)


def passed_along_2(value, axis, by):
    size = lax.axis_size(axis)
    pairs = [(i, i + by) for i in range(size) if 0 <= i + by < size]
    return lax.ppermute(value, axis, pairs)


def gathered_rows(value, axis):
    count = lax.axis_size(axis)
    spread = jnp.broadcast_to(value[None], (count,) + value.shape)
    return lax.all_to_all(spread, axis, 0, 0, tiled=False).reshape((-1,) + value.shape[1:])


def summed_rows(value, axis):
    count = lax.axis_size(axis)
    pieces = lax.all_to_all(value.reshape((count, -1) + value.shape[1:]), axis, 0, 0, tiled=False)
    return jnp.sum(pieces.astype(jnp.float32), axis=0)


def rope_tables(positions, head_dim):
    half_width = head_dim // 2
    inv_freq = ROPE_BASE ** (-(jnp.arange(half_width, dtype=jnp.float32) * 2.0 / head_dim))
    angles = positions.astype(jnp.float32)[:, None] * inv_freq[None, :]
    angles = jnp.concatenate([angles, angles], axis=1)
    return (jnp.cos(angles), jnp.sin(angles))


def unrotate(gradient, positions):
    cosine, sine_table = rope_tables(positions, gradient.shape[1])
    half_width = gradient.shape[1] // 2
    turned = jnp.concatenate([-gradient[:, half_width:], gradient[:, :half_width]], axis=1)
    return gradient * cosine - turned * sine_table


def doc_ids(positions, lengths):
    doc_ends = jnp.cumsum(lengths)[:-1]
    return jnp.sum((positions[:, None] >= doc_ends[None, :]).astype(jnp.int32), axis=1)


def seq_to_stored(rows, block_order, device, ctx_size, per_device):
    width = rows.shape[1]
    first_block = device * per_device
    blocks = rows.reshape(per_device, BLOCK, width)
    pieces = []
    for slot_k in range(per_device):
        offset = slot_k * ctx_size // per_device
        slot_at = (device - offset) % ctx_size * per_device + slot_k
        local_index = block_order[slot_at] - first_block
        chosen = lax.dynamic_index_in_dim(blocks, local_index, 0, keepdims=False)
        if slot_k > 0:
            chosen = passed_along(chosen, "ctx", -offset)
        pieces.append(chosen)
    return jnp.concatenate(pieces, axis=0)


def stored_to_seq(rows, block_order, device, ctx_size, per_device):
    width = rows.shape[1]
    first_block = device * per_device
    blocks = rows.reshape(per_device, BLOCK, width)
    pieces = []
    local_ids = []
    for slot_k in range(per_device):
        offset = slot_k * ctx_size // per_device
        piece = blocks[slot_k]
        if slot_k > 0:
            piece = passed_along(piece, "ctx", offset)
        pieces.append(piece)
        sender_slot = (device - offset) % ctx_size * per_device + slot_k
        local_ids.append(block_order[sender_slot] - first_block)
    stacked = jnp.stack(pieces)
    index_list = jnp.stack(local_ids)
    choose = (jnp.arange(per_device, dtype=jnp.int32)[:, None] == index_list[None, :]).astype(
        rows.dtype
    )
    placed = jnp.einsum("pk,kbw->pbw", choose, stacked, preferred_element_type=jnp.float32)
    return placed.astype(rows.dtype).reshape(-1, width)


def contract_rows(left_rows, right_rows):
    return lax.dot_general(
        left_rows, right_rows, (((0,), (0,)), ((), ())), preferred_element_type=jnp.float32
    )


def contract_cols(left_rows, right_rows):
    return lax.dot_general(
        left_rows, right_rows, (((1,), (1,)), ((), ())), preferred_element_type=jnp.float32
    )


def block_scores(query_rows, key_rows, query_pos, query_doc, key_pos, key_doc, score_scale):
    scores = contract_cols(query_rows, key_rows) * score_scale
    visible = (query_doc[:, None] == key_doc[None, :]) & (key_pos[None, :] <= query_pos[:, None])
    return (scores, visible)


def body(grad_in, query, keyval, w_qkv, w_out, doc_lengths, order):
    section_grad_in = grad_in[0]
    stored_query = query[0]
    stored_keyval = keyval[0]
    in_weight = w_qkv[0]
    out_weight = w_out[0]
    lengths = doc_lengths[0]
    block_order = order[0]
    ctx_size = lax.axis_size("ctx")
    device = lax.axis_index("ctx")
    local_rows = section_grad_in.shape[0]
    head_dim = stored_keyval.shape[1] // 2
    group = stored_query.shape[1] // head_dim
    per_device = local_rows // BLOCK
    block_count = block_order.shape[0]
    seq_len = local_rows * ctx_size
    first_row = device * local_rows
    score_scale = 1.0 / math.sqrt(head_dim)
    key_block = math.gcd(seq_len, 512)
    key_steps = seq_len // key_block
    within = jnp.arange(BLOCK, dtype=jnp.int32)
    query_width = stored_query.shape[1]
    next_shard = passed_along_2(in_weight, "pipe", -1)
    next_grad_in = passed_along_2(section_grad_in, "pipe", -1)
    out_grad = jnp.dot(
        section_grad_in,
        lax.all_gather(out_weight, "ctx", axis=0, tiled=True),
        preferred_element_type=jnp.float32,
    ).astype(jnp.bfloat16)
    local_out_grad = seq_to_stored(out_grad, block_order, device, ctx_size, per_device)
    query_positions = (block_order[:, None] * BLOCK + within[None, :]).reshape(-1)
    gathered = gathered_rows(stored_keyval, "ctx")
    slot_ids = jnp.arange(block_count, dtype=jnp.int32)
    inverse = jnp.sum(
        jnp.where(block_order[None, :] == slot_ids[:, None], slot_ids[None, :], 0), axis=1
    )
    all_keyval = gathered.reshape(block_count, BLOCK, 2 * head_dim)[inverse].reshape(
        seq_len, 2 * head_dim
    )
    key_positions = jnp.arange(seq_len, dtype=jnp.int32)
    key_docs = doc_ids(key_positions, lengths)
    query_pos = lax.dynamic_slice_in_dim(query_positions, first_row, local_rows)
    query_doc = doc_ids(query_pos, lengths)
    flat_rows = local_rows * group
    flat_query = stored_query.reshape(flat_rows, head_dim)
    flat_grad = local_out_grad.reshape(flat_rows, head_dim)
    flat_pos = jnp.repeat(query_pos, group)
    flat_doc = jnp.repeat(query_doc, group)
    key_blocks = (
        all_keyval.reshape(key_steps, key_block, 2 * head_dim),
        key_positions.reshape(key_steps, key_block),
        key_docs.reshape(key_steps, key_block),
    )

    def running_total(carried, current):
        row_top, row_total, weighted = carried
        pair_rows, key_pos, key_doc = current
        scores, visible = block_scores(
            flat_query, pair_rows[:, :head_dim], flat_pos, flat_doc, key_pos, key_doc, score_scale
        )
        new_top = jnp.maximum(row_top, jnp.max(jnp.where(visible, scores, MASKED), axis=1))
        rescale = jnp.exp(row_top - new_top)
        weights = jnp.where(visible, jnp.exp(scores - new_top[:, None]), 0.0)
        row_total = row_total * rescale + jnp.sum(weights, axis=1)
        value_wide = pair_rows[:, head_dim:].astype(jnp.float32)
        weighted = weighted * rescale[:, None] + jnp.dot(
            weights, value_wide, precision=lax.Precision.HIGHEST
        )
        return ((new_top, row_total, weighted), None)

    start_top = jnp.full((flat_rows,), MASKED, jnp.float32)
    start_carry = (
        start_top,
        jnp.zeros((flat_rows,), jnp.float32),
        jnp.zeros((flat_rows, head_dim), jnp.float32),
    )
    (row_top, row_total, weighted), unused = lax.scan(running_total, start_carry, key_blocks)
    next_shard, weighted = lax.optimization_barrier((next_shard, weighted))
    next_weight = lax.all_gather(next_shard, "ctx", axis=0, tiled=True)
    log_total = row_top + jnp.log(row_total)
    attn_out = weighted / row_total[:, None]
    row_delta = jnp.sum(flat_grad.astype(jnp.float32) * attn_out, axis=1)

    def grad_step(summed, current):
        pair_rows, key_pos, key_doc = current
        scores, visible = block_scores(
            flat_query, pair_rows[:, :head_dim], flat_pos, flat_doc, key_pos, key_doc, score_scale
        )
        attn_prob = jnp.where(visible, jnp.exp(scores - log_total[:, None]), 0.0)
        prob_grad = contract_cols(flat_grad, pair_rows[:, head_dim:])
        score_grad = (score_scale * attn_prob * (prob_grad - row_delta[:, None])).astype(
            jnp.bfloat16
        )
        summed = summed + jnp.dot(
            score_grad, pair_rows[:, :head_dim], preferred_element_type=jnp.float32
        )
        key_term = contract_rows(score_grad, flat_query)
        value_term = contract_rows(attn_prob.astype(jnp.bfloat16), flat_grad)
        return (summed, jnp.concatenate([key_term, value_term], axis=1))

    query_grad_rot, key_terms = lax.scan(
        grad_step, jnp.zeros((flat_rows, head_dim), jnp.float32), key_blocks
    )
    own_positions = first_row + jnp.arange(local_rows, dtype=jnp.int32)
    query_grad = (
        unrotate(query_grad_rot, flat_pos)
        .reshape(local_rows, group * head_dim)
        .astype(jnp.bfloat16)
    )
    query_grad = stored_to_seq(query_grad, block_order, device, ctx_size, per_device)
    next_query_grad = passed_along_2(query_grad, "pipe", -1)
    partial = lax.optimization_barrier(
        next_grad_in.astype(jnp.float32)
        + contract_cols(next_query_grad, next_weight[:, :query_width])
    )
    keyval_grad = summed_rows(
        key_terms.reshape(seq_len, 2 * head_dim).astype(jnp.bfloat16), "ctx"
    )
    key_grad = unrotate(keyval_grad[:, :head_dim], own_positions).astype(jnp.bfloat16)
    value_grad = keyval_grad[:, head_dim:].astype(jnp.bfloat16)
    next_keyval_grad = passed_along_2(
        jnp.concatenate([key_grad, value_grad], axis=1), "pipe", -1
    )
    passed = (partial + contract_cols(next_keyval_grad, next_weight[:, query_width:])).astype(jnp.bfloat16)
    return passed[None]


def solution(mesh):
    return jax.shard_map(
        body,
        mesh=mesh,
        in_specs=(
            P("pipe", "ctx", None),
            P("pipe", "ctx", None),
            P("pipe", "ctx", None),
            P("pipe", "ctx", None),
            P("pipe", "ctx", None),
            P("pipe", None),
            P("pipe", None),
        ),
        out_specs=P("pipe", "ctx", None),
        check_vma=False,
    )
```

```python
import math

import jax
import jax.numpy as jnp
from jax import lax
from jax.sharding import PartitionSpec as P

BLOCK = 128


ROPE_BASE = 500000.0
MASKED = -1e30


def passed_along(value, axis, steps):
    count = lax.axis_size(axis)
    pairs = [(source, (source + steps) % count) for source in range(count)]
    return lax.ppermute(value, axis, pairs)


def passed_along_2(value, axis, by):
    size = lax.axis_size(axis)
    pairs = [(i, i + by) for i in range(size) if 0 <= i + by < size]
    return lax.ppermute(value, axis, pairs)


def gathered_rows(value, axis):
    count = lax.axis_size(axis)
    spread = jnp.broadcast_to(value[None], (count,) + value.shape)
    return lax.all_to_all(spread, axis, 0, 0, tiled=False).reshape((-1,) + value.shape[1:])


def summed_rows(value, axis):
    count = lax.axis_size(axis)
    pieces = lax.all_to_all(value.reshape((count, -1) + value.shape[1:]), axis, 0, 0, tiled=False)
    return jnp.sum(pieces.astype(jnp.float32), axis=0)


def rope_tables(positions, head_dim):
    half_width = head_dim // 2
    inv_freq = ROPE_BASE ** (-(jnp.arange(half_width, dtype=jnp.float32) * 2.0 / head_dim))
    angles = positions.astype(jnp.float32)[:, None] * inv_freq[None, :]
    angles = jnp.concatenate([angles, angles], axis=1)
    return (jnp.cos(angles), jnp.sin(angles))


def unrotate(gradient, positions):
    cosine, sine_table = rope_tables(positions, gradient.shape[1])
    half_width = gradient.shape[1] // 2
    turned = jnp.concatenate([-gradient[:, half_width:], gradient[:, :half_width]], axis=1)
    return gradient * cosine - turned * sine_table


def doc_ids(positions, lengths):
    doc_ends = jnp.cumsum(lengths)[:-1]
    return jnp.sum((positions[:, None] >= doc_ends[None, :]).astype(jnp.int32), axis=1)


def seq_to_stored(rows, block_order, device, ctx_size, per_device):
    width = rows.shape[1]
    first_block = device * per_device
    blocks = rows.reshape(per_device, BLOCK, width)
    pieces = []
    for slot_k in range(per_device):
        offset = slot_k * ctx_size // per_device
        slot_at = (device - offset) % ctx_size * per_device + slot_k
        local_index = block_order[slot_at] - first_block
        chosen = lax.dynamic_index_in_dim(blocks, local_index, 0, keepdims=False)
        if slot_k > 0:
            chosen = passed_along(chosen, "ctx", -offset)
        pieces.append(chosen)
    return jnp.concatenate(pieces, axis=0)


def stored_to_seq(rows, block_order, device, ctx_size, per_device):
    width = rows.shape[1]
    first_block = device * per_device
    blocks = rows.reshape(per_device, BLOCK, width)
    pieces = []
    local_ids = []
    for slot_k in range(per_device):
        offset = slot_k * ctx_size // per_device
        piece = blocks[slot_k]
        if slot_k > 0:
            piece = passed_along(piece, "ctx", offset)
        pieces.append(piece)
        sender_slot = (device - offset) % ctx_size * per_device + slot_k
        local_ids.append(block_order[sender_slot] - first_block)
    stacked = jnp.stack(pieces)
    index_list = jnp.stack(local_ids)
    choose = (jnp.arange(per_device, dtype=jnp.int32)[:, None] == index_list[None, :]).astype(
        rows.dtype
    )
    placed = jnp.einsum("pk,kbw->pbw", choose, stacked, preferred_element_type=jnp.float32)
    return placed.astype(rows.dtype).reshape(-1, width)


def contract_rows(left_rows, right_rows):
    return lax.dot_general(
        left_rows, right_rows, (((0,), (0,)), ((), ())), preferred_element_type=jnp.float32
    )


def contract_cols(left_rows, right_rows):
    return lax.dot_general(
        left_rows, right_rows, (((1,), (1,)), ((), ())), preferred_element_type=jnp.float32
    )


def block_scores(query_rows, key_rows, query_pos, query_doc, key_pos, key_doc, score_scale):
    scores = contract_cols(query_rows, key_rows) * score_scale
    visible = (query_doc[:, None] == key_doc[None, :]) & (key_pos[None, :] <= query_pos[:, None])
    return (scores, visible)


def body(grad_in, query, keyval, w_qkv, w_out, doc_lengths, order):
    section_grad_in = grad_in[0]
    stored_query = query[0]
    stored_keyval = keyval[0]
    in_weight = w_qkv[0]
    out_weight = w_out[0]
    lengths = doc_lengths[0]
    block_order = order[0]
    ctx_size = lax.axis_size("ctx")
    device = lax.axis_index("ctx")
    local_rows = section_grad_in.shape[0]
    head_dim = stored_keyval.shape[1] // 2
    group = stored_query.shape[1] // head_dim
    per_device = local_rows // BLOCK
    block_count = block_order.shape[0]
    seq_len = local_rows * ctx_size
    first_row = device * local_rows
    score_scale = 1.0 / math.sqrt(head_dim)
    key_block = math.gcd(seq_len, 512)
    key_steps = seq_len // key_block
    within = jnp.arange(BLOCK, dtype=jnp.int32)
    next_grad_in = passed_along_2(section_grad_in, "pipe", -1)
    next_weight = lax.all_gather(passed_along_2(in_weight, "pipe", -1), "ctx", axis=0, tiled=True)
    out_grad = jnp.dot(
        section_grad_in,
        lax.all_gather(out_weight, "ctx", axis=0, tiled=True),
        preferred_element_type=jnp.float32,
    ).astype(jnp.bfloat16)
    local_out_grad = out_grad
    seq_query = stored_to_seq(stored_query, block_order, device, ctx_size, per_device)
    gathered = gathered_rows(stored_keyval, "ctx")
    slot_ids = jnp.arange(block_count, dtype=jnp.int32)
    inverse = jnp.sum(
        jnp.where(block_order[None, :] == slot_ids[:, None], slot_ids[None, :], 0), axis=1
    )
    all_keyval = gathered.reshape(block_count, BLOCK, 2 * head_dim)[inverse].reshape(
        seq_len, 2 * head_dim
    )
    key_positions = jnp.arange(seq_len, dtype=jnp.int32)
    key_docs = doc_ids(key_positions, lengths)
    query_pos = first_row + jnp.arange(local_rows, dtype=jnp.int32)
    query_doc = doc_ids(query_pos, lengths)
    flat_rows = local_rows * group
    flat_query = seq_query.reshape(flat_rows, head_dim)
    flat_grad = local_out_grad.reshape(flat_rows, head_dim)
    flat_pos = jnp.repeat(query_pos, group)
    flat_doc = jnp.repeat(query_doc, group)
    key_blocks = (
        all_keyval.reshape(key_steps, key_block, 2 * head_dim),
        key_positions.reshape(key_steps, key_block),
        key_docs.reshape(key_steps, key_block),
    )

    def running_total(carried, current):
        row_top, row_total, weighted = carried
        pair_rows, key_pos, key_doc = current
        scores, visible = block_scores(
            flat_query, pair_rows[:, :head_dim], flat_pos, flat_doc, key_pos, key_doc, score_scale
        )
        new_top = jnp.maximum(row_top, jnp.max(jnp.where(visible, scores, MASKED), axis=1))
        rescale = jnp.exp(row_top - new_top)
        weights = jnp.where(visible, jnp.exp(scores - new_top[:, None]), 0.0)
        row_total = row_total * rescale + jnp.sum(weights, axis=1)
        value_wide = pair_rows[:, head_dim:].astype(jnp.float32)
        weighted = weighted * rescale[:, None] + jnp.dot(
            weights, value_wide, precision=lax.Precision.HIGHEST
        )
        return ((new_top, row_total, weighted), None)

    start_top = jnp.full((flat_rows,), MASKED, jnp.float32)
    start_carry = (
        start_top,
        jnp.zeros((flat_rows,), jnp.float32),
        jnp.zeros((flat_rows, head_dim), jnp.float32),
    )
    (row_top, row_total, weighted), unused = lax.scan(running_total, start_carry, key_blocks)
    log_total = row_top + jnp.log(row_total)
    attn_out = weighted / row_total[:, None]
    row_delta = jnp.sum(flat_grad.astype(jnp.float32) * attn_out, axis=1)

    def grad_step(summed, current):
        pair_rows, key_pos, key_doc = current
        scores, visible = block_scores(
            flat_query, pair_rows[:, :head_dim], flat_pos, flat_doc, key_pos, key_doc, score_scale
        )
        attn_prob = jnp.where(visible, jnp.exp(scores - log_total[:, None]), 0.0)
        prob_grad = contract_cols(flat_grad, pair_rows[:, head_dim:])
        score_grad = (score_scale * attn_prob * (prob_grad - row_delta[:, None])).astype(
            jnp.bfloat16
        )
        summed = summed + jnp.dot(
            score_grad, pair_rows[:, :head_dim], preferred_element_type=jnp.float32
        )
        key_term = contract_rows(score_grad, flat_query)
        value_term = contract_rows(attn_prob.astype(jnp.bfloat16), flat_grad)
        return (summed, jnp.concatenate([key_term, value_term], axis=1))

    query_grad_rot, key_terms = lax.scan(
        grad_step, jnp.zeros((flat_rows, head_dim), jnp.float32), key_blocks
    )
    own_positions = first_row + jnp.arange(local_rows, dtype=jnp.int32)
    keyval_grad = summed_rows(
        key_terms.reshape(seq_len, 2 * head_dim).astype(jnp.bfloat16), "ctx"
    )
    query_grad = (
        unrotate(query_grad_rot, flat_pos)
        .reshape(local_rows, group * head_dim)
        .astype(jnp.bfloat16)
    )
    key_grad = unrotate(keyval_grad[:, :head_dim], own_positions).astype(jnp.bfloat16)
    value_grad = keyval_grad[:, head_dim:].astype(jnp.bfloat16)
    qkv_grad = jnp.concatenate([query_grad, key_grad, value_grad], axis=1)
    next_qkv_grad = passed_along_2(qkv_grad, "pipe", -1)
    projected = contract_cols(next_qkv_grad, next_weight)
    passed = (next_grad_in.astype(jnp.float32) + projected).astype(jnp.bfloat16)
    return passed[None]


def solution(mesh):
    return jax.shard_map(
        body,
        mesh=mesh,
        in_specs=(
            P("pipe", "ctx", None),
            P("pipe", "ctx", None),
            P("pipe", "ctx", None),
            P("pipe", "ctx", None),
            P("pipe", "ctx", None),
            P("pipe", None),
            P("pipe", None),
        ),
        out_specs=P("pipe", "ctx", None),
        check_vma=False,
    )
```

```python
import math

import jax
import jax.numpy as jnp
from jax import lax
from jax.sharding import PartitionSpec as P

BLOCK = 128


ROPE_BASE = 500000.0
MASKED = -1e30


def passed_along(value, axis, steps):
    count = lax.axis_size(axis)
    pairs = [(source, (source + steps) % count) for source in range(count)]
    return lax.ppermute(value, axis, pairs)


def passed_along_2(value, axis, by):
    size = lax.axis_size(axis)
    pairs = [(i, i + by) for i in range(size) if 0 <= i + by < size]
    return lax.ppermute(value, axis, pairs)


def gathered_rows(value, axis):
    count = lax.axis_size(axis)
    spread = jnp.broadcast_to(value[None], (count,) + value.shape)
    return lax.all_to_all(spread, axis, 0, 0, tiled=False).reshape((-1,) + value.shape[1:])


def summed_rows(value, axis):
    count = lax.axis_size(axis)
    pieces = lax.all_to_all(value.reshape((count, -1) + value.shape[1:]), axis, 0, 0, tiled=False)
    return jnp.sum(pieces.astype(jnp.float32), axis=0)


def rope_tables(positions, head_dim):
    half_width = head_dim // 2
    inv_freq = ROPE_BASE ** (-(jnp.arange(half_width, dtype=jnp.float32) * 2.0 / head_dim))
    angles = positions.astype(jnp.float32)[:, None] * inv_freq[None, :]
    angles = jnp.concatenate([angles, angles], axis=1)
    return (jnp.cos(angles), jnp.sin(angles))


def unrotate(gradient, positions):
    cosine, sine_table = rope_tables(positions, gradient.shape[1])
    half_width = gradient.shape[1] // 2
    turned = jnp.concatenate([-gradient[:, half_width:], gradient[:, :half_width]], axis=1)
    return gradient * cosine - turned * sine_table


def doc_ids(positions, lengths):
    doc_ends = jnp.cumsum(lengths)[:-1]
    return jnp.sum((positions[:, None] >= doc_ends[None, :]).astype(jnp.int32), axis=1)


def seq_to_stored(rows, block_order, device, ctx_size, per_device):
    width = rows.shape[1]
    first_block = device * per_device
    blocks = rows.reshape(per_device, BLOCK, width)
    pieces = []
    for slot_k in range(per_device):
        offset = slot_k * ctx_size // per_device
        slot_at = (device - offset) % ctx_size * per_device + slot_k
        local_index = block_order[slot_at] - first_block
        chosen = lax.dynamic_index_in_dim(blocks, local_index, 0, keepdims=False)
        if slot_k > 0:
            chosen = passed_along(chosen, "ctx", -offset)
        pieces.append(chosen)
    return jnp.concatenate(pieces, axis=0)


def stored_to_seq(rows, block_order, device, ctx_size, per_device):
    width = rows.shape[1]
    first_block = device * per_device
    blocks = rows.reshape(per_device, BLOCK, width)
    pieces = []
    local_ids = []
    for slot_k in range(per_device):
        offset = slot_k * ctx_size // per_device
        piece = blocks[slot_k]
        if slot_k > 0:
            piece = passed_along(piece, "ctx", offset)
        pieces.append(piece)
        sender_slot = (device - offset) % ctx_size * per_device + slot_k
        local_ids.append(block_order[sender_slot] - first_block)
    stacked = jnp.stack(pieces)
    index_list = jnp.stack(local_ids)
    choose = (jnp.arange(per_device, dtype=jnp.int32)[:, None] == index_list[None, :]).astype(
        rows.dtype
    )
    placed = jnp.einsum("pk,kbw->pbw", choose, stacked, preferred_element_type=jnp.float32)
    return placed.astype(rows.dtype).reshape(-1, width)


def contract_rows(left_rows, right_rows):
    return lax.dot_general(
        left_rows, right_rows, (((0,), (0,)), ((), ())), preferred_element_type=jnp.float32
    )


def contract_cols(left_rows, right_rows):
    return lax.dot_general(
        left_rows, right_rows, (((1,), (1,)), ((), ())), preferred_element_type=jnp.float32
    )


def block_scores(query_rows, key_rows, query_pos, query_doc, key_pos, key_doc, score_scale):
    scores = contract_cols(query_rows, key_rows) * score_scale
    visible = (query_doc[:, None] == key_doc[None, :]) & (key_pos[None, :] <= query_pos[:, None])
    return (scores, visible)


def body(grad_in, query, keyval, w_qkv, w_out, doc_lengths, order):
    section_grad_in = grad_in[0]
    stored_query = query[0]
    stored_keyval = keyval[0]
    in_weight = w_qkv[0]
    out_weight = w_out[0]
    lengths = doc_lengths[0]
    block_order = order[0]
    ctx_size = lax.axis_size("ctx")
    device = lax.axis_index("ctx")
    local_rows = section_grad_in.shape[0]
    head_dim = stored_keyval.shape[1] // 2
    group = stored_query.shape[1] // head_dim
    per_device = local_rows // BLOCK
    block_count = block_order.shape[0]
    seq_len = local_rows * ctx_size
    first_row = device * local_rows
    score_scale = 1.0 / math.sqrt(head_dim)
    key_block = math.gcd(seq_len, 512)
    key_steps = seq_len // key_block
    within = jnp.arange(BLOCK, dtype=jnp.int32)
    query_width = stored_query.shape[1]
    next_shard = passed_along_2(in_weight, "pipe", -1)
    next_weight_q = lax.all_gather(next_shard[:, :query_width], "ctx", axis=0, tiled=True)
    next_weight_kv = gathered_rows(next_shard[:, query_width:], "ctx")
    out_grad = jnp.dot(
        section_grad_in,
        lax.all_gather(out_weight, "ctx", axis=0, tiled=True),
        preferred_element_type=jnp.float32,
    ).astype(jnp.bfloat16)
    local_out_grad = out_grad
    seq_query = stored_to_seq(stored_query, block_order, device, ctx_size, per_device)
    gathered = gathered_rows(stored_keyval, "ctx")
    gathered, grad_source = lax.optimization_barrier((gathered, section_grad_in))
    next_grad_in = passed_along_2(grad_source, "pipe", -1)
    slot_ids = jnp.arange(block_count, dtype=jnp.int32)
    inverse = jnp.sum(
        jnp.where(block_order[None, :] == slot_ids[:, None], slot_ids[None, :], 0), axis=1
    )
    all_keyval = gathered.reshape(block_count, BLOCK, 2 * head_dim)[inverse].reshape(
        seq_len, 2 * head_dim
    )
    key_positions = jnp.arange(seq_len, dtype=jnp.int32)
    key_docs = doc_ids(key_positions, lengths)
    query_pos = first_row + jnp.arange(local_rows, dtype=jnp.int32)
    query_doc = doc_ids(query_pos, lengths)
    flat_rows = local_rows * group
    flat_query = seq_query.reshape(flat_rows, head_dim)
    next_weight_kv, local_out_grad = lax.optimization_barrier((next_weight_kv, local_out_grad))
    flat_grad = local_out_grad.reshape(flat_rows, head_dim)
    flat_pos = jnp.repeat(query_pos, group)
    flat_doc = jnp.repeat(query_doc, group)
    key_blocks = (
        all_keyval.reshape(key_steps, key_block, 2 * head_dim),
        key_positions.reshape(key_steps, key_block),
        key_docs.reshape(key_steps, key_block),
    )

    def running_total(carried, current):
        row_top, row_total, weighted = carried
        pair_rows, key_pos, key_doc = current
        scores, visible = block_scores(
            flat_query, pair_rows[:, :head_dim], flat_pos, flat_doc, key_pos, key_doc, score_scale
        )
        new_top = jnp.maximum(row_top, jnp.max(jnp.where(visible, scores, MASKED), axis=1))
        rescale = jnp.exp(row_top - new_top)
        weights = jnp.where(visible, jnp.exp(scores - new_top[:, None]), 0.0)
        row_total = row_total * rescale + jnp.sum(weights, axis=1)
        value_wide = pair_rows[:, head_dim:].astype(jnp.float32)
        weighted = weighted * rescale[:, None] + jnp.dot(
            weights, value_wide, precision=lax.Precision.HIGHEST
        )
        return ((new_top, row_total, weighted), None)

    start_top = jnp.full((flat_rows,), MASKED, jnp.float32)
    start_carry = (
        start_top,
        jnp.zeros((flat_rows,), jnp.float32),
        jnp.zeros((flat_rows, head_dim), jnp.float32),
    )
    (row_top, row_total, weighted), unused = lax.scan(running_total, start_carry, key_blocks)
    log_total = row_top + jnp.log(row_total)
    attn_out = weighted / row_total[:, None]
    row_delta = jnp.sum(flat_grad.astype(jnp.float32) * attn_out, axis=1)

    def grad_step(summed, current):
        pair_rows, key_pos, key_doc = current
        scores, visible = block_scores(
            flat_query, pair_rows[:, :head_dim], flat_pos, flat_doc, key_pos, key_doc, score_scale
        )
        attn_prob = jnp.where(visible, jnp.exp(scores - log_total[:, None]), 0.0)
        prob_grad = contract_cols(flat_grad, pair_rows[:, head_dim:])
        score_grad = (score_scale * attn_prob * (prob_grad - row_delta[:, None])).astype(
            jnp.bfloat16
        )
        summed = summed + jnp.dot(
            score_grad, pair_rows[:, :head_dim], preferred_element_type=jnp.float32
        )
        key_term = contract_rows(score_grad, flat_query)
        value_term = contract_rows(attn_prob.astype(jnp.bfloat16), flat_grad)
        return (summed, jnp.concatenate([key_term, value_term], axis=1))

    query_grad_rot, key_terms = lax.scan(
        grad_step, jnp.zeros((flat_rows, head_dim), jnp.float32), key_blocks
    )
    own_positions = first_row + jnp.arange(local_rows, dtype=jnp.int32)
    keyval_grad = summed_rows(
        key_terms.reshape(seq_len, 2 * head_dim).astype(jnp.bfloat16), "ctx"
    )
    query_grad = (
        unrotate(query_grad_rot, flat_pos)
        .reshape(local_rows, group * head_dim)
        .astype(jnp.bfloat16)
    )
    key_grad = unrotate(keyval_grad[:, :head_dim], own_positions).astype(jnp.bfloat16)
    value_grad = keyval_grad[:, head_dim:].astype(jnp.bfloat16)
    qkv_grad = jnp.concatenate([query_grad, key_grad, value_grad], axis=1)
    next_qkv_grad = passed_along_2(qkv_grad, "pipe", -1)
    projected = contract_cols(next_qkv_grad[:, :query_width], next_weight_q) + contract_cols(
        next_qkv_grad[:, query_width:], next_weight_kv
    )
    passed = (next_grad_in.astype(jnp.float32) + projected).astype(jnp.bfloat16)
    return passed[None]


def solution(mesh):
    return jax.shard_map(
        body,
        mesh=mesh,
        in_specs=(
            P("pipe", "ctx", None),
            P("pipe", "ctx", None),
            P("pipe", "ctx", None),
            P("pipe", "ctx", None),
            P("pipe", "ctx", None),
            P("pipe", None),
            P("pipe", None),
        ),
        out_specs=P("pipe", "ctx", None),
        check_vma=False,
    )
```

```python
import math

import jax
import jax.numpy as jnp
from jax import lax
from jax.sharding import PartitionSpec as P

BLOCK = 128


ROPE_BASE = 500000.0
MASKED = -1e30


def passed_along(value, axis, steps):
    count = lax.axis_size(axis)
    pairs = [(source, (source + steps) % count) for source in range(count)]
    return lax.ppermute(value, axis, pairs)


def passed_along_2(value, axis, by):
    size = lax.axis_size(axis)
    pairs = [(i, i + by) for i in range(size) if 0 <= i + by < size]
    return lax.ppermute(value, axis, pairs)


def gathered_rows(value, axis):
    count = lax.axis_size(axis)
    spread = jnp.broadcast_to(value[None], (count,) + value.shape)
    return lax.all_to_all(spread, axis, 0, 0, tiled=False).reshape((-1,) + value.shape[1:])


def summed_rows(value, axis):
    count = lax.axis_size(axis)
    pieces = lax.all_to_all(value.reshape((count, -1) + value.shape[1:]), axis, 0, 0, tiled=False)
    return jnp.sum(pieces.astype(jnp.float32), axis=0)


def rope_tables(positions, head_dim):
    half_width = head_dim // 2
    inv_freq = ROPE_BASE ** (-(jnp.arange(half_width, dtype=jnp.float32) * 2.0 / head_dim))
    angles = positions.astype(jnp.float32)[:, None] * inv_freq[None, :]
    angles = jnp.concatenate([angles, angles], axis=1)
    return (jnp.cos(angles), jnp.sin(angles))


def unrotate(gradient, positions):
    cosine, sine_table = rope_tables(positions, gradient.shape[1])
    half_width = gradient.shape[1] // 2
    turned = jnp.concatenate([-gradient[:, half_width:], gradient[:, :half_width]], axis=1)
    return gradient * cosine - turned * sine_table


def doc_ids(positions, lengths):
    doc_ends = jnp.cumsum(lengths)[:-1]
    return jnp.sum((positions[:, None] >= doc_ends[None, :]).astype(jnp.int32), axis=1)


def seq_to_stored(rows, block_order, device, ctx_size, per_device):
    width = rows.shape[1]
    first_block = device * per_device
    blocks = rows.reshape(per_device, BLOCK, width)
    pieces = []
    for slot_k in range(per_device):
        offset = slot_k * ctx_size // per_device
        slot_at = (device - offset) % ctx_size * per_device + slot_k
        local_index = block_order[slot_at] - first_block
        chosen = lax.dynamic_index_in_dim(blocks, local_index, 0, keepdims=False)
        if slot_k > 0:
            chosen = passed_along(chosen, "ctx", -offset)
        pieces.append(chosen)
    return jnp.concatenate(pieces, axis=0)


def stored_to_seq(rows, block_order, device, ctx_size, per_device):
    width = rows.shape[1]
    first_block = device * per_device
    blocks = rows.reshape(per_device, BLOCK, width)
    pieces = []
    local_ids = []
    for slot_k in range(per_device):
        offset = slot_k * ctx_size // per_device
        piece = blocks[slot_k]
        if slot_k > 0:
            piece = passed_along(piece, "ctx", offset)
        pieces.append(piece)
        sender_slot = (device - offset) % ctx_size * per_device + slot_k
        local_ids.append(block_order[sender_slot] - first_block)
    stacked = jnp.stack(pieces)
    index_list = jnp.stack(local_ids)
    choose = (jnp.arange(per_device, dtype=jnp.int32)[:, None] == index_list[None, :]).astype(
        rows.dtype
    )
    placed = jnp.einsum("pk,kbw->pbw", choose, stacked, preferred_element_type=jnp.float32)
    return placed.astype(rows.dtype).reshape(-1, width)


def contract_rows(left_rows, right_rows):
    return lax.dot_general(
        left_rows, right_rows, (((0,), (0,)), ((), ())), preferred_element_type=jnp.float32
    )


def contract_cols(left_rows, right_rows):
    return lax.dot_general(
        left_rows, right_rows, (((1,), (1,)), ((), ())), preferred_element_type=jnp.float32
    )


def block_scores(query_rows, key_rows, query_pos, query_doc, key_pos, key_doc, score_scale):
    scores = contract_cols(query_rows, key_rows) * score_scale
    visible = (query_doc[:, None] == key_doc[None, :]) & (key_pos[None, :] <= query_pos[:, None])
    return (scores, visible)


def body(grad_in, query, keyval, w_qkv, w_out, doc_lengths, order):
    section_grad_in = grad_in[0]
    stored_query = query[0]
    stored_keyval = keyval[0]
    in_weight = w_qkv[0]
    out_weight = w_out[0]
    lengths = doc_lengths[0]
    block_order = order[0]
    ctx_size = lax.axis_size("ctx")
    device = lax.axis_index("ctx")
    local_rows = section_grad_in.shape[0]
    head_dim = stored_keyval.shape[1] // 2
    group = stored_query.shape[1] // head_dim
    per_device = local_rows // BLOCK
    block_count = block_order.shape[0]
    seq_len = local_rows * ctx_size
    first_row = device * local_rows
    score_scale = 1.0 / math.sqrt(head_dim)
    key_block = math.gcd(seq_len, 512)
    key_steps = seq_len // key_block
    within = jnp.arange(BLOCK, dtype=jnp.int32)
    next_weight = lax.all_gather(passed_along_2(in_weight, "pipe", -1), "ctx", axis=0, tiled=True)
    out_grad = jnp.dot(
        section_grad_in,
        lax.all_gather(out_weight, "ctx", axis=0, tiled=True),
        preferred_element_type=jnp.float32,
    ).astype(jnp.bfloat16)
    local_out_grad = out_grad
    seq_query = stored_to_seq(stored_query, block_order, device, ctx_size, per_device)
    gathered = gathered_rows(stored_keyval, "ctx")
    gathered, grad_source = lax.optimization_barrier((gathered, section_grad_in))
    next_grad_in = passed_along_2(grad_source, "pipe", -1)
    slot_ids = jnp.arange(block_count, dtype=jnp.int32)
    inverse = jnp.sum(
        jnp.where(block_order[None, :] == slot_ids[:, None], slot_ids[None, :], 0), axis=1
    )
    all_keyval = gathered.reshape(block_count, BLOCK, 2 * head_dim)[inverse].reshape(
        seq_len, 2 * head_dim
    )
    key_positions = jnp.arange(seq_len, dtype=jnp.int32)
    key_docs = doc_ids(key_positions, lengths)
    query_pos = first_row + jnp.arange(local_rows, dtype=jnp.int32)
    query_doc = doc_ids(query_pos, lengths)
    flat_rows = local_rows * group
    flat_query = seq_query.reshape(flat_rows, head_dim)
    flat_grad = local_out_grad.reshape(flat_rows, head_dim)
    flat_pos = jnp.repeat(query_pos, group)
    flat_doc = jnp.repeat(query_doc, group)
    key_blocks = (
        all_keyval.reshape(key_steps, key_block, 2 * head_dim),
        key_positions.reshape(key_steps, key_block),
        key_docs.reshape(key_steps, key_block),
    )

    def running_total(carried, current):
        row_top, row_total, weighted = carried
        pair_rows, key_pos, key_doc = current
        scores, visible = block_scores(
            flat_query, pair_rows[:, :head_dim], flat_pos, flat_doc, key_pos, key_doc, score_scale
        )
        new_top = jnp.maximum(row_top, jnp.max(jnp.where(visible, scores, MASKED), axis=1))
        rescale = jnp.exp(row_top - new_top)
        weights = jnp.where(visible, jnp.exp(scores - new_top[:, None]), 0.0)
        row_total = row_total * rescale + jnp.sum(weights, axis=1)
        value_wide = pair_rows[:, head_dim:].astype(jnp.float32)
        weighted = weighted * rescale[:, None] + jnp.dot(
            weights, value_wide, precision=lax.Precision.HIGHEST
        )
        return ((new_top, row_total, weighted), None)

    start_top = jnp.full((flat_rows,), MASKED, jnp.float32)
    start_carry = (
        start_top,
        jnp.zeros((flat_rows,), jnp.float32),
        jnp.zeros((flat_rows, head_dim), jnp.float32),
    )
    (row_top, row_total, weighted), unused = lax.scan(running_total, start_carry, key_blocks)
    log_total = row_top + jnp.log(row_total)
    attn_out = weighted / row_total[:, None]
    row_delta = jnp.sum(flat_grad.astype(jnp.float32) * attn_out, axis=1)

    def grad_step(summed, current):
        pair_rows, key_pos, key_doc = current
        scores, visible = block_scores(
            flat_query, pair_rows[:, :head_dim], flat_pos, flat_doc, key_pos, key_doc, score_scale
        )
        attn_prob = jnp.where(visible, jnp.exp(scores - log_total[:, None]), 0.0)
        prob_grad = contract_cols(flat_grad, pair_rows[:, head_dim:])
        score_grad = (score_scale * attn_prob * (prob_grad - row_delta[:, None])).astype(
            jnp.bfloat16
        )
        summed = summed + jnp.dot(
            score_grad, pair_rows[:, :head_dim], preferred_element_type=jnp.float32
        )
        key_term = contract_rows(score_grad, flat_query)
        value_term = contract_rows(attn_prob.astype(jnp.bfloat16), flat_grad)
        return (summed, jnp.concatenate([key_term, value_term], axis=1))

    query_grad_rot, key_terms = lax.scan(
        grad_step, jnp.zeros((flat_rows, head_dim), jnp.float32), key_blocks
    )
    own_positions = first_row + jnp.arange(local_rows, dtype=jnp.int32)
    query_grad = (
        unrotate(query_grad_rot, flat_pos)
        .reshape(local_rows, group * head_dim)
        .astype(jnp.bfloat16)
    )
    next_query_grad = passed_along_2(query_grad, "pipe", -1)
    keyval_grad = summed_rows(
        key_terms.reshape(seq_len, 2 * head_dim).astype(jnp.bfloat16), "ctx"
    )
    key_grad = unrotate(keyval_grad[:, :head_dim], own_positions).astype(jnp.bfloat16)
    value_grad = keyval_grad[:, head_dim:].astype(jnp.bfloat16)
    next_keyval_grad = passed_along_2(
        jnp.concatenate([key_grad, value_grad], axis=1), "pipe", -1
    )
    next_qkv_grad = jnp.concatenate([next_query_grad, next_keyval_grad], axis=1)
    projected = contract_cols(next_qkv_grad, next_weight)
    passed = (next_grad_in.astype(jnp.float32) + projected).astype(jnp.bfloat16)
    return passed[None]


def solution(mesh):
    return jax.shard_map(
        body,
        mesh=mesh,
        in_specs=(
            P("pipe", "ctx", None),
            P("pipe", "ctx", None),
            P("pipe", "ctx", None),
            P("pipe", "ctx", None),
            P("pipe", "ctx", None),
            P("pipe", None),
            P("pipe", None),
        ),
        out_specs=P("pipe", "ctx", None),
        check_vma=False,
    )
```

```python
import math

import jax
import jax.numpy as jnp
from jax import lax
from jax.experimental import pallas as pl
from jax.sharding import PartitionSpec as P

BLOCK = 128


ROPE_BASE = 500000.0
MASKED = -1e30


def passed_along(value, axis, steps):
    count = lax.axis_size(axis)
    pairs = [(source, (source + steps) % count) for source in range(count)]
    return lax.ppermute(value, axis, pairs)


def passed_along_2(value, axis, by):
    size = lax.axis_size(axis)
    pairs = [(i, i + by) for i in range(size) if 0 <= i + by < size]
    return lax.ppermute(value, axis, pairs)


def gathered_rows(value, axis):
    count = lax.axis_size(axis)
    spread = jnp.broadcast_to(value[None], (count,) + value.shape)
    return lax.all_to_all(spread, axis, 0, 0, tiled=False).reshape((-1,) + value.shape[1:])


def summed_rows(value, axis):
    count = lax.axis_size(axis)
    pieces = lax.all_to_all(value.reshape((count, -1) + value.shape[1:]), axis, 0, 0, tiled=False)
    return jnp.sum(pieces.astype(jnp.float32), axis=0)


def projection_kernel(grad_ref, weight_ref, base_ref, out_ref):
    product = lax.dot_general(
        grad_ref[...], weight_ref[...], (((1,), (1,)), ((), ())), preferred_element_type=jnp.float32
    )
    out_ref[...] = (base_ref[...].astype(jnp.float32) + product).astype(out_ref.dtype)


def projected_sum(grad_rows, weight, base, tile=1024):
    rows, inner = grad_rows.shape
    width = weight.shape[0]
    return pl.pallas_call(
        projection_kernel,
        grid=(width // tile,),
        in_specs=[
            pl.BlockSpec((rows, inner), lambda j: (0, 0)),
            pl.BlockSpec((tile, inner), lambda j: (j, 0)),
            pl.BlockSpec((rows, tile), lambda j: (0, j)),
        ],
        out_specs=pl.BlockSpec((rows, tile), lambda j: (0, j)),
        out_shape=jax.ShapeDtypeStruct((rows, width), base.dtype),
        cost_estimate=pl.CostEstimate(
            flops=2 * rows * inner * width,
            bytes_accessed=2 * (rows * inner + width * inner + 2 * rows * width),
            transcendentals=0,
        ),
    )(grad_rows, weight, base)


def rope_tables(positions, head_dim):
    half_width = head_dim // 2
    inv_freq = ROPE_BASE ** (-(jnp.arange(half_width, dtype=jnp.float32) * 2.0 / head_dim))
    angles = positions.astype(jnp.float32)[:, None] * inv_freq[None, :]
    angles = jnp.concatenate([angles, angles], axis=1)
    return (jnp.cos(angles), jnp.sin(angles))


def unrotate(gradient, positions):
    cosine, sine_table = rope_tables(positions, gradient.shape[1])
    half_width = gradient.shape[1] // 2
    turned = jnp.concatenate([-gradient[:, half_width:], gradient[:, :half_width]], axis=1)
    return gradient * cosine - turned * sine_table


def doc_ids(positions, lengths):
    doc_ends = jnp.cumsum(lengths)[:-1]
    return jnp.sum((positions[:, None] >= doc_ends[None, :]).astype(jnp.int32), axis=1)


def seq_to_stored(rows, block_order, device, ctx_size, per_device):
    width = rows.shape[1]
    first_block = device * per_device
    blocks = rows.reshape(per_device, BLOCK, width)
    pieces = []
    for slot_k in range(per_device):
        offset = slot_k * ctx_size // per_device
        slot_at = (device - offset) % ctx_size * per_device + slot_k
        local_index = block_order[slot_at] - first_block
        chosen = lax.dynamic_index_in_dim(blocks, local_index, 0, keepdims=False)
        if slot_k > 0:
            chosen = passed_along(chosen, "ctx", -offset)
        pieces.append(chosen)
    return jnp.concatenate(pieces, axis=0)


def stored_to_seq(rows, block_order, device, ctx_size, per_device):
    width = rows.shape[1]
    first_block = device * per_device
    blocks = rows.reshape(per_device, BLOCK, width)
    pieces = []
    local_ids = []
    for slot_k in range(per_device):
        offset = slot_k * ctx_size // per_device
        piece = blocks[slot_k]
        if slot_k > 0:
            piece = passed_along(piece, "ctx", offset)
        pieces.append(piece)
        sender_slot = (device - offset) % ctx_size * per_device + slot_k
        local_ids.append(block_order[sender_slot] - first_block)
    stacked = jnp.stack(pieces)
    index_list = jnp.stack(local_ids)
    choose = (jnp.arange(per_device, dtype=jnp.int32)[:, None] == index_list[None, :]).astype(
        rows.dtype
    )
    placed = jnp.einsum("pk,kbw->pbw", choose, stacked, preferred_element_type=jnp.float32)
    return placed.astype(rows.dtype).reshape(-1, width)


def contract_rows(left_rows, right_rows):
    return lax.dot_general(
        left_rows, right_rows, (((0,), (0,)), ((), ())), preferred_element_type=jnp.float32
    )


def contract_cols(left_rows, right_rows):
    return lax.dot_general(
        left_rows, right_rows, (((1,), (1,)), ((), ())), preferred_element_type=jnp.float32
    )


def block_scores(query_rows, key_rows, query_pos, query_doc, key_pos, key_doc, score_scale):
    scores = contract_cols(query_rows, key_rows) * score_scale
    visible = (query_doc[:, None] == key_doc[None, :]) & (key_pos[None, :] <= query_pos[:, None])
    return (scores, visible)


def body(grad_in, query, keyval, w_qkv, w_out, doc_lengths, order):
    section_grad_in = grad_in[0]
    stored_query = query[0]
    stored_keyval = keyval[0]
    in_weight = w_qkv[0]
    out_weight = w_out[0]
    lengths = doc_lengths[0]
    block_order = order[0]
    ctx_size = lax.axis_size("ctx")
    device = lax.axis_index("ctx")
    local_rows = section_grad_in.shape[0]
    head_dim = stored_keyval.shape[1] // 2
    group = stored_query.shape[1] // head_dim
    per_device = local_rows // BLOCK
    block_count = block_order.shape[0]
    seq_len = local_rows * ctx_size
    first_row = device * local_rows
    score_scale = 1.0 / math.sqrt(head_dim)
    key_block = math.gcd(seq_len, 512)
    key_steps = seq_len // key_block
    within = jnp.arange(BLOCK, dtype=jnp.int32)
    next_weight = lax.all_gather(passed_along_2(in_weight, "pipe", -1), "ctx", axis=0, tiled=True)
    out_grad = jnp.dot(
        section_grad_in,
        lax.all_gather(out_weight, "ctx", axis=0, tiled=True),
        preferred_element_type=jnp.float32,
    ).astype(jnp.bfloat16)
    local_out_grad = out_grad
    seq_query = stored_to_seq(stored_query, block_order, device, ctx_size, per_device)
    gathered = gathered_rows(stored_keyval, "ctx")
    gathered, grad_source = lax.optimization_barrier((gathered, section_grad_in))
    next_grad_in = passed_along_2(grad_source, "pipe", -1)
    slot_ids = jnp.arange(block_count, dtype=jnp.int32)
    inverse = jnp.sum(
        jnp.where(block_order[None, :] == slot_ids[:, None], slot_ids[None, :], 0), axis=1
    )
    all_keyval = gathered.reshape(block_count, BLOCK, 2 * head_dim)[inverse].reshape(
        seq_len, 2 * head_dim
    )
    key_positions = jnp.arange(seq_len, dtype=jnp.int32)
    key_docs = doc_ids(key_positions, lengths)
    query_pos = first_row + jnp.arange(local_rows, dtype=jnp.int32)
    query_doc = doc_ids(query_pos, lengths)
    flat_rows = local_rows * group
    flat_query = seq_query.reshape(flat_rows, head_dim)
    flat_grad = local_out_grad.reshape(flat_rows, head_dim)
    flat_pos = jnp.repeat(query_pos, group)
    flat_doc = jnp.repeat(query_doc, group)
    key_blocks = (
        all_keyval.reshape(key_steps, key_block, 2 * head_dim),
        key_positions.reshape(key_steps, key_block),
        key_docs.reshape(key_steps, key_block),
    )

    def running_total(carried, current):
        row_top, row_total, weighted = carried
        pair_rows, key_pos, key_doc = current
        scores, visible = block_scores(
            flat_query, pair_rows[:, :head_dim], flat_pos, flat_doc, key_pos, key_doc, score_scale
        )
        new_top = jnp.maximum(row_top, jnp.max(jnp.where(visible, scores, MASKED), axis=1))
        rescale = jnp.exp(row_top - new_top)
        weights = jnp.where(visible, jnp.exp(scores - new_top[:, None]), 0.0)
        row_total = row_total * rescale + jnp.sum(weights, axis=1)
        value_wide = pair_rows[:, head_dim:].astype(jnp.float32)
        weighted = weighted * rescale[:, None] + jnp.dot(
            weights, value_wide, precision=lax.Precision.HIGHEST
        )
        return ((new_top, row_total, weighted), None)

    start_top = jnp.full((flat_rows,), MASKED, jnp.float32)
    start_carry = (
        start_top,
        jnp.zeros((flat_rows,), jnp.float32),
        jnp.zeros((flat_rows, head_dim), jnp.float32),
    )
    (row_top, row_total, weighted), unused = lax.scan(running_total, start_carry, key_blocks)
    log_total = row_top + jnp.log(row_total)
    attn_out = weighted / row_total[:, None]
    row_delta = jnp.sum(flat_grad.astype(jnp.float32) * attn_out, axis=1)

    def grad_step(summed, current):
        pair_rows, key_pos, key_doc = current
        scores, visible = block_scores(
            flat_query, pair_rows[:, :head_dim], flat_pos, flat_doc, key_pos, key_doc, score_scale
        )
        attn_prob = jnp.where(visible, jnp.exp(scores - log_total[:, None]), 0.0)
        prob_grad = contract_cols(flat_grad, pair_rows[:, head_dim:])
        score_grad = (score_scale * attn_prob * (prob_grad - row_delta[:, None])).astype(
            jnp.bfloat16
        )
        summed = summed + jnp.dot(
            score_grad, pair_rows[:, :head_dim], preferred_element_type=jnp.float32
        )
        key_term = contract_rows(score_grad, flat_query)
        value_term = contract_rows(attn_prob.astype(jnp.bfloat16), flat_grad)
        return (summed, jnp.concatenate([key_term, value_term], axis=1))

    query_grad_rot, key_terms = lax.scan(
        grad_step, jnp.zeros((flat_rows, head_dim), jnp.float32), key_blocks
    )
    own_positions = first_row + jnp.arange(local_rows, dtype=jnp.int32)
    query_grad = (
        unrotate(query_grad_rot, flat_pos)
        .reshape(local_rows, group * head_dim)
        .astype(jnp.bfloat16)
    )
    next_query_grad = passed_along_2(query_grad, "pipe", -1)
    keyval_grad = summed_rows(
        key_terms.reshape(seq_len, 2 * head_dim).astype(jnp.bfloat16), "ctx"
    )
    key_grad = unrotate(keyval_grad[:, :head_dim], own_positions).astype(jnp.bfloat16)
    value_grad = keyval_grad[:, head_dim:].astype(jnp.bfloat16)
    next_keyval_grad = passed_along_2(
        jnp.concatenate([key_grad, value_grad], axis=1), "pipe", -1
    )
    next_qkv_grad = jnp.concatenate([next_query_grad, next_keyval_grad], axis=1)
    passed = projected_sum(next_qkv_grad, next_weight, next_grad_in)
    return passed[None]


def solution(mesh):
    return jax.shard_map(
        body,
        mesh=mesh,
        in_specs=(
            P("pipe", "ctx", None),
            P("pipe", "ctx", None),
            P("pipe", "ctx", None),
            P("pipe", "ctx", None),
            P("pipe", "ctx", None),
            P("pipe", None),
            P("pipe", None),
        ),
        out_specs=P("pipe", "ctx", None),
        check_vma=False,
    )
```

```python
import math

import jax
import jax.numpy as jnp
from jax import lax
from jax.experimental import pallas as pl
from jax.sharding import PartitionSpec as P

BLOCK = 128


ROPE_BASE = 500000.0
MASKED = -1e30


def passed_along(value, axis, steps):
    count = lax.axis_size(axis)
    pairs = [(source, (source + steps) % count) for source in range(count)]
    return lax.ppermute(value, axis, pairs)


def passed_along_2(value, axis, by):
    size = lax.axis_size(axis)
    pairs = [(i, i + by) for i in range(size) if 0 <= i + by < size]
    return lax.ppermute(value, axis, pairs)


def gathered_rows(value, axis):
    count = lax.axis_size(axis)
    spread = jnp.broadcast_to(value[None], (count,) + value.shape)
    return lax.all_to_all(spread, axis, 0, 0, tiled=False).reshape((-1,) + value.shape[1:])


def summed_rows(value, axis):
    count = lax.axis_size(axis)
    pieces = lax.all_to_all(value.reshape((count, -1) + value.shape[1:]), axis, 0, 0, tiled=False)
    return jnp.sum(pieces.astype(jnp.float32), axis=0)


def projection_kernel(grad_ref, weight_ref, base_ref, out_ref):
    product = lax.dot_general(
        grad_ref[...], weight_ref[...], (((1,), (1,)), ((), ())), preferred_element_type=jnp.float32
    )
    out_ref[...] = (base_ref[...].astype(jnp.float32) + product).astype(out_ref.dtype)


def projected_sum(grad_rows, weight, base, tile=4096):
    rows, inner = grad_rows.shape
    width = weight.shape[0]
    return pl.pallas_call(
        projection_kernel,
        grid=(width // tile,),
        in_specs=[
            pl.BlockSpec((rows, inner), lambda j: (0, 0)),
            pl.BlockSpec((tile, inner), lambda j: (j, 0)),
            pl.BlockSpec((rows, tile), lambda j: (0, j)),
        ],
        out_specs=pl.BlockSpec((rows, tile), lambda j: (0, j)),
        out_shape=jax.ShapeDtypeStruct((rows, width), base.dtype),
        cost_estimate=pl.CostEstimate(
            flops=2 * rows * inner * width,
            bytes_accessed=2 * (rows * inner + width * inner + 2 * rows * width),
            transcendentals=0,
        ),
    )(grad_rows, weight, base)


def rope_tables(positions, head_dim):
    half_width = head_dim // 2
    inv_freq = ROPE_BASE ** (-(jnp.arange(half_width, dtype=jnp.float32) * 2.0 / head_dim))
    angles = positions.astype(jnp.float32)[:, None] * inv_freq[None, :]
    angles = jnp.concatenate([angles, angles], axis=1)
    return (jnp.cos(angles), jnp.sin(angles))


def unrotate(gradient, positions):
    cosine, sine_table = rope_tables(positions, gradient.shape[1])
    half_width = gradient.shape[1] // 2
    turned = jnp.concatenate([-gradient[:, half_width:], gradient[:, :half_width]], axis=1)
    return gradient * cosine - turned * sine_table


def doc_ids(positions, lengths):
    doc_ends = jnp.cumsum(lengths)[:-1]
    return jnp.sum((positions[:, None] >= doc_ends[None, :]).astype(jnp.int32), axis=1)


def seq_to_stored(rows, block_order, device, ctx_size, per_device):
    width = rows.shape[1]
    first_block = device * per_device
    blocks = rows.reshape(per_device, BLOCK, width)
    pieces = []
    for slot_k in range(per_device):
        offset = slot_k * ctx_size // per_device
        slot_at = (device - offset) % ctx_size * per_device + slot_k
        local_index = block_order[slot_at] - first_block
        chosen = lax.dynamic_index_in_dim(blocks, local_index, 0, keepdims=False)
        if slot_k > 0:
            chosen = passed_along(chosen, "ctx", -offset)
        pieces.append(chosen)
    return jnp.concatenate(pieces, axis=0)


def stored_to_seq(rows, block_order, device, ctx_size, per_device):
    width = rows.shape[1]
    first_block = device * per_device
    blocks = rows.reshape(per_device, BLOCK, width)
    pieces = []
    local_ids = []
    for slot_k in range(per_device):
        offset = slot_k * ctx_size // per_device
        piece = blocks[slot_k]
        if slot_k > 0:
            piece = passed_along(piece, "ctx", offset)
        pieces.append(piece)
        sender_slot = (device - offset) % ctx_size * per_device + slot_k
        local_ids.append(block_order[sender_slot] - first_block)
    stacked = jnp.stack(pieces)
    index_list = jnp.stack(local_ids)
    choose = (jnp.arange(per_device, dtype=jnp.int32)[:, None] == index_list[None, :]).astype(
        rows.dtype
    )
    placed = jnp.einsum("pk,kbw->pbw", choose, stacked, preferred_element_type=jnp.float32)
    return placed.astype(rows.dtype).reshape(-1, width)


def contract_rows(left_rows, right_rows):
    return lax.dot_general(
        left_rows, right_rows, (((0,), (0,)), ((), ())), preferred_element_type=jnp.float32
    )


def contract_cols(left_rows, right_rows):
    return lax.dot_general(
        left_rows, right_rows, (((1,), (1,)), ((), ())), preferred_element_type=jnp.float32
    )


def block_scores(query_rows, key_rows, query_pos, query_doc, key_pos, key_doc, score_scale):
    scores = contract_cols(query_rows, key_rows) * score_scale
    visible = (query_doc[:, None] == key_doc[None, :]) & (key_pos[None, :] <= query_pos[:, None])
    return (scores, visible)


def body(grad_in, query, keyval, w_qkv, w_out, doc_lengths, order):
    section_grad_in = grad_in[0]
    stored_query = query[0]
    stored_keyval = keyval[0]
    in_weight = w_qkv[0]
    out_weight = w_out[0]
    lengths = doc_lengths[0]
    block_order = order[0]
    ctx_size = lax.axis_size("ctx")
    device = lax.axis_index("ctx")
    local_rows = section_grad_in.shape[0]
    head_dim = stored_keyval.shape[1] // 2
    group = stored_query.shape[1] // head_dim
    per_device = local_rows // BLOCK
    block_count = block_order.shape[0]
    seq_len = local_rows * ctx_size
    first_row = device * local_rows
    score_scale = 1.0 / math.sqrt(head_dim)
    key_block = math.gcd(seq_len, 512)
    key_steps = seq_len // key_block
    within = jnp.arange(BLOCK, dtype=jnp.int32)
    next_weight = lax.all_gather(passed_along_2(in_weight, "pipe", -1), "ctx", axis=0, tiled=True)
    out_grad = jnp.dot(
        section_grad_in,
        lax.all_gather(out_weight, "ctx", axis=0, tiled=True),
        preferred_element_type=jnp.float32,
    ).astype(jnp.bfloat16)
    local_out_grad = out_grad
    seq_query = stored_to_seq(stored_query, block_order, device, ctx_size, per_device)
    gathered = gathered_rows(stored_keyval, "ctx")
    gathered, grad_source = lax.optimization_barrier((gathered, section_grad_in))
    next_grad_in = passed_along_2(grad_source, "pipe", -1)
    slot_ids = jnp.arange(block_count, dtype=jnp.int32)
    inverse = jnp.sum(
        jnp.where(block_order[None, :] == slot_ids[:, None], slot_ids[None, :], 0), axis=1
    )
    all_keyval = gathered.reshape(block_count, BLOCK, 2 * head_dim)[inverse].reshape(
        seq_len, 2 * head_dim
    )
    key_positions = jnp.arange(seq_len, dtype=jnp.int32)
    key_docs = doc_ids(key_positions, lengths)
    query_pos = first_row + jnp.arange(local_rows, dtype=jnp.int32)
    query_doc = doc_ids(query_pos, lengths)
    flat_rows = local_rows * group
    flat_query = seq_query.reshape(flat_rows, head_dim)
    flat_grad = local_out_grad.reshape(flat_rows, head_dim)
    flat_pos = jnp.repeat(query_pos, group)
    flat_doc = jnp.repeat(query_doc, group)
    key_blocks = (
        all_keyval.reshape(key_steps, key_block, 2 * head_dim),
        key_positions.reshape(key_steps, key_block),
        key_docs.reshape(key_steps, key_block),
    )

    def running_total(carried, current):
        row_top, row_total, weighted = carried
        pair_rows, key_pos, key_doc = current
        scores, visible = block_scores(
            flat_query, pair_rows[:, :head_dim], flat_pos, flat_doc, key_pos, key_doc, score_scale
        )
        new_top = jnp.maximum(row_top, jnp.max(jnp.where(visible, scores, MASKED), axis=1))
        rescale = jnp.exp(row_top - new_top)
        weights = jnp.where(visible, jnp.exp(scores - new_top[:, None]), 0.0)
        row_total = row_total * rescale + jnp.sum(weights, axis=1)
        value_wide = pair_rows[:, head_dim:].astype(jnp.float32)
        weighted = weighted * rescale[:, None] + jnp.dot(
            weights, value_wide, precision=lax.Precision.HIGH
        )
        return ((new_top, row_total, weighted), None)

    start_top = jnp.full((flat_rows,), MASKED, jnp.float32)
    start_carry = (
        start_top,
        jnp.zeros((flat_rows,), jnp.float32),
        jnp.zeros((flat_rows, head_dim), jnp.float32),
    )
    (row_top, row_total, weighted), unused = lax.scan(running_total, start_carry, key_blocks)
    log_total = row_top + jnp.log(row_total)
    attn_out = weighted / row_total[:, None]
    row_delta = jnp.sum(flat_grad.astype(jnp.float32) * attn_out, axis=1)

    def grad_step(summed, current):
        pair_rows, key_pos, key_doc = current
        scores, visible = block_scores(
            flat_query, pair_rows[:, :head_dim], flat_pos, flat_doc, key_pos, key_doc, score_scale
        )
        attn_prob = jnp.where(visible, jnp.exp(scores - log_total[:, None]), 0.0)
        prob_grad = contract_cols(flat_grad, pair_rows[:, head_dim:])
        score_grad = (score_scale * attn_prob * (prob_grad - row_delta[:, None])).astype(
            jnp.bfloat16
        )
        summed = summed + jnp.dot(
            score_grad, pair_rows[:, :head_dim], preferred_element_type=jnp.float32
        )
        key_term = contract_rows(score_grad, flat_query)
        value_term = contract_rows(attn_prob.astype(jnp.bfloat16), flat_grad)
        return (summed, jnp.concatenate([key_term, value_term], axis=1))

    query_grad_rot, key_terms = lax.scan(
        grad_step, jnp.zeros((flat_rows, head_dim), jnp.float32), key_blocks
    )
    own_positions = first_row + jnp.arange(local_rows, dtype=jnp.int32)
    query_grad = (
        unrotate(query_grad_rot, flat_pos)
        .reshape(local_rows, group * head_dim)
        .astype(jnp.bfloat16)
    )
    next_query_grad = passed_along_2(query_grad, "pipe", -1)
    keyval_grad = summed_rows(
        key_terms.reshape(seq_len, 2 * head_dim).astype(jnp.bfloat16), "ctx"
    )
    key_grad = unrotate(keyval_grad[:, :head_dim], own_positions).astype(jnp.bfloat16)
    value_grad = keyval_grad[:, head_dim:].astype(jnp.bfloat16)
    next_keyval_grad = passed_along_2(
        jnp.concatenate([key_grad, value_grad], axis=1), "pipe", -1
    )
    next_qkv_grad = jnp.concatenate([next_query_grad, next_keyval_grad], axis=1)
    passed = projected_sum(next_qkv_grad, next_weight, next_grad_in)
    return passed[None]


def solution(mesh):
    return jax.shard_map(
        body,
        mesh=mesh,
        in_specs=(
            P("pipe", "ctx", None),
            P("pipe", "ctx", None),
            P("pipe", "ctx", None),
            P("pipe", "ctx", None),
            P("pipe", "ctx", None),
            P("pipe", None),
            P("pipe", None),
        ),
        out_specs=P("pipe", "ctx", None),
        check_vma=False,
    )
```

```python
import math

import jax
import jax.numpy as jnp
from jax import lax
from jax.experimental import pallas as pl
from jax.sharding import PartitionSpec as P

BLOCK = 128


ROPE_BASE = 500000.0
MASKED = -1e30


def passed_along(value, axis, steps):
    count = lax.axis_size(axis)
    pairs = [(source, (source + steps) % count) for source in range(count)]
    return lax.ppermute(value, axis, pairs)


def passed_along_2(value, axis, by):
    size = lax.axis_size(axis)
    pairs = [(i, i + by) for i in range(size) if 0 <= i + by < size]
    return lax.ppermute(value, axis, pairs)


def gathered_rows(value, axis):
    count = lax.axis_size(axis)
    spread = jnp.broadcast_to(value[None], (count,) + value.shape)
    return lax.all_to_all(spread, axis, 0, 0, tiled=False).reshape((-1,) + value.shape[1:])


def summed_rows(value, axis):
    count = lax.axis_size(axis)
    pieces = lax.all_to_all(value.reshape((count, -1) + value.shape[1:]), axis, 0, 0, tiled=False)
    return jnp.sum(pieces.astype(jnp.float32), axis=0)


def projection_kernel(grad_ref, weight_ref, base_ref, out_ref):
    product = lax.dot_general(
        grad_ref[...], weight_ref[...], (((1,), (1,)), ((), ())), preferred_element_type=jnp.float32
    )
    out_ref[...] = (base_ref[...].astype(jnp.float32) + product).astype(out_ref.dtype)


def projected_sum(grad_rows, weight, base, tile=4096):
    rows, inner = grad_rows.shape
    width = weight.shape[0]
    return pl.pallas_call(
        projection_kernel,
        grid=(width // tile,),
        in_specs=[
            pl.BlockSpec((rows, inner), lambda j: (0, 0)),
            pl.BlockSpec((tile, inner), lambda j: (j, 0)),
            pl.BlockSpec((rows, tile), lambda j: (0, j)),
        ],
        out_specs=pl.BlockSpec((rows, tile), lambda j: (0, j)),
        out_shape=jax.ShapeDtypeStruct((rows, width), base.dtype),
        cost_estimate=pl.CostEstimate(
            flops=2 * rows * inner * width,
            bytes_accessed=2 * (rows * inner + width * inner + 2 * rows * width),
            transcendentals=0,
        ),
    )(grad_rows, weight, base)


RING_OFFSETS = (0, -1, 1, -2)
RING_INDEX_OF_DELTA = (0, 2, 3, 1)


def ring_shift(value, phase, step, side):
    pairs = []
    for source in range(side * side):
        row, col = divmod(source, side)
        if phase == 0:
            target = row * side + (col + step) % side
        else:
            target = ((row + step) % side) * side + col
        pairs.append((source, target))
    return lax.ppermute(value, "ctx", pairs)


def ring_four(value, phase, side):
    from_left = ring_shift(value, phase, 1, side)
    from_right = ring_shift(value, phase, -1, side)
    from_far = ring_shift(from_left, phase, 1, side)
    return jnp.stack([value, from_left, from_right, from_far])


def ring_gather(value, first_phase, side):
    inner = ring_four(value, first_phase, side)
    return ring_four(inner, 1 - first_phase, side).reshape((side * side,) + value.shape)


def ring_position(device, source, first_phase, side):
    index_of_delta = jnp.asarray(RING_INDEX_OF_DELTA, jnp.int32)
    row_delta = index_of_delta[(source // side - device // side) % side]
    col_delta = index_of_delta[(source % side - device % side) % side]
    if first_phase == 0:
        return row_delta * side + col_delta
    return col_delta * side + row_delta


def rope_tables(positions, head_dim):
    half_width = head_dim // 2
    inv_freq = ROPE_BASE ** (-(jnp.arange(half_width, dtype=jnp.float32) * 2.0 / head_dim))
    angles = positions.astype(jnp.float32)[:, None] * inv_freq[None, :]
    angles = jnp.concatenate([angles, angles], axis=1)
    return (jnp.cos(angles), jnp.sin(angles))


def unrotate(gradient, positions):
    cosine, sine_table = rope_tables(positions, gradient.shape[1])
    half_width = gradient.shape[1] // 2
    turned = jnp.concatenate([-gradient[:, half_width:], gradient[:, :half_width]], axis=1)
    return gradient * cosine - turned * sine_table


def doc_ids(positions, lengths):
    doc_ends = jnp.cumsum(lengths)[:-1]
    return jnp.sum((positions[:, None] >= doc_ends[None, :]).astype(jnp.int32), axis=1)


def seq_to_stored(rows, block_order, device, ctx_size, per_device):
    width = rows.shape[1]
    first_block = device * per_device
    blocks = rows.reshape(per_device, BLOCK, width)
    pieces = []
    for slot_k in range(per_device):
        offset = slot_k * ctx_size // per_device
        slot_at = (device - offset) % ctx_size * per_device + slot_k
        local_index = block_order[slot_at] - first_block
        chosen = lax.dynamic_index_in_dim(blocks, local_index, 0, keepdims=False)
        if slot_k > 0:
            chosen = passed_along(chosen, "ctx", -offset)
        pieces.append(chosen)
    return jnp.concatenate(pieces, axis=0)


def stored_to_seq(rows, block_order, device, ctx_size, per_device):
    width = rows.shape[1]
    first_block = device * per_device
    blocks = rows.reshape(per_device, BLOCK, width)
    pieces = []
    local_ids = []
    for slot_k in range(per_device):
        offset = slot_k * ctx_size // per_device
        piece = blocks[slot_k]
        if slot_k > 0:
            piece = passed_along(piece, "ctx", offset)
        pieces.append(piece)
        sender_slot = (device - offset) % ctx_size * per_device + slot_k
        local_ids.append(block_order[sender_slot] - first_block)
    stacked = jnp.stack(pieces)
    index_list = jnp.stack(local_ids)
    choose = (jnp.arange(per_device, dtype=jnp.int32)[:, None] == index_list[None, :]).astype(
        rows.dtype
    )
    placed = jnp.einsum("pk,kbw->pbw", choose, stacked, preferred_element_type=jnp.float32)
    return placed.astype(rows.dtype).reshape(-1, width)


def contract_rows(left_rows, right_rows):
    return lax.dot_general(
        left_rows, right_rows, (((0,), (0,)), ((), ())), preferred_element_type=jnp.float32
    )


def contract_cols(left_rows, right_rows):
    return lax.dot_general(
        left_rows, right_rows, (((1,), (1,)), ((), ())), preferred_element_type=jnp.float32
    )


def block_scores(query_rows, key_rows, query_pos, query_doc, key_pos, key_doc, score_scale):
    scores = contract_cols(query_rows, key_rows) * score_scale
    visible = (query_doc[:, None] == key_doc[None, :]) & (key_pos[None, :] <= query_pos[:, None])
    return (scores, visible)


def body(grad_in, query, keyval, w_qkv, w_out, doc_lengths, order):
    section_grad_in = grad_in[0]
    stored_query = query[0]
    stored_keyval = keyval[0]
    in_weight = w_qkv[0]
    out_weight = w_out[0]
    lengths = doc_lengths[0]
    block_order = order[0]
    ctx_size = lax.axis_size("ctx")
    device = lax.axis_index("ctx")
    local_rows = section_grad_in.shape[0]
    head_dim = stored_keyval.shape[1] // 2
    group = stored_query.shape[1] // head_dim
    per_device = local_rows // BLOCK
    block_count = block_order.shape[0]
    seq_len = local_rows * ctx_size
    first_row = device * local_rows
    score_scale = 1.0 / math.sqrt(head_dim)
    key_block = math.gcd(seq_len, 512)
    key_steps = seq_len // key_block
    within = jnp.arange(BLOCK, dtype=jnp.int32)
    next_weight = lax.all_gather(passed_along_2(in_weight, "pipe", -1), "ctx", axis=0, tiled=True)
    out_grad = jnp.dot(
        section_grad_in,
        lax.all_gather(out_weight, "ctx", axis=0, tiled=True),
        preferred_element_type=jnp.float32,
    ).astype(jnp.bfloat16)
    local_out_grad = out_grad
    seq_query = stored_to_seq(stored_query, block_order, device, ctx_size, per_device)
    side = math.isqrt(ctx_size)
    slot_ids = jnp.arange(block_count, dtype=jnp.int32)
    if side == len(RING_OFFSETS) and per_device == 2:
        gathered = jnp.concatenate(
            [
                ring_gather(stored_keyval[:BLOCK], 0, side),
                ring_gather(stored_keyval[BLOCK:], 1, side),
            ]
        ).reshape(seq_len, 2 * head_dim)
        holder = slot_ids // per_device
        slot_place = jnp.where(
            slot_ids % per_device == 0,
            ring_position(device, holder, 0, side),
            ctx_size + ring_position(device, holder, 1, side),
        )
    else:
        gathered = gathered_rows(stored_keyval, "ctx")
        slot_place = slot_ids
    gathered, grad_source = lax.optimization_barrier((gathered, section_grad_in))
    next_grad_in = passed_along_2(grad_source, "pipe", -1)
    inverse = jnp.sum(
        jnp.where(block_order[None, :] == slot_ids[:, None], slot_place[None, :], 0), axis=1
    )
    all_keyval = gathered.reshape(block_count, BLOCK, 2 * head_dim)[inverse].reshape(
        seq_len, 2 * head_dim
    )
    key_positions = jnp.arange(seq_len, dtype=jnp.int32)
    key_docs = doc_ids(key_positions, lengths)
    query_pos = first_row + jnp.arange(local_rows, dtype=jnp.int32)
    query_doc = doc_ids(query_pos, lengths)
    flat_rows = local_rows * group
    flat_query = seq_query.reshape(flat_rows, head_dim)
    flat_grad = local_out_grad.reshape(flat_rows, head_dim)
    flat_pos = jnp.repeat(query_pos, group)
    flat_doc = jnp.repeat(query_doc, group)
    key_blocks = (
        all_keyval.reshape(key_steps, key_block, 2 * head_dim),
        key_positions.reshape(key_steps, key_block),
        key_docs.reshape(key_steps, key_block),
    )

    def running_total(carried, current):
        row_top, row_total, weighted = carried
        pair_rows, key_pos, key_doc = current
        scores, visible = block_scores(
            flat_query, pair_rows[:, :head_dim], flat_pos, flat_doc, key_pos, key_doc, score_scale
        )
        new_top = jnp.maximum(row_top, jnp.max(jnp.where(visible, scores, MASKED), axis=1))
        rescale = jnp.exp(row_top - new_top)
        weights = jnp.where(visible, jnp.exp(scores - new_top[:, None]), 0.0)
        row_total = row_total * rescale + jnp.sum(weights, axis=1)
        value_wide = pair_rows[:, head_dim:].astype(jnp.float32)
        weighted = weighted * rescale[:, None] + jnp.dot(
            weights, value_wide, precision=lax.Precision.HIGH
        )
        return ((new_top, row_total, weighted), None)

    start_top = jnp.full((flat_rows,), MASKED, jnp.float32)
    start_carry = (
        start_top,
        jnp.zeros((flat_rows,), jnp.float32),
        jnp.zeros((flat_rows, head_dim), jnp.float32),
    )
    (row_top, row_total, weighted), unused = lax.scan(running_total, start_carry, key_blocks)
    log_total = row_top + jnp.log(row_total)
    attn_out = weighted / row_total[:, None]
    row_delta = jnp.sum(flat_grad.astype(jnp.float32) * attn_out, axis=1)

    def grad_step(summed, current):
        pair_rows, key_pos, key_doc = current
        scores, visible = block_scores(
            flat_query, pair_rows[:, :head_dim], flat_pos, flat_doc, key_pos, key_doc, score_scale
        )
        attn_prob = jnp.where(visible, jnp.exp(scores - log_total[:, None]), 0.0)
        prob_grad = contract_cols(flat_grad, pair_rows[:, head_dim:])
        score_grad = (score_scale * attn_prob * (prob_grad - row_delta[:, None])).astype(
            jnp.bfloat16
        )
        summed = summed + jnp.dot(
            score_grad, pair_rows[:, :head_dim], preferred_element_type=jnp.float32
        )
        key_term = contract_rows(score_grad, flat_query)
        value_term = contract_rows(attn_prob.astype(jnp.bfloat16), flat_grad)
        return (summed, jnp.concatenate([key_term, value_term], axis=1))

    query_grad_rot, key_terms = lax.scan(
        grad_step, jnp.zeros((flat_rows, head_dim), jnp.float32), key_blocks
    )
    own_positions = first_row + jnp.arange(local_rows, dtype=jnp.int32)
    query_grad = (
        unrotate(query_grad_rot, flat_pos)
        .reshape(local_rows, group * head_dim)
        .astype(jnp.bfloat16)
    )
    next_query_grad = passed_along_2(query_grad, "pipe", -1)
    keyval_grad = summed_rows(
        key_terms.reshape(seq_len, 2 * head_dim).astype(jnp.bfloat16), "ctx"
    )
    key_grad = unrotate(keyval_grad[:, :head_dim], own_positions).astype(jnp.bfloat16)
    value_grad = keyval_grad[:, head_dim:].astype(jnp.bfloat16)
    next_keyval_grad = passed_along_2(
        jnp.concatenate([key_grad, value_grad], axis=1), "pipe", -1
    )
    next_qkv_grad = jnp.concatenate([next_query_grad, next_keyval_grad], axis=1)
    passed = projected_sum(next_qkv_grad, next_weight, next_grad_in)
    return passed[None]


def solution(mesh):
    return jax.shard_map(
        body,
        mesh=mesh,
        in_specs=(
            P("pipe", "ctx", None),
            P("pipe", "ctx", None),
            P("pipe", "ctx", None),
            P("pipe", "ctx", None),
            P("pipe", "ctx", None),
            P("pipe", None),
            P("pipe", None),
        ),
        out_specs=P("pipe", "ctx", None),
        check_vma=False,
    )
```

```python
import math

import jax
import jax.numpy as jnp
from jax import lax
from jax.experimental import pallas as pl
from jax.sharding import PartitionSpec as P

BLOCK = 128


ROPE_BASE = 500000.0
MASKED = -1e30


def passed_along(value, axis, steps):
    count = lax.axis_size(axis)
    pairs = [(source, (source + steps) % count) for source in range(count)]
    return lax.ppermute(value, axis, pairs)


def passed_along_2(value, axis, by):
    size = lax.axis_size(axis)
    pairs = [(i, i + by) for i in range(size) if 0 <= i + by < size]
    return lax.ppermute(value, axis, pairs)


def gathered_rows(value, axis):
    count = lax.axis_size(axis)
    spread = jnp.broadcast_to(value[None], (count,) + value.shape)
    return lax.all_to_all(spread, axis, 0, 0, tiled=False).reshape((-1,) + value.shape[1:])


def summed_rows(value, axis):
    count = lax.axis_size(axis)
    pieces = lax.all_to_all(value.reshape((count, -1) + value.shape[1:]), axis, 0, 0, tiled=False)
    return jnp.sum(pieces.astype(jnp.float32), axis=0)


def projection_kernel(grad_ref, weight_ref, base_ref, out_ref):
    product = lax.dot_general(
        grad_ref[...], weight_ref[...], (((1,), (1,)), ((), ())), preferred_element_type=jnp.float32
    )
    out_ref[...] = (base_ref[...].astype(jnp.float32) + product).astype(out_ref.dtype)


def projected_sum(grad_rows, weight, base, tile=4096):
    rows, inner = grad_rows.shape
    width = weight.shape[0]
    return pl.pallas_call(
        projection_kernel,
        grid=(width // tile,),
        in_specs=[
            pl.BlockSpec((rows, inner), lambda j: (0, 0)),
            pl.BlockSpec((tile, inner), lambda j: (j, 0)),
            pl.BlockSpec((rows, tile), lambda j: (0, j)),
        ],
        out_specs=pl.BlockSpec((rows, tile), lambda j: (0, j)),
        out_shape=jax.ShapeDtypeStruct((rows, width), base.dtype),
        cost_estimate=pl.CostEstimate(
            flops=2 * rows * inner * width,
            bytes_accessed=2 * (rows * inner + width * inner + 2 * rows * width),
            transcendentals=0,
        ),
    )(grad_rows, weight, base)


RING_OFFSETS = (0, -1, 1, -2)
RING_INDEX_OF_DELTA = (0, 2, 3, 1)


def ring_shift(value, phase, step, side):
    pairs = []
    for source in range(side * side):
        row, col = divmod(source, side)
        if phase == 0:
            target = row * side + (col + step) % side
        else:
            target = ((row + step) % side) * side + col
        pairs.append((source, target))
    return lax.ppermute(value, "ctx", pairs)


def ring_four(value, phase, side):
    from_left = ring_shift(value, phase, 1, side)
    from_right = ring_shift(value, phase, -1, side)
    from_far = ring_shift(from_left, phase, 1, side)
    return jnp.stack([value, from_left, from_right, from_far])


def ring_gather(value, first_phase, side):
    inner = ring_four(value, first_phase, side)
    return ring_four(inner, 1 - first_phase, side).reshape((side * side,) + value.shape)


def ring_reduce(chunks, phase, device, side):
    me = device % side if phase == 0 else device // side
    rel = lax.dynamic_slice_in_dim(jnp.concatenate([chunks, chunks]), me, side, axis=0)
    from_far = ring_shift(rel[2].astype(jnp.bfloat16), phase, 1, side)
    from_right = ring_shift(rel[3].astype(jnp.bfloat16), phase, -1, side)
    carried = (rel[1] + from_far.astype(jnp.float32)).astype(jnp.bfloat16)
    from_left = ring_shift(carried, phase, 1, side)
    return rel[0] + from_right.astype(jnp.float32) + from_left.astype(jnp.float32)


def ring_scatter_sum(rows, device, side):
    region = rows.shape[0] // (side * side)
    width = rows.shape[1]
    tiles = rows.reshape(side, side, region, width)
    half = width // 2
    first = ring_reduce(jnp.moveaxis(tiles[..., :half], 1, 0), 0, device, side)
    first = ring_reduce(first, 1, device, side)
    second = ring_reduce(tiles[..., half:], 1, device, side)
    second = ring_reduce(second, 0, device, side)
    return jnp.concatenate([first, second], axis=1)


def ring_position(device, source, first_phase, side):
    index_of_delta = jnp.asarray(RING_INDEX_OF_DELTA, jnp.int32)
    row_delta = index_of_delta[(source // side - device // side) % side]
    col_delta = index_of_delta[(source % side - device % side) % side]
    if first_phase == 0:
        return row_delta * side + col_delta
    return col_delta * side + row_delta


def rope_tables(positions, head_dim):
    half_width = head_dim // 2
    inv_freq = ROPE_BASE ** (-(jnp.arange(half_width, dtype=jnp.float32) * 2.0 / head_dim))
    angles = positions.astype(jnp.float32)[:, None] * inv_freq[None, :]
    angles = jnp.concatenate([angles, angles], axis=1)
    return (jnp.cos(angles), jnp.sin(angles))


def unrotate(gradient, positions):
    cosine, sine_table = rope_tables(positions, gradient.shape[1])
    half_width = gradient.shape[1] // 2
    turned = jnp.concatenate([-gradient[:, half_width:], gradient[:, :half_width]], axis=1)
    return gradient * cosine - turned * sine_table


def doc_ids(positions, lengths):
    doc_ends = jnp.cumsum(lengths)[:-1]
    return jnp.sum((positions[:, None] >= doc_ends[None, :]).astype(jnp.int32), axis=1)


def seq_to_stored(rows, block_order, device, ctx_size, per_device):
    width = rows.shape[1]
    first_block = device * per_device
    blocks = rows.reshape(per_device, BLOCK, width)
    pieces = []
    for slot_k in range(per_device):
        offset = slot_k * ctx_size // per_device
        slot_at = (device - offset) % ctx_size * per_device + slot_k
        local_index = block_order[slot_at] - first_block
        chosen = lax.dynamic_index_in_dim(blocks, local_index, 0, keepdims=False)
        if slot_k > 0:
            chosen = passed_along(chosen, "ctx", -offset)
        pieces.append(chosen)
    return jnp.concatenate(pieces, axis=0)


def stored_to_seq(rows, block_order, device, ctx_size, per_device):
    width = rows.shape[1]
    first_block = device * per_device
    blocks = rows.reshape(per_device, BLOCK, width)
    pieces = []
    local_ids = []
    for slot_k in range(per_device):
        offset = slot_k * ctx_size // per_device
        piece = blocks[slot_k]
        if slot_k > 0:
            piece = passed_along(piece, "ctx", offset)
        pieces.append(piece)
        sender_slot = (device - offset) % ctx_size * per_device + slot_k
        local_ids.append(block_order[sender_slot] - first_block)
    stacked = jnp.stack(pieces)
    index_list = jnp.stack(local_ids)
    choose = (jnp.arange(per_device, dtype=jnp.int32)[:, None] == index_list[None, :]).astype(
        rows.dtype
    )
    placed = jnp.einsum("pk,kbw->pbw", choose, stacked, preferred_element_type=jnp.float32)
    return placed.astype(rows.dtype).reshape(-1, width)


def contract_rows(left_rows, right_rows):
    return lax.dot_general(
        left_rows, right_rows, (((0,), (0,)), ((), ())), preferred_element_type=jnp.float32
    )


def contract_cols(left_rows, right_rows):
    return lax.dot_general(
        left_rows, right_rows, (((1,), (1,)), ((), ())), preferred_element_type=jnp.float32
    )


def block_scores(query_rows, key_rows, query_pos, query_doc, key_pos, key_doc, score_scale):
    scores = contract_cols(query_rows, key_rows) * score_scale
    visible = (query_doc[:, None] == key_doc[None, :]) & (key_pos[None, :] <= query_pos[:, None])
    return (scores, visible)


def body(grad_in, query, keyval, w_qkv, w_out, doc_lengths, order):
    section_grad_in = grad_in[0]
    stored_query = query[0]
    stored_keyval = keyval[0]
    in_weight = w_qkv[0]
    out_weight = w_out[0]
    lengths = doc_lengths[0]
    block_order = order[0]
    ctx_size = lax.axis_size("ctx")
    device = lax.axis_index("ctx")
    local_rows = section_grad_in.shape[0]
    head_dim = stored_keyval.shape[1] // 2
    group = stored_query.shape[1] // head_dim
    per_device = local_rows // BLOCK
    block_count = block_order.shape[0]
    seq_len = local_rows * ctx_size
    first_row = device * local_rows
    score_scale = 1.0 / math.sqrt(head_dim)
    key_block = math.gcd(seq_len, 512)
    key_steps = seq_len // key_block
    within = jnp.arange(BLOCK, dtype=jnp.int32)
    next_weight = lax.all_gather(passed_along_2(in_weight, "pipe", -1), "ctx", axis=0, tiled=True)
    out_grad = jnp.dot(
        section_grad_in,
        lax.all_gather(out_weight, "ctx", axis=0, tiled=True),
        preferred_element_type=jnp.float32,
    ).astype(jnp.bfloat16)
    local_out_grad = out_grad
    seq_query = stored_to_seq(stored_query, block_order, device, ctx_size, per_device)
    side = math.isqrt(ctx_size)
    slot_ids = jnp.arange(block_count, dtype=jnp.int32)
    if side == len(RING_OFFSETS) and per_device == 2:
        gathered = jnp.concatenate(
            [
                ring_gather(stored_keyval[:BLOCK], 0, side),
                ring_gather(stored_keyval[BLOCK:], 1, side),
            ]
        ).reshape(seq_len, 2 * head_dim)
        holder = slot_ids // per_device
        slot_place = jnp.where(
            slot_ids % per_device == 0,
            ring_position(device, holder, 0, side),
            ctx_size + ring_position(device, holder, 1, side),
        )
    else:
        gathered = gathered_rows(stored_keyval, "ctx")
        slot_place = slot_ids
    gathered, grad_source = lax.optimization_barrier((gathered, section_grad_in))
    next_grad_in = passed_along_2(grad_source, "pipe", -1)
    inverse = jnp.sum(
        jnp.where(block_order[None, :] == slot_ids[:, None], slot_place[None, :], 0), axis=1
    )
    all_keyval = gathered.reshape(block_count, BLOCK, 2 * head_dim)[inverse].reshape(
        seq_len, 2 * head_dim
    )
    key_positions = jnp.arange(seq_len, dtype=jnp.int32)
    key_docs = doc_ids(key_positions, lengths)
    query_pos = first_row + jnp.arange(local_rows, dtype=jnp.int32)
    query_doc = doc_ids(query_pos, lengths)
    flat_rows = local_rows * group
    flat_query = seq_query.reshape(flat_rows, head_dim)
    flat_grad = local_out_grad.reshape(flat_rows, head_dim)
    flat_pos = jnp.repeat(query_pos, group)
    flat_doc = jnp.repeat(query_doc, group)
    key_blocks = (
        all_keyval.reshape(key_steps, key_block, 2 * head_dim),
        key_positions.reshape(key_steps, key_block),
        key_docs.reshape(key_steps, key_block),
    )

    def running_total(carried, current):
        row_top, row_total, weighted = carried
        pair_rows, key_pos, key_doc = current
        scores, visible = block_scores(
            flat_query, pair_rows[:, :head_dim], flat_pos, flat_doc, key_pos, key_doc, score_scale
        )
        new_top = jnp.maximum(row_top, jnp.max(jnp.where(visible, scores, MASKED), axis=1))
        rescale = jnp.exp(row_top - new_top)
        weights = jnp.where(visible, jnp.exp(scores - new_top[:, None]), 0.0)
        row_total = row_total * rescale + jnp.sum(weights, axis=1)
        value_wide = pair_rows[:, head_dim:].astype(jnp.float32)
        weighted = weighted * rescale[:, None] + jnp.dot(
            weights, value_wide, precision=lax.Precision.HIGH
        )
        return ((new_top, row_total, weighted), None)

    start_top = jnp.full((flat_rows,), MASKED, jnp.float32)
    start_carry = (
        start_top,
        jnp.zeros((flat_rows,), jnp.float32),
        jnp.zeros((flat_rows, head_dim), jnp.float32),
    )
    (row_top, row_total, weighted), unused = lax.scan(running_total, start_carry, key_blocks)
    log_total = row_top + jnp.log(row_total)
    attn_out = weighted / row_total[:, None]
    row_delta = jnp.sum(flat_grad.astype(jnp.float32) * attn_out, axis=1)

    def grad_step(summed, current):
        pair_rows, key_pos, key_doc = current
        scores, visible = block_scores(
            flat_query, pair_rows[:, :head_dim], flat_pos, flat_doc, key_pos, key_doc, score_scale
        )
        attn_prob = jnp.where(visible, jnp.exp(scores - log_total[:, None]), 0.0)
        prob_grad = contract_cols(flat_grad, pair_rows[:, head_dim:])
        score_grad = (score_scale * attn_prob * (prob_grad - row_delta[:, None])).astype(
            jnp.bfloat16
        )
        summed = summed + jnp.dot(
            score_grad, pair_rows[:, :head_dim], preferred_element_type=jnp.float32
        )
        key_term = contract_rows(score_grad, flat_query)
        value_term = contract_rows(attn_prob.astype(jnp.bfloat16), flat_grad)
        return (summed, jnp.concatenate([key_term, value_term], axis=1))

    query_grad_rot, key_terms = lax.scan(
        grad_step, jnp.zeros((flat_rows, head_dim), jnp.float32), key_blocks
    )
    own_positions = first_row + jnp.arange(local_rows, dtype=jnp.int32)
    query_grad = (
        unrotate(query_grad_rot, flat_pos)
        .reshape(local_rows, group * head_dim)
        .astype(jnp.bfloat16)
    )
    next_query_grad = passed_along_2(query_grad, "pipe", -1)
    if side == len(RING_OFFSETS):
        keyval_grad = ring_scatter_sum(key_terms.reshape(seq_len, 2 * head_dim), device, side)
    else:
        keyval_grad = summed_rows(
            key_terms.reshape(seq_len, 2 * head_dim).astype(jnp.bfloat16), "ctx"
        )
    key_grad = unrotate(keyval_grad[:, :head_dim], own_positions).astype(jnp.bfloat16)
    value_grad = keyval_grad[:, head_dim:].astype(jnp.bfloat16)
    next_keyval_grad = passed_along_2(
        jnp.concatenate([key_grad, value_grad], axis=1), "pipe", -1
    )
    next_qkv_grad = jnp.concatenate([next_query_grad, next_keyval_grad], axis=1)
    passed = projected_sum(next_qkv_grad, next_weight, next_grad_in)
    return passed[None]


def solution(mesh):
    return jax.shard_map(
        body,
        mesh=mesh,
        in_specs=(
            P("pipe", "ctx", None),
            P("pipe", "ctx", None),
            P("pipe", "ctx", None),
            P("pipe", "ctx", None),
            P("pipe", "ctx", None),
            P("pipe", None),
            P("pipe", None),
        ),
        out_specs=P("pipe", "ctx", None),
        check_vma=False,
    )
```

```python
import math

import jax
import jax.numpy as jnp
from jax import lax
from jax.experimental import pallas as pl
from jax.sharding import PartitionSpec as P

BLOCK = 128


ROPE_BASE = 500000.0
MASKED = -1e30


def passed_along(value, axis, steps):
    count = lax.axis_size(axis)
    pairs = [(source, (source + steps) % count) for source in range(count)]
    return lax.ppermute(value, axis, pairs)


def passed_along_2(value, axis, by):
    size = lax.axis_size(axis)
    pairs = [(i, i + by) for i in range(size) if 0 <= i + by < size]
    return lax.ppermute(value, axis, pairs)


def gathered_rows(value, axis):
    count = lax.axis_size(axis)
    spread = jnp.broadcast_to(value[None], (count,) + value.shape)
    return lax.all_to_all(spread, axis, 0, 0, tiled=False).reshape((-1,) + value.shape[1:])


def summed_rows(value, axis):
    count = lax.axis_size(axis)
    pieces = lax.all_to_all(value.reshape((count, -1) + value.shape[1:]), axis, 0, 0, tiled=False)
    return jnp.sum(pieces.astype(jnp.float32), axis=0)


def projection_kernel(grad_ref, weight_ref, base_ref, out_ref):
    product = lax.dot_general(
        grad_ref[...], weight_ref[...], (((1,), (1,)), ((), ())), preferred_element_type=jnp.float32
    )
    out_ref[...] = (base_ref[...].astype(jnp.float32) + product).astype(out_ref.dtype)


def projected_sum(grad_rows, weight, base, tile=4096):
    rows, inner = grad_rows.shape
    width = weight.shape[0]
    return pl.pallas_call(
        projection_kernel,
        grid=(width // tile,),
        in_specs=[
            pl.BlockSpec((rows, inner), lambda j: (0, 0)),
            pl.BlockSpec((tile, inner), lambda j: (j, 0)),
            pl.BlockSpec((rows, tile), lambda j: (0, j)),
        ],
        out_specs=pl.BlockSpec((rows, tile), lambda j: (0, j)),
        out_shape=jax.ShapeDtypeStruct((rows, width), base.dtype),
        cost_estimate=pl.CostEstimate(
            flops=2 * rows * inner * width,
            bytes_accessed=2 * (rows * inner + width * inner + 2 * rows * width),
            transcendentals=0,
        ),
    )(grad_rows, weight, base)


RING_OFFSETS = (0, -1, 1, -2)
RING_INDEX_OF_DELTA = (0, 2, 3, 1)


def ring_shift(value, phase, step, side):
    pairs = []
    for source in range(side * side):
        row, col = divmod(source, side)
        if phase == 0:
            target = row * side + (col + step) % side
        else:
            target = ((row + step) % side) * side + col
        pairs.append((source, target))
    return lax.ppermute(value, "ctx", pairs)


def ring_four(value, phase, side):
    from_left = ring_shift(value, phase, 1, side)
    from_right = ring_shift(value, phase, -1, side)
    from_far = ring_shift(value, phase, 2, side)
    return jnp.stack([value, from_left, from_right, from_far])


def ring_gather(value, first_phase, side):
    inner = ring_four(value, first_phase, side)
    return ring_four(inner, 1 - first_phase, side).reshape((side * side,) + value.shape)


def ring_reduce(chunks, phase, device, side):
    me = device % side if phase == 0 else device // side
    rel = lax.dynamic_slice_in_dim(jnp.concatenate([chunks, chunks]), me, side, axis=0)
    from_left = ring_shift(rel[1].astype(jnp.bfloat16), phase, 1, side)
    from_far = ring_shift(rel[2].astype(jnp.bfloat16), phase, 2, side)
    from_right = ring_shift(rel[3].astype(jnp.bfloat16), phase, -1, side)
    return (
        rel[0]
        + from_right.astype(jnp.float32)
        + from_far.astype(jnp.float32)
        + from_left.astype(jnp.float32)
    )


def ring_scatter_sum(rows, device, side):
    region = rows.shape[0] // (side * side)
    width = rows.shape[1]
    tiles = rows.reshape(side, side, region, width)
    half = width // 2
    first = ring_reduce(jnp.moveaxis(tiles[..., :half], 1, 0), 0, device, side)
    first = ring_reduce(first, 1, device, side)
    second = ring_reduce(tiles[..., half:], 1, device, side)
    second = ring_reduce(second, 0, device, side)
    return jnp.concatenate([first, second], axis=1)


def ring_position(device, source, first_phase, side):
    index_of_delta = jnp.asarray(RING_INDEX_OF_DELTA, jnp.int32)
    row_delta = index_of_delta[(source // side - device // side) % side]
    col_delta = index_of_delta[(source % side - device % side) % side]
    if first_phase == 0:
        return row_delta * side + col_delta
    return col_delta * side + row_delta


def rope_tables(positions, head_dim):
    half_width = head_dim // 2
    inv_freq = ROPE_BASE ** (-(jnp.arange(half_width, dtype=jnp.float32) * 2.0 / head_dim))
    angles = positions.astype(jnp.float32)[:, None] * inv_freq[None, :]
    angles = jnp.concatenate([angles, angles], axis=1)
    return (jnp.cos(angles), jnp.sin(angles))


def unrotate(gradient, positions):
    cosine, sine_table = rope_tables(positions, gradient.shape[1])
    half_width = gradient.shape[1] // 2
    turned = jnp.concatenate([-gradient[:, half_width:], gradient[:, :half_width]], axis=1)
    return gradient * cosine - turned * sine_table


def doc_ids(positions, lengths):
    doc_ends = jnp.cumsum(lengths)[:-1]
    return jnp.sum((positions[:, None] >= doc_ends[None, :]).astype(jnp.int32), axis=1)


def seq_to_stored(rows, block_order, device, ctx_size, per_device):
    width = rows.shape[1]
    first_block = device * per_device
    blocks = rows.reshape(per_device, BLOCK, width)
    pieces = []
    for slot_k in range(per_device):
        offset = slot_k * ctx_size // per_device
        slot_at = (device - offset) % ctx_size * per_device + slot_k
        local_index = block_order[slot_at] - first_block
        chosen = lax.dynamic_index_in_dim(blocks, local_index, 0, keepdims=False)
        if slot_k > 0:
            chosen = passed_along(chosen, "ctx", -offset)
        pieces.append(chosen)
    return jnp.concatenate(pieces, axis=0)


def stored_to_seq(rows, block_order, device, ctx_size, per_device):
    width = rows.shape[1]
    first_block = device * per_device
    blocks = rows.reshape(per_device, BLOCK, width)
    pieces = []
    local_ids = []
    for slot_k in range(per_device):
        offset = slot_k * ctx_size // per_device
        piece = blocks[slot_k]
        if slot_k > 0:
            piece = passed_along(piece, "ctx", offset)
        pieces.append(piece)
        sender_slot = (device - offset) % ctx_size * per_device + slot_k
        local_ids.append(block_order[sender_slot] - first_block)
    stacked = jnp.stack(pieces)
    index_list = jnp.stack(local_ids)
    choose = (jnp.arange(per_device, dtype=jnp.int32)[:, None] == index_list[None, :]).astype(
        rows.dtype
    )
    placed = jnp.einsum("pk,kbw->pbw", choose, stacked, preferred_element_type=jnp.float32)
    return placed.astype(rows.dtype).reshape(-1, width)


def contract_rows(left_rows, right_rows):
    return lax.dot_general(
        left_rows, right_rows, (((0,), (0,)), ((), ())), preferred_element_type=jnp.float32
    )


def contract_cols(left_rows, right_rows):
    return lax.dot_general(
        left_rows, right_rows, (((1,), (1,)), ((), ())), preferred_element_type=jnp.float32
    )


def block_scores(query_rows, key_rows, query_pos, query_doc, key_pos, key_doc, score_scale):
    scores = contract_cols(query_rows, key_rows) * score_scale
    visible = (query_doc[:, None] == key_doc[None, :]) & (key_pos[None, :] <= query_pos[:, None])
    return (scores, visible)


def body(grad_in, query, keyval, w_qkv, w_out, doc_lengths, order):
    section_grad_in = grad_in[0]
    stored_query = query[0]
    stored_keyval = keyval[0]
    in_weight = w_qkv[0]
    out_weight = w_out[0]
    lengths = doc_lengths[0]
    block_order = order[0]
    ctx_size = lax.axis_size("ctx")
    device = lax.axis_index("ctx")
    local_rows = section_grad_in.shape[0]
    head_dim = stored_keyval.shape[1] // 2
    group = stored_query.shape[1] // head_dim
    per_device = local_rows // BLOCK
    block_count = block_order.shape[0]
    seq_len = local_rows * ctx_size
    first_row = device * local_rows
    score_scale = 1.0 / math.sqrt(head_dim)
    key_block = math.gcd(seq_len, 512)
    key_steps = seq_len // key_block
    within = jnp.arange(BLOCK, dtype=jnp.int32)
    next_weight = lax.all_gather(passed_along_2(in_weight, "pipe", -1), "ctx", axis=0, tiled=True)
    out_grad = jnp.dot(
        section_grad_in,
        lax.all_gather(out_weight, "ctx", axis=0, tiled=True),
        preferred_element_type=jnp.float32,
    ).astype(jnp.bfloat16)
    local_out_grad = out_grad
    seq_query = stored_to_seq(stored_query, block_order, device, ctx_size, per_device)
    side = math.isqrt(ctx_size)
    slot_ids = jnp.arange(block_count, dtype=jnp.int32)
    if side == len(RING_OFFSETS) and per_device == 2:
        gathered = jnp.concatenate(
            [
                ring_gather(stored_keyval[:BLOCK], 0, side),
                ring_gather(stored_keyval[BLOCK:], 1, side),
            ]
        ).reshape(seq_len, 2 * head_dim)
        holder = slot_ids // per_device
        slot_place = jnp.where(
            slot_ids % per_device == 0,
            ring_position(device, holder, 0, side),
            ctx_size + ring_position(device, holder, 1, side),
        )
    else:
        gathered = gathered_rows(stored_keyval, "ctx")
        slot_place = slot_ids
    gathered, grad_source = lax.optimization_barrier((gathered, section_grad_in))
    next_grad_in = passed_along_2(grad_source, "pipe", -1)
    inverse = jnp.sum(
        jnp.where(block_order[None, :] == slot_ids[:, None], slot_place[None, :], 0), axis=1
    )
    all_keyval = gathered.reshape(block_count, BLOCK, 2 * head_dim)[inverse].reshape(
        seq_len, 2 * head_dim
    )
    key_positions = jnp.arange(seq_len, dtype=jnp.int32)
    key_docs = doc_ids(key_positions, lengths)
    query_pos = first_row + jnp.arange(local_rows, dtype=jnp.int32)
    query_doc = doc_ids(query_pos, lengths)
    flat_rows = local_rows * group
    flat_query = seq_query.reshape(flat_rows, head_dim)
    flat_grad = local_out_grad.reshape(flat_rows, head_dim)
    flat_pos = jnp.repeat(query_pos, group)
    flat_doc = jnp.repeat(query_doc, group)
    key_blocks = (
        all_keyval.reshape(key_steps, key_block, 2 * head_dim),
        key_positions.reshape(key_steps, key_block),
        key_docs.reshape(key_steps, key_block),
    )

    def running_total(carried, current):
        row_top, row_total, weighted = carried
        pair_rows, key_pos, key_doc = current
        scores, visible = block_scores(
            flat_query, pair_rows[:, :head_dim], flat_pos, flat_doc, key_pos, key_doc, score_scale
        )
        new_top = jnp.maximum(row_top, jnp.max(jnp.where(visible, scores, MASKED), axis=1))
        rescale = jnp.exp(row_top - new_top)
        weights = jnp.where(visible, jnp.exp(scores - new_top[:, None]), 0.0)
        row_total = row_total * rescale + jnp.sum(weights, axis=1)
        value_wide = pair_rows[:, head_dim:].astype(jnp.float32)
        weighted = weighted * rescale[:, None] + jnp.dot(
            weights, value_wide, precision=lax.Precision.HIGH
        )
        return ((new_top, row_total, weighted), None)

    start_top = jnp.full((flat_rows,), MASKED, jnp.float32)
    start_carry = (
        start_top,
        jnp.zeros((flat_rows,), jnp.float32),
        jnp.zeros((flat_rows, head_dim), jnp.float32),
    )
    (row_top, row_total, weighted), unused = lax.scan(running_total, start_carry, key_blocks)
    log_total = row_top + jnp.log(row_total)
    attn_out = weighted / row_total[:, None]
    row_delta = jnp.sum(flat_grad.astype(jnp.float32) * attn_out, axis=1)

    def grad_step(summed, current):
        pair_rows, key_pos, key_doc = current
        scores, visible = block_scores(
            flat_query, pair_rows[:, :head_dim], flat_pos, flat_doc, key_pos, key_doc, score_scale
        )
        attn_prob = jnp.where(visible, jnp.exp(scores - log_total[:, None]), 0.0)
        prob_grad = contract_cols(flat_grad, pair_rows[:, head_dim:])
        score_grad = (score_scale * attn_prob * (prob_grad - row_delta[:, None])).astype(
            jnp.bfloat16
        )
        summed = summed + jnp.dot(
            score_grad, pair_rows[:, :head_dim], preferred_element_type=jnp.float32
        )
        key_term = contract_rows(score_grad, flat_query)
        value_term = contract_rows(attn_prob.astype(jnp.bfloat16), flat_grad)
        return (summed, jnp.concatenate([key_term, value_term], axis=1))

    query_grad_rot, key_terms = lax.scan(
        grad_step, jnp.zeros((flat_rows, head_dim), jnp.float32), key_blocks
    )
    own_positions = first_row + jnp.arange(local_rows, dtype=jnp.int32)
    query_grad = (
        unrotate(query_grad_rot, flat_pos)
        .reshape(local_rows, group * head_dim)
        .astype(jnp.bfloat16)
    )
    next_query_grad = passed_along_2(query_grad, "pipe", -1)
    if side == len(RING_OFFSETS):
        keyval_grad = ring_scatter_sum(key_terms.reshape(seq_len, 2 * head_dim), device, side)
    else:
        keyval_grad = summed_rows(
            key_terms.reshape(seq_len, 2 * head_dim).astype(jnp.bfloat16), "ctx"
        )
    key_grad = unrotate(keyval_grad[:, :head_dim], own_positions).astype(jnp.bfloat16)
    value_grad = keyval_grad[:, head_dim:].astype(jnp.bfloat16)
    next_keyval_grad = passed_along_2(
        jnp.concatenate([key_grad, value_grad], axis=1), "pipe", -1
    )
    next_qkv_grad = jnp.concatenate([next_query_grad, next_keyval_grad], axis=1)
    passed = projected_sum(next_qkv_grad, next_weight, next_grad_in)
    return passed[None]


def solution(mesh):
    return jax.shard_map(
        body,
        mesh=mesh,
        in_specs=(
            P("pipe", "ctx", None),
            P("pipe", "ctx", None),
            P("pipe", "ctx", None),
            P("pipe", "ctx", None),
            P("pipe", "ctx", None),
            P("pipe", None),
            P("pipe", None),
        ),
        out_specs=P("pipe", "ctx", None),
        check_vma=False,
    )
```

```python
import math

import jax
import jax.numpy as jnp
from jax import lax
from jax.experimental import pallas as pl
from jax.sharding import PartitionSpec as P

BLOCK = 128


ROPE_BASE = 500000.0
MASKED = -1e30


def passed_along(value, axis, steps):
    count = lax.axis_size(axis)
    pairs = [(source, (source + steps) % count) for source in range(count)]
    return lax.ppermute(value, axis, pairs)


def passed_along_2(value, axis, by):
    size = lax.axis_size(axis)
    pairs = [(i, i + by) for i in range(size) if 0 <= i + by < size]
    return lax.ppermute(value, axis, pairs)


def gathered_rows(value, axis):
    count = lax.axis_size(axis)
    spread = jnp.broadcast_to(value[None], (count,) + value.shape)
    return lax.all_to_all(spread, axis, 0, 0, tiled=False).reshape((-1,) + value.shape[1:])


def summed_rows(value, axis):
    count = lax.axis_size(axis)
    pieces = lax.all_to_all(value.reshape((count, -1) + value.shape[1:]), axis, 0, 0, tiled=False)
    return jnp.sum(pieces.astype(jnp.float32), axis=0)


def projection_kernel(grad_ref, weight_ref, base_ref, out_ref):
    product = lax.dot_general(
        grad_ref[...], weight_ref[...], (((1,), (1,)), ((), ())), preferred_element_type=jnp.float32
    )
    out_ref[...] = (base_ref[...].astype(jnp.float32) + product).astype(out_ref.dtype)


def projected_sum(grad_rows, weight, base, tile=4096):
    rows, inner = grad_rows.shape
    width = weight.shape[0]
    return pl.pallas_call(
        projection_kernel,
        grid=(width // tile,),
        in_specs=[
            pl.BlockSpec((rows, inner), lambda j: (0, 0)),
            pl.BlockSpec((tile, inner), lambda j: (j, 0)),
            pl.BlockSpec((rows, tile), lambda j: (0, j)),
        ],
        out_specs=pl.BlockSpec((rows, tile), lambda j: (0, j)),
        out_shape=jax.ShapeDtypeStruct((rows, width), base.dtype),
        cost_estimate=pl.CostEstimate(
            flops=2 * rows * inner * width,
            bytes_accessed=2 * (rows * inner + width * inner + 2 * rows * width),
            transcendentals=0,
        ),
    )(grad_rows, weight, base)


RING_OFFSETS = (0, -1, 1, -2)
RING_INDEX_OF_DELTA = (0, 2, 3, 1)


def ring_shift(value, phase, step, side):
    pairs = []
    for source in range(side * side):
        row, col = divmod(source, side)
        if phase == 0:
            target = row * side + (col + step) % side
        else:
            target = ((row + step) % side) * side + col
        pairs.append((source, target))
    return lax.ppermute(value, "ctx", pairs)


def ring_four(value, phase, side):
    from_left = ring_shift(value, phase, 1, side)
    from_right = ring_shift(value, phase, -1, side)
    from_far = ring_shift(from_left, phase, 1, side)
    return jnp.stack([value, from_left, from_right, from_far])


def ring_gather(value, first_phase, side):
    inner = ring_four(value, first_phase, side)
    return ring_four(inner, 1 - first_phase, side).reshape((side * side,) + value.shape)


def ring_position(device, source, first_phase, side):
    index_of_delta = jnp.asarray(RING_INDEX_OF_DELTA, jnp.int32)
    row_delta = index_of_delta[(source // side - device // side) % side]
    col_delta = index_of_delta[(source % side - device % side) % side]
    if first_phase == 0:
        return row_delta * side + col_delta
    return col_delta * side + row_delta


def rope_tables(positions, head_dim):
    half_width = head_dim // 2
    inv_freq = ROPE_BASE ** (-(jnp.arange(half_width, dtype=jnp.float32) * 2.0 / head_dim))
    angles = positions.astype(jnp.float32)[:, None] * inv_freq[None, :]
    angles = jnp.concatenate([angles, angles], axis=1)
    return (jnp.cos(angles), jnp.sin(angles))


def unrotate(gradient, positions):
    cosine, sine_table = rope_tables(positions, gradient.shape[1])
    half_width = gradient.shape[1] // 2
    turned = jnp.concatenate([-gradient[:, half_width:], gradient[:, :half_width]], axis=1)
    return gradient * cosine - turned * sine_table


def doc_ids(positions, lengths):
    doc_ends = jnp.cumsum(lengths)[:-1]
    return jnp.sum((positions[:, None] >= doc_ends[None, :]).astype(jnp.int32), axis=1)


def seq_to_stored(rows, block_order, device, ctx_size, per_device):
    width = rows.shape[1]
    first_block = device * per_device
    blocks = rows.reshape(per_device, BLOCK, width)
    pieces = []
    for slot_k in range(per_device):
        offset = slot_k * ctx_size // per_device
        slot_at = (device - offset) % ctx_size * per_device + slot_k
        local_index = block_order[slot_at] - first_block
        chosen = lax.dynamic_index_in_dim(blocks, local_index, 0, keepdims=False)
        if slot_k > 0:
            chosen = passed_along(chosen, "ctx", -offset)
        pieces.append(chosen)
    return jnp.concatenate(pieces, axis=0)


def stored_to_seq(rows, block_order, device, ctx_size, per_device):
    width = rows.shape[1]
    first_block = device * per_device
    blocks = rows.reshape(per_device, BLOCK, width)
    pieces = []
    local_ids = []
    for slot_k in range(per_device):
        offset = slot_k * ctx_size // per_device
        piece = blocks[slot_k]
        if slot_k > 0:
            piece = passed_along(piece, "ctx", offset)
        pieces.append(piece)
        sender_slot = (device - offset) % ctx_size * per_device + slot_k
        local_ids.append(block_order[sender_slot] - first_block)
    stacked = jnp.stack(pieces)
    index_list = jnp.stack(local_ids)
    choose = (jnp.arange(per_device, dtype=jnp.int32)[:, None] == index_list[None, :]).astype(
        rows.dtype
    )
    placed = jnp.einsum("pk,kbw->pbw", choose, stacked, preferred_element_type=jnp.float32)
    return placed.astype(rows.dtype).reshape(-1, width)


def contract_rows(left_rows, right_rows):
    return lax.dot_general(
        left_rows, right_rows, (((0,), (0,)), ((), ())), preferred_element_type=jnp.float32
    )


def contract_cols(left_rows, right_rows):
    return lax.dot_general(
        left_rows, right_rows, (((1,), (1,)), ((), ())), preferred_element_type=jnp.float32
    )


def block_scores(query_rows, key_rows, query_pos, query_doc, key_pos, key_doc, score_scale):
    scores = contract_cols(query_rows, key_rows) * score_scale
    visible = (query_doc[:, None] == key_doc[None, :]) & (key_pos[None, :] <= query_pos[:, None])
    return (scores, visible)


def body(grad_in, query, keyval, w_qkv, w_out, doc_lengths, order):
    section_grad_in = grad_in[0]
    stored_query = query[0]
    stored_keyval = keyval[0]
    in_weight = w_qkv[0]
    out_weight = w_out[0]
    lengths = doc_lengths[0]
    block_order = order[0]
    ctx_size = lax.axis_size("ctx")
    device = lax.axis_index("ctx")
    local_rows = section_grad_in.shape[0]
    head_dim = stored_keyval.shape[1] // 2
    group = stored_query.shape[1] // head_dim
    per_device = local_rows // BLOCK
    block_count = block_order.shape[0]
    seq_len = local_rows * ctx_size
    first_row = device * local_rows
    score_scale = 1.0 / math.sqrt(head_dim)
    key_block = math.gcd(seq_len, 512)
    key_steps = seq_len // key_block
    within = jnp.arange(BLOCK, dtype=jnp.int32)
    next_weight = lax.all_gather(passed_along_2(in_weight, "pipe", -1), "ctx", axis=0, tiled=True)
    out_grad = jnp.dot(
        section_grad_in,
        lax.all_gather(out_weight, "ctx", axis=0, tiled=True),
        preferred_element_type=jnp.float32,
    ).astype(jnp.bfloat16)
    local_out_grad = out_grad
    seq_query = stored_to_seq(stored_query, block_order, device, ctx_size, per_device)
    side = math.isqrt(ctx_size)
    slot_ids = jnp.arange(block_count, dtype=jnp.int32)
    if side == len(RING_OFFSETS) and per_device == 2:
        gathered = jnp.concatenate(
            [
                ring_gather(stored_keyval[:BLOCK], 0, side),
                ring_gather(stored_keyval[BLOCK:], 1, side),
            ]
        ).reshape(seq_len, 2 * head_dim)
        holder = slot_ids // per_device
        slot_place = jnp.where(
            slot_ids % per_device == 0,
            ring_position(device, holder, 0, side),
            ctx_size + ring_position(device, holder, 1, side),
        )
    else:
        gathered = gathered_rows(stored_keyval, "ctx")
        slot_place = slot_ids
    gathered, grad_source = lax.optimization_barrier((gathered, section_grad_in))
    next_grad_in = passed_along_2(grad_source, "pipe", -1)
    inverse = jnp.sum(
        jnp.where(block_order[None, :] == slot_ids[:, None], slot_place[None, :], 0), axis=1
    )
    all_keyval = gathered.reshape(block_count, BLOCK, 2 * head_dim)[inverse].reshape(
        seq_len, 2 * head_dim
    )
    key_positions = jnp.arange(seq_len, dtype=jnp.int32)
    key_docs = doc_ids(key_positions, lengths)
    query_pos = first_row + jnp.arange(local_rows, dtype=jnp.int32)
    query_doc = doc_ids(query_pos, lengths)
    flat_rows = local_rows * group
    flat_query = seq_query.reshape(flat_rows, head_dim)
    flat_grad = local_out_grad.reshape(flat_rows, head_dim)
    flat_pos = jnp.repeat(query_pos, group)
    flat_doc = jnp.repeat(query_doc, group)
    key_blocks = (
        all_keyval.reshape(key_steps, key_block, 2 * head_dim),
        key_positions.reshape(key_steps, key_block),
        key_docs.reshape(key_steps, key_block),
    )

    def running_total(carried, current):
        row_top, row_total, weighted = carried
        pair_rows, key_pos, key_doc = current
        scores, visible = block_scores(
            flat_query, pair_rows[:, :head_dim], flat_pos, flat_doc, key_pos, key_doc, score_scale
        )
        new_top = jnp.maximum(row_top, jnp.max(jnp.where(visible, scores, MASKED), axis=1))
        rescale = jnp.exp(row_top - new_top)
        weights = jnp.where(visible, jnp.exp(scores - new_top[:, None]), 0.0)
        row_total = row_total * rescale + jnp.sum(weights, axis=1)
        value_wide = pair_rows[:, head_dim:].astype(jnp.float32)
        weighted = weighted * rescale[:, None] + jnp.dot(
            weights, value_wide, precision=lax.Precision.HIGH
        )
        return ((new_top, row_total, weighted), None)

    start_top = jnp.full((flat_rows,), MASKED, jnp.float32)
    start_carry = (
        start_top,
        jnp.zeros((flat_rows,), jnp.float32),
        jnp.zeros((flat_rows, head_dim), jnp.float32),
    )
    (row_top, row_total, weighted), unused = lax.scan(running_total, start_carry, key_blocks)
    log_total = row_top + jnp.log(row_total)
    attn_out = weighted / row_total[:, None]
    row_delta = jnp.sum(flat_grad.astype(jnp.float32) * attn_out, axis=1)

    def grad_step(summed, current):
        pair_rows, key_pos, key_doc = current
        scores, visible = block_scores(
            flat_query, pair_rows[:, :head_dim], flat_pos, flat_doc, key_pos, key_doc, score_scale
        )
        attn_prob = jnp.where(visible, jnp.exp(scores - log_total[:, None]), 0.0)
        prob_grad = contract_cols(flat_grad, pair_rows[:, head_dim:])
        score_grad = (score_scale * attn_prob * (prob_grad - row_delta[:, None])).astype(
            jnp.bfloat16
        )
        summed = summed + jnp.dot(
            score_grad, pair_rows[:, :head_dim], preferred_element_type=jnp.float32
        )
        key_term = contract_rows(score_grad, flat_query)
        value_term = contract_rows(attn_prob.astype(jnp.bfloat16), flat_grad)
        return (summed, jnp.concatenate([key_term, value_term], axis=1))

    query_grad_rot = jnp.zeros((flat_rows, head_dim), jnp.float32)
    term_list = []
    for step in range(key_steps):
        query_grad_rot, term = grad_step(query_grad_rot, tuple(part[step] for part in key_blocks))
        term_list.append(term)
    key_terms = jnp.stack(term_list)
    own_positions = first_row + jnp.arange(local_rows, dtype=jnp.int32)
    query_grad = (
        unrotate(query_grad_rot, flat_pos)
        .reshape(local_rows, group * head_dim)
        .astype(jnp.bfloat16)
    )
    next_query_grad = passed_along_2(query_grad, "pipe", -1)
    keyval_grad = summed_rows(
        key_terms.reshape(seq_len, 2 * head_dim).astype(jnp.bfloat16), "ctx"
    )
    key_grad = unrotate(keyval_grad[:, :head_dim], own_positions).astype(jnp.bfloat16)
    value_grad = keyval_grad[:, head_dim:].astype(jnp.bfloat16)
    next_keyval_grad = passed_along_2(
        jnp.concatenate([key_grad, value_grad], axis=1), "pipe", -1
    )
    next_qkv_grad = jnp.concatenate([next_query_grad, next_keyval_grad], axis=1)
    passed = projected_sum(next_qkv_grad, next_weight, next_grad_in)
    return passed[None]


def solution(mesh):
    return jax.shard_map(
        body,
        mesh=mesh,
        in_specs=(
            P("pipe", "ctx", None),
            P("pipe", "ctx", None),
            P("pipe", "ctx", None),
            P("pipe", "ctx", None),
            P("pipe", "ctx", None),
            P("pipe", None),
            P("pipe", None),
        ),
        out_specs=P("pipe", "ctx", None),
        check_vma=False,
    )
```

```python
import math

import jax
import jax.numpy as jnp
from jax import lax
from jax.experimental import pallas as pl
from jax.sharding import PartitionSpec as P

BLOCK = 128


ROPE_BASE = 500000.0
MASKED = -1e30


def passed_along(value, axis, steps):
    count = lax.axis_size(axis)
    pairs = [(source, (source + steps) % count) for source in range(count)]
    return lax.ppermute(value, axis, pairs)


def passed_along_2(value, axis, by):
    size = lax.axis_size(axis)
    pairs = [(i, i + by) for i in range(size) if 0 <= i + by < size]
    return lax.ppermute(value, axis, pairs)


def gathered_rows(value, axis):
    count = lax.axis_size(axis)
    spread = jnp.broadcast_to(value[None], (count,) + value.shape)
    return lax.all_to_all(spread, axis, 0, 0, tiled=False).reshape((-1,) + value.shape[1:])


def summed_rows(value, axis):
    count = lax.axis_size(axis)
    pieces = lax.all_to_all(value.reshape((count, -1) + value.shape[1:]), axis, 0, 0, tiled=False)
    return jnp.sum(pieces.astype(jnp.float32), axis=0)


def projection_kernel(grad_ref, weight_ref, base_ref, out_ref):
    product = lax.dot_general(
        grad_ref[...], weight_ref[...], (((1,), (1,)), ((), ())), preferred_element_type=jnp.float32
    )
    out_ref[...] = (base_ref[...].astype(jnp.float32) + product).astype(out_ref.dtype)


def projected_sum(grad_rows, weight, base, first_column, out_dtype, tile=4096):
    rows, inner = grad_rows.shape
    width = weight.shape[0]
    column_block = first_column // inner
    return pl.pallas_call(
        projection_kernel,
        grid=(width // tile,),
        in_specs=[
            pl.BlockSpec((rows, inner), lambda j: (0, 0)),
            pl.BlockSpec((tile, inner), lambda j: (j, column_block)),
            pl.BlockSpec((rows, tile), lambda j: (0, j)),
        ],
        out_specs=pl.BlockSpec((rows, tile), lambda j: (0, j)),
        out_shape=jax.ShapeDtypeStruct((rows, width), out_dtype),
        cost_estimate=pl.CostEstimate(
            flops=2 * rows * inner * width,
            bytes_accessed=2 * (rows * inner + width * inner) + 6 * rows * width,
            transcendentals=0,
        ),
    )(grad_rows, weight, base)


RING_OFFSETS = (0, -1, 1, -2)
RING_INDEX_OF_DELTA = (0, 2, 3, 1)


def ring_shift(value, phase, step, side):
    pairs = []
    for source in range(side * side):
        row, col = divmod(source, side)
        if phase == 0:
            target = row * side + (col + step) % side
        else:
            target = ((row + step) % side) * side + col
        pairs.append((source, target))
    return lax.ppermute(value, "ctx", pairs)


def ring_four(value, phase, side):
    from_left = ring_shift(value, phase, 1, side)
    from_right = ring_shift(value, phase, -1, side)
    from_far = ring_shift(from_left, phase, 1, side)
    return jnp.stack([value, from_left, from_right, from_far])


def ring_gather(value, first_phase, side):
    inner = ring_four(value, first_phase, side)
    return ring_four(inner, 1 - first_phase, side).reshape((side * side,) + value.shape)


def ring_position(device, source, first_phase, side):
    index_of_delta = jnp.asarray(RING_INDEX_OF_DELTA, jnp.int32)
    row_delta = index_of_delta[(source // side - device // side) % side]
    col_delta = index_of_delta[(source % side - device % side) % side]
    if first_phase == 0:
        return row_delta * side + col_delta
    return col_delta * side + row_delta


def rope_tables(positions, head_dim):
    half_width = head_dim // 2
    inv_freq = ROPE_BASE ** (-(jnp.arange(half_width, dtype=jnp.float32) * 2.0 / head_dim))
    angles = positions.astype(jnp.float32)[:, None] * inv_freq[None, :]
    angles = jnp.concatenate([angles, angles], axis=1)
    return (jnp.cos(angles), jnp.sin(angles))


def unrotate(gradient, positions):
    cosine, sine_table = rope_tables(positions, gradient.shape[1])
    half_width = gradient.shape[1] // 2
    turned = jnp.concatenate([-gradient[:, half_width:], gradient[:, :half_width]], axis=1)
    return gradient * cosine - turned * sine_table


def doc_ids(positions, lengths):
    doc_ends = jnp.cumsum(lengths)[:-1]
    return jnp.sum((positions[:, None] >= doc_ends[None, :]).astype(jnp.int32), axis=1)


def seq_to_stored(rows, block_order, device, ctx_size, per_device):
    width = rows.shape[1]
    first_block = device * per_device
    blocks = rows.reshape(per_device, BLOCK, width)
    pieces = []
    for slot_k in range(per_device):
        offset = slot_k * ctx_size // per_device
        slot_at = (device - offset) % ctx_size * per_device + slot_k
        local_index = block_order[slot_at] - first_block
        chosen = lax.dynamic_index_in_dim(blocks, local_index, 0, keepdims=False)
        if slot_k > 0:
            chosen = passed_along(chosen, "ctx", -offset)
        pieces.append(chosen)
    return jnp.concatenate(pieces, axis=0)


def stored_to_seq(rows, block_order, device, ctx_size, per_device):
    width = rows.shape[1]
    first_block = device * per_device
    blocks = rows.reshape(per_device, BLOCK, width)
    pieces = []
    local_ids = []
    for slot_k in range(per_device):
        offset = slot_k * ctx_size // per_device
        piece = blocks[slot_k]
        if slot_k > 0:
            piece = passed_along(piece, "ctx", offset)
        pieces.append(piece)
        sender_slot = (device - offset) % ctx_size * per_device + slot_k
        local_ids.append(block_order[sender_slot] - first_block)
    stacked = jnp.stack(pieces)
    index_list = jnp.stack(local_ids)
    choose = (jnp.arange(per_device, dtype=jnp.int32)[:, None] == index_list[None, :]).astype(
        rows.dtype
    )
    placed = jnp.einsum("pk,kbw->pbw", choose, stacked, preferred_element_type=jnp.float32)
    return placed.astype(rows.dtype).reshape(-1, width)


def contract_rows(left_rows, right_rows):
    return lax.dot_general(
        left_rows, right_rows, (((0,), (0,)), ((), ())), preferred_element_type=jnp.float32
    )


def contract_cols(left_rows, right_rows):
    return lax.dot_general(
        left_rows, right_rows, (((1,), (1,)), ((), ())), preferred_element_type=jnp.float32
    )


def block_scores(query_rows, key_rows, query_pos, query_doc, key_pos, key_doc, score_scale):
    scores = contract_cols(query_rows, key_rows) * score_scale
    visible = (query_doc[:, None] == key_doc[None, :]) & (key_pos[None, :] <= query_pos[:, None])
    return (scores, visible)


def body(grad_in, query, keyval, w_qkv, w_out, doc_lengths, order):
    section_grad_in = grad_in[0]
    stored_query = query[0]
    stored_keyval = keyval[0]
    in_weight = w_qkv[0]
    out_weight = w_out[0]
    lengths = doc_lengths[0]
    block_order = order[0]
    ctx_size = lax.axis_size("ctx")
    device = lax.axis_index("ctx")
    local_rows = section_grad_in.shape[0]
    head_dim = stored_keyval.shape[1] // 2
    group = stored_query.shape[1] // head_dim
    per_device = local_rows // BLOCK
    block_count = block_order.shape[0]
    seq_len = local_rows * ctx_size
    first_row = device * local_rows
    score_scale = 1.0 / math.sqrt(head_dim)
    key_block = math.gcd(seq_len, 512)
    key_steps = seq_len // key_block
    within = jnp.arange(BLOCK, dtype=jnp.int32)
    next_weight = lax.all_gather(passed_along_2(in_weight, "pipe", -1), "ctx", axis=0, tiled=True)
    out_grad = jnp.dot(
        section_grad_in,
        lax.all_gather(out_weight, "ctx", axis=0, tiled=True),
        preferred_element_type=jnp.float32,
    ).astype(jnp.bfloat16)
    local_out_grad = out_grad
    seq_query = stored_to_seq(stored_query, block_order, device, ctx_size, per_device)
    side = math.isqrt(ctx_size)
    slot_ids = jnp.arange(block_count, dtype=jnp.int32)
    if side == len(RING_OFFSETS) and per_device == 2:
        gathered = jnp.concatenate(
            [
                ring_gather(stored_keyval[:BLOCK], 0, side),
                ring_gather(stored_keyval[BLOCK:], 1, side),
            ]
        ).reshape(seq_len, 2 * head_dim)
        holder = slot_ids // per_device
        slot_place = jnp.where(
            slot_ids % per_device == 0,
            ring_position(device, holder, 0, side),
            ctx_size + ring_position(device, holder, 1, side),
        )
    else:
        gathered = gathered_rows(stored_keyval, "ctx")
        slot_place = slot_ids
    gathered, grad_source = lax.optimization_barrier((gathered, section_grad_in))
    next_grad_in = passed_along_2(grad_source, "pipe", -1)
    inverse = jnp.sum(
        jnp.where(block_order[None, :] == slot_ids[:, None], slot_place[None, :], 0), axis=1
    )
    all_keyval = gathered.reshape(block_count, BLOCK, 2 * head_dim)[inverse].reshape(
        seq_len, 2 * head_dim
    )
    key_positions = jnp.arange(seq_len, dtype=jnp.int32)
    key_docs = doc_ids(key_positions, lengths)
    query_pos = first_row + jnp.arange(local_rows, dtype=jnp.int32)
    query_doc = doc_ids(query_pos, lengths)
    flat_rows = local_rows * group
    flat_query = seq_query.reshape(flat_rows, head_dim)
    flat_grad = local_out_grad.reshape(flat_rows, head_dim)
    flat_pos = jnp.repeat(query_pos, group)
    flat_doc = jnp.repeat(query_doc, group)
    key_blocks = (
        all_keyval.reshape(key_steps, key_block, 2 * head_dim),
        key_positions.reshape(key_steps, key_block),
        key_docs.reshape(key_steps, key_block),
    )

    def running_total(carried, current):
        row_top, row_total, weighted = carried
        pair_rows, key_pos, key_doc = current
        scores, visible = block_scores(
            flat_query, pair_rows[:, :head_dim], flat_pos, flat_doc, key_pos, key_doc, score_scale
        )
        new_top = jnp.maximum(row_top, jnp.max(jnp.where(visible, scores, MASKED), axis=1))
        rescale = jnp.exp(row_top - new_top)
        weights = jnp.where(visible, jnp.exp(scores - new_top[:, None]), 0.0)
        row_total = row_total * rescale + jnp.sum(weights, axis=1)
        value_wide = pair_rows[:, head_dim:].astype(jnp.float32)
        weighted = weighted * rescale[:, None] + jnp.dot(
            weights, value_wide, precision=lax.Precision.HIGH
        )
        return ((new_top, row_total, weighted), None)

    start_top = jnp.full((flat_rows,), MASKED, jnp.float32)
    start_carry = (
        start_top,
        jnp.zeros((flat_rows,), jnp.float32),
        jnp.zeros((flat_rows, head_dim), jnp.float32),
    )
    (row_top, row_total, weighted), unused = lax.scan(running_total, start_carry, key_blocks)
    log_total = row_top + jnp.log(row_total)
    attn_out = weighted / row_total[:, None]
    row_delta = jnp.sum(flat_grad.astype(jnp.float32) * attn_out, axis=1)

    def grad_step(summed, current):
        pair_rows, key_pos, key_doc = current
        scores, visible = block_scores(
            flat_query, pair_rows[:, :head_dim], flat_pos, flat_doc, key_pos, key_doc, score_scale
        )
        attn_prob = jnp.where(visible, jnp.exp(scores - log_total[:, None]), 0.0)
        prob_grad = contract_cols(flat_grad, pair_rows[:, head_dim:])
        score_grad = (score_scale * attn_prob * (prob_grad - row_delta[:, None])).astype(
            jnp.bfloat16
        )
        summed = summed + jnp.dot(
            score_grad, pair_rows[:, :head_dim], preferred_element_type=jnp.float32
        )
        key_term = contract_rows(score_grad, flat_query)
        value_term = contract_rows(attn_prob.astype(jnp.bfloat16), flat_grad)
        return (summed, jnp.concatenate([key_term, value_term], axis=1))

    query_grad_rot, key_terms = lax.scan(
        grad_step, jnp.zeros((flat_rows, head_dim), jnp.float32), key_blocks
    )
    own_positions = first_row + jnp.arange(local_rows, dtype=jnp.int32)
    query_grad = (
        unrotate(query_grad_rot, flat_pos)
        .reshape(local_rows, group * head_dim)
        .astype(jnp.bfloat16)
    )
    next_query_grad = passed_along_2(query_grad, "pipe", -1)
    keyval_grad = summed_rows(
        key_terms.reshape(seq_len, 2 * head_dim).astype(jnp.bfloat16), "ctx"
    )
    key_grad = unrotate(keyval_grad[:, :head_dim], own_positions).astype(jnp.bfloat16)
    value_grad = keyval_grad[:, head_dim:].astype(jnp.bfloat16)
    next_keyval_grad = passed_along_2(
        jnp.concatenate([key_grad, value_grad], axis=1), "pipe", -1
    )
    query_width = next_query_grad.shape[1]
    partial = projected_sum(next_query_grad, next_weight, next_grad_in, 0, jnp.float32)
    passed = projected_sum(next_keyval_grad, next_weight, partial, query_width, jnp.bfloat16)
    return passed[None]


def solution(mesh):
    return jax.shard_map(
        body,
        mesh=mesh,
        in_specs=(
            P("pipe", "ctx", None),
            P("pipe", "ctx", None),
            P("pipe", "ctx", None),
            P("pipe", "ctx", None),
            P("pipe", "ctx", None),
            P("pipe", None),
            P("pipe", None),
        ),
        out_specs=P("pipe", "ctx", None),
        check_vma=False,
    )
```

```python
import math

import jax
import jax.numpy as jnp
from jax import lax
from jax.experimental import pallas as pl
from jax.sharding import PartitionSpec as P

BLOCK = 128


ROPE_BASE = 500000.0
MASKED = -1e30


def passed_along(value, axis, steps):
    count = lax.axis_size(axis)
    pairs = [(source, (source + steps) % count) for source in range(count)]
    return lax.ppermute(value, axis, pairs)


def passed_along_2(value, axis, by):
    size = lax.axis_size(axis)
    pairs = [(i, i + by) for i in range(size) if 0 <= i + by < size]
    return lax.ppermute(value, axis, pairs)


def gathered_rows(value, axis):
    count = lax.axis_size(axis)
    spread = jnp.broadcast_to(value[None], (count,) + value.shape)
    return lax.all_to_all(spread, axis, 0, 0, tiled=False).reshape((-1,) + value.shape[1:])


def summed_rows(value, axis):
    count = lax.axis_size(axis)
    pieces = lax.all_to_all(value.reshape((count, -1) + value.shape[1:]), axis, 0, 0, tiled=False)
    return jnp.sum(pieces.astype(jnp.float32), axis=0)


def projection_kernel(grad_ref, weight_ref, base_ref, out_ref):
    product = lax.dot_general(
        grad_ref[...], weight_ref[...], (((1,), (1,)), ((), ())), preferred_element_type=jnp.float32
    )
    out_ref[...] = (base_ref[...].astype(jnp.float32) + product).astype(out_ref.dtype)


def projected_sum(grad_rows, weight, base, tile=4096):
    rows, inner = grad_rows.shape
    width = weight.shape[0]
    return pl.pallas_call(
        projection_kernel,
        grid=(width // tile,),
        in_specs=[
            pl.BlockSpec((rows, inner), lambda j: (0, 0)),
            pl.BlockSpec((tile, inner), lambda j: (j, 0)),
            pl.BlockSpec((rows, tile), lambda j: (0, j)),
        ],
        out_specs=pl.BlockSpec((rows, tile), lambda j: (0, j)),
        out_shape=jax.ShapeDtypeStruct((rows, width), base.dtype),
        cost_estimate=pl.CostEstimate(
            flops=2 * rows * inner * width,
            bytes_accessed=2 * (rows * inner + width * inner + 2 * rows * width),
            transcendentals=0,
        ),
    )(grad_rows, weight, base)


RING_OFFSETS = (0, -1, 1, -2)
RING_INDEX_OF_DELTA = (0, 2, 3, 1)


def ring_shift(value, phase, step, side):
    pairs = []
    for source in range(side * side):
        row, col = divmod(source, side)
        if phase == 0:
            target = row * side + (col + step) % side
        else:
            target = ((row + step) % side) * side + col
        pairs.append((source, target))
    return lax.ppermute(value, "ctx", pairs)


def ring_four(value, phase, side):
    from_left = ring_shift(value, phase, 1, side)
    from_right = ring_shift(value, phase, -1, side)
    from_far = ring_shift(from_left, phase, 1, side)
    return jnp.stack([value, from_left, from_right, from_far])


def ring_gather(value, first_phase, side):
    inner = ring_four(value, first_phase, side)
    return ring_four(inner, 1 - first_phase, side).reshape((side * side,) + value.shape)


def grid_scatter_sum(rows, side):
    region = rows.shape[0] // (side * side)
    tiles = rows.reshape(side, side, region, rows.shape[1])
    along_x = [[row * side + col for col in range(side)] for row in range(side)]
    along_y = [[row * side + col for row in range(side)] for col in range(side)]
    first = lax.all_to_all(
        jnp.moveaxis(tiles, 1, 0).astype(jnp.bfloat16), "ctx", 0, 0, axis_index_groups=along_x
    )
    first = jnp.sum(first.astype(jnp.float32), axis=0)
    second = lax.all_to_all(first.astype(jnp.bfloat16), "ctx", 0, 0, axis_index_groups=along_y)
    return jnp.sum(second.astype(jnp.float32), axis=0)


def ring_position(device, source, first_phase, side):
    index_of_delta = jnp.asarray(RING_INDEX_OF_DELTA, jnp.int32)
    row_delta = index_of_delta[(source // side - device // side) % side]
    col_delta = index_of_delta[(source % side - device % side) % side]
    if first_phase == 0:
        return row_delta * side + col_delta
    return col_delta * side + row_delta


def rope_tables(positions, head_dim):
    half_width = head_dim // 2
    inv_freq = ROPE_BASE ** (-(jnp.arange(half_width, dtype=jnp.float32) * 2.0 / head_dim))
    angles = positions.astype(jnp.float32)[:, None] * inv_freq[None, :]
    angles = jnp.concatenate([angles, angles], axis=1)
    return (jnp.cos(angles), jnp.sin(angles))


def unrotate(gradient, positions):
    cosine, sine_table = rope_tables(positions, gradient.shape[1])
    half_width = gradient.shape[1] // 2
    turned = jnp.concatenate([-gradient[:, half_width:], gradient[:, :half_width]], axis=1)
    return gradient * cosine - turned * sine_table


def doc_ids(positions, lengths):
    doc_ends = jnp.cumsum(lengths)[:-1]
    return jnp.sum((positions[:, None] >= doc_ends[None, :]).astype(jnp.int32), axis=1)


def seq_to_stored(rows, block_order, device, ctx_size, per_device):
    width = rows.shape[1]
    first_block = device * per_device
    blocks = rows.reshape(per_device, BLOCK, width)
    pieces = []
    for slot_k in range(per_device):
        offset = slot_k * ctx_size // per_device
        slot_at = (device - offset) % ctx_size * per_device + slot_k
        local_index = block_order[slot_at] - first_block
        chosen = lax.dynamic_index_in_dim(blocks, local_index, 0, keepdims=False)
        if slot_k > 0:
            chosen = passed_along(chosen, "ctx", -offset)
        pieces.append(chosen)
    return jnp.concatenate(pieces, axis=0)


def stored_to_seq(rows, block_order, device, ctx_size, per_device):
    width = rows.shape[1]
    first_block = device * per_device
    blocks = rows.reshape(per_device, BLOCK, width)
    pieces = []
    local_ids = []
    for slot_k in range(per_device):
        offset = slot_k * ctx_size // per_device
        piece = blocks[slot_k]
        if slot_k > 0:
            piece = passed_along(piece, "ctx", offset)
        pieces.append(piece)
        sender_slot = (device - offset) % ctx_size * per_device + slot_k
        local_ids.append(block_order[sender_slot] - first_block)
    stacked = jnp.stack(pieces)
    index_list = jnp.stack(local_ids)
    choose = (jnp.arange(per_device, dtype=jnp.int32)[:, None] == index_list[None, :]).astype(
        rows.dtype
    )
    placed = jnp.einsum("pk,kbw->pbw", choose, stacked, preferred_element_type=jnp.float32)
    return placed.astype(rows.dtype).reshape(-1, width)


def contract_rows(left_rows, right_rows):
    return lax.dot_general(
        left_rows, right_rows, (((0,), (0,)), ((), ())), preferred_element_type=jnp.float32
    )


def contract_cols(left_rows, right_rows):
    return lax.dot_general(
        left_rows, right_rows, (((1,), (1,)), ((), ())), preferred_element_type=jnp.float32
    )


def block_scores(query_rows, key_rows, query_pos, query_doc, key_pos, key_doc, score_scale):
    scores = contract_cols(query_rows, key_rows) * score_scale
    visible = (query_doc[:, None] == key_doc[None, :]) & (key_pos[None, :] <= query_pos[:, None])
    return (scores, visible)


def body(grad_in, query, keyval, w_qkv, w_out, doc_lengths, order):
    section_grad_in = grad_in[0]
    stored_query = query[0]
    stored_keyval = keyval[0]
    in_weight = w_qkv[0]
    out_weight = w_out[0]
    lengths = doc_lengths[0]
    block_order = order[0]
    ctx_size = lax.axis_size("ctx")
    device = lax.axis_index("ctx")
    local_rows = section_grad_in.shape[0]
    head_dim = stored_keyval.shape[1] // 2
    group = stored_query.shape[1] // head_dim
    per_device = local_rows // BLOCK
    block_count = block_order.shape[0]
    seq_len = local_rows * ctx_size
    first_row = device * local_rows
    score_scale = 1.0 / math.sqrt(head_dim)
    key_block = math.gcd(seq_len, 512)
    key_steps = seq_len // key_block
    within = jnp.arange(BLOCK, dtype=jnp.int32)
    next_weight = lax.all_gather(passed_along_2(in_weight, "pipe", -1), "ctx", axis=0, tiled=True)
    out_grad = jnp.dot(
        section_grad_in,
        lax.all_gather(out_weight, "ctx", axis=0, tiled=True),
        preferred_element_type=jnp.float32,
    ).astype(jnp.bfloat16)
    local_out_grad = out_grad
    seq_query = stored_to_seq(stored_query, block_order, device, ctx_size, per_device)
    side = math.isqrt(ctx_size)
    slot_ids = jnp.arange(block_count, dtype=jnp.int32)
    if side == len(RING_OFFSETS) and per_device == 2:
        gathered = jnp.concatenate(
            [
                ring_gather(stored_keyval[:BLOCK], 0, side),
                ring_gather(stored_keyval[BLOCK:], 1, side),
            ]
        ).reshape(seq_len, 2 * head_dim)
        holder = slot_ids // per_device
        slot_place = jnp.where(
            slot_ids % per_device == 0,
            ring_position(device, holder, 0, side),
            ctx_size + ring_position(device, holder, 1, side),
        )
    else:
        gathered = gathered_rows(stored_keyval, "ctx")
        slot_place = slot_ids
    gathered, grad_source = lax.optimization_barrier((gathered, section_grad_in))
    next_grad_in = passed_along_2(grad_source, "pipe", -1)
    inverse = jnp.sum(
        jnp.where(block_order[None, :] == slot_ids[:, None], slot_place[None, :], 0), axis=1
    )
    all_keyval = gathered.reshape(block_count, BLOCK, 2 * head_dim)[inverse].reshape(
        seq_len, 2 * head_dim
    )
    key_positions = jnp.arange(seq_len, dtype=jnp.int32)
    key_docs = doc_ids(key_positions, lengths)
    query_pos = first_row + jnp.arange(local_rows, dtype=jnp.int32)
    query_doc = doc_ids(query_pos, lengths)
    flat_rows = local_rows * group
    flat_query = seq_query.reshape(flat_rows, head_dim)
    flat_grad = local_out_grad.reshape(flat_rows, head_dim)
    flat_pos = jnp.repeat(query_pos, group)
    flat_doc = jnp.repeat(query_doc, group)
    key_blocks = (
        all_keyval.reshape(key_steps, key_block, 2 * head_dim),
        key_positions.reshape(key_steps, key_block),
        key_docs.reshape(key_steps, key_block),
    )

    def running_total(carried, current):
        row_top, row_total, weighted = carried
        pair_rows, key_pos, key_doc = current
        scores, visible = block_scores(
            flat_query, pair_rows[:, :head_dim], flat_pos, flat_doc, key_pos, key_doc, score_scale
        )
        new_top = jnp.maximum(row_top, jnp.max(jnp.where(visible, scores, MASKED), axis=1))
        rescale = jnp.exp(row_top - new_top)
        weights = jnp.where(visible, jnp.exp(scores - new_top[:, None]), 0.0)
        row_total = row_total * rescale + jnp.sum(weights, axis=1)
        value_wide = pair_rows[:, head_dim:].astype(jnp.float32)
        weighted = weighted * rescale[:, None] + jnp.dot(
            weights, value_wide, precision=lax.Precision.HIGH
        )
        return ((new_top, row_total, weighted), None)

    start_top = jnp.full((flat_rows,), MASKED, jnp.float32)
    start_carry = (
        start_top,
        jnp.zeros((flat_rows,), jnp.float32),
        jnp.zeros((flat_rows, head_dim), jnp.float32),
    )
    (row_top, row_total, weighted), unused = lax.scan(running_total, start_carry, key_blocks)
    log_total = row_top + jnp.log(row_total)
    attn_out = weighted / row_total[:, None]
    row_delta = jnp.sum(flat_grad.astype(jnp.float32) * attn_out, axis=1)

    def grad_step(summed, current):
        pair_rows, key_pos, key_doc = current
        scores, visible = block_scores(
            flat_query, pair_rows[:, :head_dim], flat_pos, flat_doc, key_pos, key_doc, score_scale
        )
        attn_prob = jnp.where(visible, jnp.exp(scores - log_total[:, None]), 0.0)
        prob_grad = contract_cols(flat_grad, pair_rows[:, head_dim:])
        score_grad = (score_scale * attn_prob * (prob_grad - row_delta[:, None])).astype(
            jnp.bfloat16
        )
        summed = summed + jnp.dot(
            score_grad, pair_rows[:, :head_dim], preferred_element_type=jnp.float32
        )
        key_term = contract_rows(score_grad, flat_query)
        value_term = contract_rows(attn_prob.astype(jnp.bfloat16), flat_grad)
        return (summed, jnp.concatenate([key_term, value_term], axis=1))

    query_grad_rot, key_terms = lax.scan(
        grad_step, jnp.zeros((flat_rows, head_dim), jnp.float32), key_blocks
    )
    own_positions = first_row + jnp.arange(local_rows, dtype=jnp.int32)
    query_grad = (
        unrotate(query_grad_rot, flat_pos)
        .reshape(local_rows, group * head_dim)
        .astype(jnp.bfloat16)
    )
    next_query_grad = passed_along_2(query_grad, "pipe", -1)
    if side == len(RING_OFFSETS):
        keyval_grad = grid_scatter_sum(key_terms.reshape(seq_len, 2 * head_dim), side)
    else:
        keyval_grad = summed_rows(
            key_terms.reshape(seq_len, 2 * head_dim).astype(jnp.bfloat16), "ctx"
        )
    key_grad = unrotate(keyval_grad[:, :head_dim], own_positions).astype(jnp.bfloat16)
    value_grad = keyval_grad[:, head_dim:].astype(jnp.bfloat16)
    next_keyval_grad = passed_along_2(
        jnp.concatenate([key_grad, value_grad], axis=1), "pipe", -1
    )
    next_qkv_grad = jnp.concatenate([next_query_grad, next_keyval_grad], axis=1)
    passed = projected_sum(next_qkv_grad, next_weight, next_grad_in)
    return passed[None]


def solution(mesh):
    return jax.shard_map(
        body,
        mesh=mesh,
        in_specs=(
            P("pipe", "ctx", None),
            P("pipe", "ctx", None),
            P("pipe", "ctx", None),
            P("pipe", "ctx", None),
            P("pipe", "ctx", None),
            P("pipe", None),
            P("pipe", None),
        ),
        out_specs=P("pipe", "ctx", None),
        check_vma=False,
    )
```

```python
import math

import jax
import jax.numpy as jnp
from jax import lax
from jax.experimental import pallas as pl
from jax.sharding import PartitionSpec as P

BLOCK = 128


ROPE_BASE = 500000.0
MASKED = -1e30


def passed_along(value, axis, steps):
    count = lax.axis_size(axis)
    pairs = [(source, (source + steps) % count) for source in range(count)]
    return lax.ppermute(value, axis, pairs)


def passed_along_2(value, axis, by):
    size = lax.axis_size(axis)
    pairs = [(i, i + by) for i in range(size) if 0 <= i + by < size]
    return lax.ppermute(value, axis, pairs)


def gathered_rows(value, axis):
    count = lax.axis_size(axis)
    spread = jnp.broadcast_to(value[None], (count,) + value.shape)
    return lax.all_to_all(spread, axis, 0, 0, tiled=False).reshape((-1,) + value.shape[1:])


def summed_rows(value, axis):
    count = lax.axis_size(axis)
    pieces = lax.all_to_all(value.reshape((count, -1) + value.shape[1:]), axis, 0, 0, tiled=False)
    return jnp.sum(pieces.astype(jnp.float32), axis=0)


def projection_kernel(grad_ref, weight_ref, base_ref, out_ref):
    product = lax.dot_general(
        grad_ref[...], weight_ref[...], (((1,), (1,)), ((), ())), preferred_element_type=jnp.float32
    )
    out_ref[...] = (base_ref[...].astype(jnp.float32) + product).astype(out_ref.dtype)


def projected_sum(grad_rows, weight, base, tile=4096):
    rows, inner = grad_rows.shape
    width = weight.shape[0]
    return pl.pallas_call(
        projection_kernel,
        grid=(width // tile,),
        in_specs=[
            pl.BlockSpec((rows, inner), lambda j: (0, 0)),
            pl.BlockSpec((tile, inner), lambda j: (j, 0)),
            pl.BlockSpec((rows, tile), lambda j: (0, j)),
        ],
        out_specs=pl.BlockSpec((rows, tile), lambda j: (0, j)),
        out_shape=jax.ShapeDtypeStruct((rows, width), base.dtype),
        cost_estimate=pl.CostEstimate(
            flops=2 * rows * inner * width,
            bytes_accessed=2 * (rows * inner + width * inner + 2 * rows * width),
            transcendentals=0,
        ),
    )(grad_rows, weight, base)


RING_OFFSETS = (0, -1, 1, -2)
RING_INDEX_OF_DELTA = (0, 2, 3, 1)


def ring_shift(value, phase, step, side):
    pairs = []
    for source in range(side * side):
        row, col = divmod(source, side)
        if phase == 0:
            target = row * side + (col + step) % side
        else:
            target = ((row + step) % side) * side + col
        pairs.append((source, target))
    return lax.ppermute(value, "ctx", pairs)


def ring_four(value, phase, side):
    from_left = ring_shift(value, phase, 1, side)
    from_right = ring_shift(value, phase, -1, side)
    from_far = ring_shift(from_left, phase, 1, side)
    return jnp.stack([value, from_left, from_right, from_far])


def ring_gather(value, first_phase, side):
    inner = ring_four(value, first_phase, side)
    return ring_four(inner, 1 - first_phase, side).reshape((side * side,) + value.shape)


def ring_position(device, source, first_phase, side):
    index_of_delta = jnp.asarray(RING_INDEX_OF_DELTA, jnp.int32)
    row_delta = index_of_delta[(source // side - device // side) % side]
    col_delta = index_of_delta[(source % side - device % side) % side]
    if first_phase == 0:
        return row_delta * side + col_delta
    return col_delta * side + row_delta


def rope_tables(positions, head_dim):
    half_width = head_dim // 2
    inv_freq = ROPE_BASE ** (-(jnp.arange(half_width, dtype=jnp.float32) * 2.0 / head_dim))
    angles = positions.astype(jnp.float32)[:, None] * inv_freq[None, :]
    angles = jnp.concatenate([angles, angles], axis=1)
    return (jnp.cos(angles), jnp.sin(angles))


def unrotate(gradient, positions):
    cosine, sine_table = rope_tables(positions, gradient.shape[1])
    half_width = gradient.shape[1] // 2
    turned = jnp.concatenate([-gradient[:, half_width:], gradient[:, :half_width]], axis=1)
    return gradient * cosine - turned * sine_table


def doc_ids(positions, lengths):
    doc_ends = jnp.cumsum(lengths)[:-1]
    return jnp.sum((positions[:, None] >= doc_ends[None, :]).astype(jnp.int32), axis=1)


def seq_to_stored(rows, block_order, device, ctx_size, per_device):
    width = rows.shape[1]
    first_block = device * per_device
    blocks = rows.reshape(per_device, BLOCK, width)
    pieces = []
    for slot_k in range(per_device):
        offset = slot_k * ctx_size // per_device
        slot_at = (device - offset) % ctx_size * per_device + slot_k
        local_index = block_order[slot_at] - first_block
        chosen = lax.dynamic_index_in_dim(blocks, local_index, 0, keepdims=False)
        if slot_k > 0:
            chosen = passed_along(chosen, "ctx", -offset)
        pieces.append(chosen)
    return jnp.concatenate(pieces, axis=0)


def stored_to_seq(rows, block_order, device, ctx_size, per_device):
    width = rows.shape[1]
    first_block = device * per_device
    blocks = rows.reshape(per_device, BLOCK, width)
    pieces = []
    local_ids = []
    for slot_k in range(per_device):
        offset = slot_k * ctx_size // per_device
        piece = blocks[slot_k]
        if slot_k > 0:
            piece = passed_along(piece, "ctx", offset)
        pieces.append(piece)
        sender_slot = (device - offset) % ctx_size * per_device + slot_k
        local_ids.append(block_order[sender_slot] - first_block)
    stacked = jnp.stack(pieces)
    index_list = jnp.stack(local_ids)
    choose = (jnp.arange(per_device, dtype=jnp.int32)[:, None] == index_list[None, :]).astype(
        rows.dtype
    )
    placed = jnp.einsum("pk,kbw->pbw", choose, stacked, preferred_element_type=jnp.float32)
    return placed.astype(rows.dtype).reshape(-1, width)


def contract_rows(left_rows, right_rows):
    return lax.dot_general(
        left_rows, right_rows, (((0,), (0,)), ((), ())), preferred_element_type=jnp.float32
    )


def contract_cols(left_rows, right_rows):
    return lax.dot_general(
        left_rows, right_rows, (((1,), (1,)), ((), ())), preferred_element_type=jnp.float32
    )


def block_scores(query_rows, key_rows, query_pos, query_doc, key_pos, key_doc, score_scale):
    scores = contract_cols(query_rows, key_rows) * score_scale
    visible = (query_doc[:, None] == key_doc[None, :]) & (key_pos[None, :] <= query_pos[:, None])
    return (scores, visible)


def body(grad_in, query, keyval, w_qkv, w_out, doc_lengths, order):
    section_grad_in = grad_in[0]
    stored_query = query[0]
    stored_keyval = keyval[0]
    in_weight = w_qkv[0]
    out_weight = w_out[0]
    lengths = doc_lengths[0]
    block_order = order[0]
    ctx_size = lax.axis_size("ctx")
    device = lax.axis_index("ctx")
    local_rows = section_grad_in.shape[0]
    head_dim = stored_keyval.shape[1] // 2
    group = stored_query.shape[1] // head_dim
    per_device = local_rows // BLOCK
    block_count = block_order.shape[0]
    seq_len = local_rows * ctx_size
    first_row = device * local_rows
    score_scale = 1.0 / math.sqrt(head_dim)
    key_block = math.gcd(seq_len, 512)
    key_steps = seq_len // key_block
    within = jnp.arange(BLOCK, dtype=jnp.int32)
    next_weight = lax.all_gather(passed_along_2(in_weight, "pipe", -1), "ctx", axis=0, tiled=True)
    out_grad = jnp.dot(
        section_grad_in,
        lax.all_gather(out_weight, "ctx", axis=0, tiled=True),
        preferred_element_type=jnp.float32,
    ).astype(jnp.bfloat16)
    local_out_grad = out_grad
    seq_query = stored_to_seq(stored_query, block_order, device, ctx_size, per_device)
    side = math.isqrt(ctx_size)
    slot_ids = jnp.arange(block_count, dtype=jnp.int32)
    if side == len(RING_OFFSETS) and per_device == 2:
        gathered = jnp.concatenate(
            [
                ring_gather(stored_keyval[:BLOCK], 0, side),
                ring_gather(stored_keyval[BLOCK:], 1, side),
            ]
        ).reshape(seq_len, 2 * head_dim)
        holder = slot_ids // per_device
        slot_place = jnp.where(
            slot_ids % per_device == 0,
            ring_position(device, holder, 0, side),
            ctx_size + ring_position(device, holder, 1, side),
        )
    else:
        gathered = gathered_rows(stored_keyval, "ctx")
        slot_place = slot_ids
    gathered, grad_source = lax.optimization_barrier((gathered, section_grad_in))
    next_grad_in = passed_along_2(grad_source, "pipe", -1)
    inverse = jnp.sum(
        jnp.where(block_order[None, :] == slot_ids[:, None], slot_place[None, :], 0), axis=1
    )
    all_keyval = gathered.reshape(block_count, BLOCK, 2 * head_dim)[inverse].reshape(
        seq_len, 2 * head_dim
    )
    key_positions = jnp.arange(seq_len, dtype=jnp.int32)
    key_docs = doc_ids(key_positions, lengths)
    query_pos = first_row + jnp.arange(local_rows, dtype=jnp.int32)
    query_doc = doc_ids(query_pos, lengths)
    flat_rows = local_rows * group
    flat_query = seq_query.reshape(flat_rows, head_dim)
    flat_grad = local_out_grad.reshape(flat_rows, head_dim)
    flat_pos = jnp.repeat(query_pos, group)
    flat_doc = jnp.repeat(query_doc, group)
    key_blocks = (
        all_keyval.reshape(key_steps, key_block, 2 * head_dim),
        key_positions.reshape(key_steps, key_block),
        key_docs.reshape(key_steps, key_block),
    )

    def running_total(carried, current):
        row_top, row_total, weighted = carried
        pair_rows, key_pos, key_doc = current
        scores, visible = block_scores(
            flat_query, pair_rows[:, :head_dim], flat_pos, flat_doc, key_pos, key_doc, score_scale
        )
        new_top = jnp.maximum(row_top, jnp.max(jnp.where(visible, scores, MASKED), axis=1))
        rescale = jnp.exp(row_top - new_top)
        weights = jnp.where(visible, jnp.exp(scores - new_top[:, None]), 0.0)
        row_total = row_total * rescale + jnp.sum(weights, axis=1)
        value_wide = pair_rows[:, head_dim:].astype(jnp.float32)
        weighted = weighted * rescale[:, None] + jnp.dot(
            weights, value_wide, precision=lax.Precision.DEFAULT
        )
        return ((new_top, row_total, weighted), None)

    start_top = jnp.full((flat_rows,), MASKED, jnp.float32)
    start_carry = (
        start_top,
        jnp.zeros((flat_rows,), jnp.float32),
        jnp.zeros((flat_rows, head_dim), jnp.float32),
    )
    (row_top, row_total, weighted), unused = lax.scan(running_total, start_carry, key_blocks)
    log_total = row_top + jnp.log(row_total)
    attn_out = weighted / row_total[:, None]
    row_delta = jnp.sum(flat_grad.astype(jnp.float32) * attn_out, axis=1)

    def grad_step(summed, current):
        pair_rows, key_pos, key_doc = current
        scores, visible = block_scores(
            flat_query, pair_rows[:, :head_dim], flat_pos, flat_doc, key_pos, key_doc, score_scale
        )
        attn_prob = jnp.where(visible, jnp.exp(scores - log_total[:, None]), 0.0)
        prob_grad = contract_cols(flat_grad, pair_rows[:, head_dim:])
        score_grad = (score_scale * attn_prob * (prob_grad - row_delta[:, None])).astype(
            jnp.bfloat16
        )
        summed = summed + jnp.dot(
            score_grad, pair_rows[:, :head_dim], preferred_element_type=jnp.float32
        )
        key_term = contract_rows(score_grad, flat_query)
        value_term = contract_rows(attn_prob.astype(jnp.bfloat16), flat_grad)
        return (summed, jnp.concatenate([key_term, value_term], axis=1))

    query_grad_rot, key_terms = lax.scan(
        grad_step, jnp.zeros((flat_rows, head_dim), jnp.float32), key_blocks
    )
    own_positions = first_row + jnp.arange(local_rows, dtype=jnp.int32)
    query_grad = (
        unrotate(query_grad_rot, flat_pos)
        .reshape(local_rows, group * head_dim)
        .astype(jnp.bfloat16)
    )
    next_query_grad = passed_along_2(query_grad, "pipe", -1)
    keyval_grad = summed_rows(
        key_terms.reshape(seq_len, 2 * head_dim).astype(jnp.bfloat16), "ctx"
    )
    key_grad = unrotate(keyval_grad[:, :head_dim], own_positions).astype(jnp.bfloat16)
    value_grad = keyval_grad[:, head_dim:].astype(jnp.bfloat16)
    next_keyval_grad = passed_along_2(
        jnp.concatenate([key_grad, value_grad], axis=1), "pipe", -1
    )
    next_qkv_grad = jnp.concatenate([next_query_grad, next_keyval_grad], axis=1)
    passed = projected_sum(next_qkv_grad, next_weight, next_grad_in)
    return passed[None]


def solution(mesh):
    return jax.shard_map(
        body,
        mesh=mesh,
        in_specs=(
            P("pipe", "ctx", None),
            P("pipe", "ctx", None),
            P("pipe", "ctx", None),
            P("pipe", "ctx", None),
            P("pipe", "ctx", None),
            P("pipe", None),
            P("pipe", None),
        ),
        out_specs=P("pipe", "ctx", None),
        check_vma=False,
    )
```

```python
import math

import jax
import jax.numpy as jnp
from jax import lax
from jax.experimental import pallas as pl
from jax.sharding import PartitionSpec as P

BLOCK = 128


ROPE_BASE = 500000.0
MASKED = -1e30


def passed_along(value, axis, steps):
    count = lax.axis_size(axis)
    pairs = [(source, (source + steps) % count) for source in range(count)]
    return lax.ppermute(value, axis, pairs)


def passed_along_2(value, axis, by):
    size = lax.axis_size(axis)
    pairs = [(i, i + by) for i in range(size) if 0 <= i + by < size]
    return lax.ppermute(value, axis, pairs)


def gathered_rows(value, axis):
    count = lax.axis_size(axis)
    spread = jnp.broadcast_to(value[None], (count,) + value.shape)
    return lax.all_to_all(spread, axis, 0, 0, tiled=False).reshape((-1,) + value.shape[1:])


def summed_rows(value, axis):
    count = lax.axis_size(axis)
    pieces = lax.all_to_all(value.reshape((count, -1) + value.shape[1:]), axis, 0, 0, tiled=False)
    return jnp.sum(pieces.astype(jnp.float32), axis=0)


def projection_kernel(grad_ref, weight_ref, base_ref, out_ref):
    product = lax.dot_general(
        grad_ref[...], weight_ref[...], (((1,), (1,)), ((), ())), preferred_element_type=jnp.float32
    )
    out_ref[...] = (base_ref[...].astype(jnp.float32) + product).astype(out_ref.dtype)


def projected_sum(grad_rows, weight, base, tile=4096):
    rows, inner = grad_rows.shape
    width = weight.shape[0]
    return pl.pallas_call(
        projection_kernel,
        grid=(width // tile,),
        in_specs=[
            pl.BlockSpec((rows, inner), lambda j: (0, 0)),
            pl.BlockSpec((tile, inner), lambda j: (j, 0)),
            pl.BlockSpec((rows, tile), lambda j: (0, j)),
        ],
        out_specs=pl.BlockSpec((rows, tile), lambda j: (0, j)),
        out_shape=jax.ShapeDtypeStruct((rows, width), base.dtype),
        cost_estimate=pl.CostEstimate(
            flops=2 * rows * inner * width,
            bytes_accessed=2 * (rows * inner + width * inner + 2 * rows * width),
            transcendentals=0,
        ),
    )(grad_rows, weight, base)


RING_OFFSETS = (0, -1, 1, -2)
RING_INDEX_OF_DELTA = (0, 2, 3, 1)


def ring_shift(value, phase, step, side):
    pairs = []
    for source in range(side * side):
        row, col = divmod(source, side)
        if phase == 0:
            target = row * side + (col + step) % side
        else:
            target = ((row + step) % side) * side + col
        pairs.append((source, target))
    return lax.ppermute(value, "ctx", pairs)


def ring_four(value, phase, side):
    from_left = ring_shift(value, phase, 1, side)
    from_right = ring_shift(value, phase, -1, side)
    from_far = ring_shift(from_left, phase, 1, side)
    return jnp.stack([value, from_left, from_right, from_far])


def ring_gather(value, first_phase, side):
    inner = ring_four(value, first_phase, side)
    return ring_four(inner, 1 - first_phase, side).reshape((side * side,) + value.shape)


def ring_reduce(chunks, phase, device, side):
    me = device % side if phase == 0 else device // side
    rel = lax.dynamic_slice_in_dim(jnp.concatenate([chunks, chunks]), me, side, axis=0)
    from_far = ring_shift(rel[2].astype(jnp.bfloat16), phase, 1, side)
    from_right = ring_shift(rel[3].astype(jnp.bfloat16), phase, -1, side)
    carried = (rel[1] + from_far.astype(jnp.float32)).astype(jnp.bfloat16)
    from_left = ring_shift(carried, phase, 1, side)
    return rel[0] + from_right.astype(jnp.float32) + from_left.astype(jnp.float32)


def ring_scatter_sum(rows, device, side):
    region = rows.shape[0] // (side * side)
    width = rows.shape[1]
    tiles = rows.reshape(side, side, region, width)
    half = width // 2
    first = ring_reduce(jnp.moveaxis(tiles[..., :half], 1, 0), 0, device, side)
    first = ring_reduce(first, 1, device, side)
    second = ring_reduce(tiles[..., half:], 1, device, side)
    second = ring_reduce(second, 0, device, side)
    return jnp.concatenate([first, second], axis=1)


def ring_position(device, source, first_phase, side):
    index_of_delta = jnp.asarray(RING_INDEX_OF_DELTA, jnp.int32)
    row_delta = index_of_delta[(source // side - device // side) % side]
    col_delta = index_of_delta[(source % side - device % side) % side]
    if first_phase == 0:
        return row_delta * side + col_delta
    return col_delta * side + row_delta


def rope_tables(positions, head_dim):
    half_width = head_dim // 2
    inv_freq = ROPE_BASE ** (-(jnp.arange(half_width, dtype=jnp.float32) * 2.0 / head_dim))
    angles = positions.astype(jnp.float32)[:, None] * inv_freq[None, :]
    angles = jnp.concatenate([angles, angles], axis=1)
    return (jnp.cos(angles), jnp.sin(angles))


def unrotate(gradient, positions):
    cosine, sine_table = rope_tables(positions, gradient.shape[1])
    half_width = gradient.shape[1] // 2
    turned = jnp.concatenate([-gradient[:, half_width:], gradient[:, :half_width]], axis=1)
    return gradient * cosine - turned * sine_table


def doc_ids(positions, lengths):
    doc_ends = jnp.cumsum(lengths)[:-1]
    return jnp.sum((positions[:, None] >= doc_ends[None, :]).astype(jnp.int32), axis=1)


def seq_to_stored(rows, block_order, device, ctx_size, per_device):
    width = rows.shape[1]
    first_block = device * per_device
    blocks = rows.reshape(per_device, BLOCK, width)
    pieces = []
    for slot_k in range(per_device):
        offset = slot_k * ctx_size // per_device
        slot_at = (device - offset) % ctx_size * per_device + slot_k
        local_index = block_order[slot_at] - first_block
        chosen = lax.dynamic_index_in_dim(blocks, local_index, 0, keepdims=False)
        if slot_k > 0:
            chosen = passed_along(chosen, "ctx", -offset)
        pieces.append(chosen)
    return jnp.concatenate(pieces, axis=0)


def stored_to_seq(rows, block_order, device, ctx_size, per_device):
    width = rows.shape[1]
    first_block = device * per_device
    blocks = rows.reshape(per_device, BLOCK, width)
    pieces = []
    local_ids = []
    for slot_k in range(per_device):
        offset = slot_k * ctx_size // per_device
        piece = blocks[slot_k]
        if slot_k > 0:
            piece = passed_along(piece, "ctx", offset)
        pieces.append(piece)
        sender_slot = (device - offset) % ctx_size * per_device + slot_k
        local_ids.append(block_order[sender_slot] - first_block)
    stacked = jnp.stack(pieces)
    index_list = jnp.stack(local_ids)
    choose = (jnp.arange(per_device, dtype=jnp.int32)[:, None] == index_list[None, :]).astype(
        rows.dtype
    )
    placed = jnp.einsum("pk,kbw->pbw", choose, stacked, preferred_element_type=jnp.float32)
    return placed.astype(rows.dtype).reshape(-1, width)


def contract_rows(left_rows, right_rows):
    return lax.dot_general(
        left_rows, right_rows, (((0,), (0,)), ((), ())), preferred_element_type=jnp.float32
    )


def contract_cols(left_rows, right_rows):
    return lax.dot_general(
        left_rows, right_rows, (((1,), (1,)), ((), ())), preferred_element_type=jnp.float32
    )


def block_scores(query_rows, key_rows, query_pos, query_doc, key_pos, key_doc, score_scale):
    scores = contract_cols(query_rows, key_rows) * score_scale
    visible = (query_doc[:, None] == key_doc[None, :]) & (key_pos[None, :] <= query_pos[:, None])
    return (scores, visible)


def body(grad_in, query, keyval, w_qkv, w_out, doc_lengths, order):
    section_grad_in = grad_in[0]
    stored_query = query[0]
    stored_keyval = keyval[0]
    in_weight = w_qkv[0]
    out_weight = w_out[0]
    lengths = doc_lengths[0]
    block_order = order[0]
    ctx_size = lax.axis_size("ctx")
    device = lax.axis_index("ctx")
    local_rows = section_grad_in.shape[0]
    head_dim = stored_keyval.shape[1] // 2
    group = stored_query.shape[1] // head_dim
    per_device = local_rows // BLOCK
    block_count = block_order.shape[0]
    seq_len = local_rows * ctx_size
    first_row = device * local_rows
    score_scale = 1.0 / math.sqrt(head_dim)
    key_block = math.gcd(seq_len, 512)
    key_steps = seq_len // key_block
    within = jnp.arange(BLOCK, dtype=jnp.int32)
    next_weight = lax.all_gather(passed_along_2(in_weight, "pipe", -1), "ctx", axis=0, tiled=True)
    out_grad = jnp.dot(
        section_grad_in,
        lax.all_gather(out_weight, "ctx", axis=0, tiled=True),
        preferred_element_type=jnp.float32,
    ).astype(jnp.bfloat16)
    local_out_grad = out_grad
    seq_query = stored_to_seq(stored_query, block_order, device, ctx_size, per_device)
    side = math.isqrt(ctx_size)
    slot_ids = jnp.arange(block_count, dtype=jnp.int32)
    if side == len(RING_OFFSETS) and per_device == 2:
        gathered = jnp.concatenate(
            [
                ring_gather(stored_keyval[:BLOCK], 0, side),
                ring_gather(stored_keyval[BLOCK:], 1, side),
            ]
        ).reshape(seq_len, 2 * head_dim)
        holder = slot_ids // per_device
        slot_place = jnp.where(
            slot_ids % per_device == 0,
            ring_position(device, holder, 0, side),
            ctx_size + ring_position(device, holder, 1, side),
        )
    else:
        gathered = gathered_rows(stored_keyval, "ctx")
        slot_place = slot_ids
    gathered, grad_source = lax.optimization_barrier((gathered, section_grad_in))
    next_grad_in = passed_along_2(grad_source, "pipe", -1)
    inverse = jnp.sum(
        jnp.where(block_order[None, :] == slot_ids[:, None], slot_place[None, :], 0), axis=1
    )
    all_keyval = gathered.reshape(block_count, BLOCK, 2 * head_dim)[inverse].reshape(
        seq_len, 2 * head_dim
    )
    key_positions = jnp.arange(seq_len, dtype=jnp.int32)
    key_docs = doc_ids(key_positions, lengths)
    query_pos = first_row + jnp.arange(local_rows, dtype=jnp.int32)
    query_doc = doc_ids(query_pos, lengths)
    flat_rows = local_rows * group
    flat_query = seq_query.reshape(flat_rows, head_dim)
    flat_grad = local_out_grad.reshape(flat_rows, head_dim)
    flat_pos = jnp.repeat(query_pos, group)
    flat_doc = jnp.repeat(query_doc, group)
    key_blocks = (
        all_keyval.reshape(key_steps, key_block, 2 * head_dim),
        key_positions.reshape(key_steps, key_block),
        key_docs.reshape(key_steps, key_block),
    )

    def running_total(carried, current):
        row_top, row_total, weighted = carried
        pair_rows, key_pos, key_doc = current
        scores, visible = block_scores(
            flat_query, pair_rows[:, :head_dim], flat_pos, flat_doc, key_pos, key_doc, score_scale
        )
        new_top = jnp.maximum(row_top, jnp.max(jnp.where(visible, scores, MASKED), axis=1))
        rescale = jnp.exp(row_top - new_top)
        weights = jnp.where(visible, jnp.exp(scores - new_top[:, None]), 0.0)
        row_total = row_total * rescale + jnp.sum(weights, axis=1)
        value_wide = pair_rows[:, head_dim:].astype(jnp.float32)
        weighted = weighted * rescale[:, None] + jnp.dot(
            weights, value_wide, precision=lax.Precision.DEFAULT
        )
        return ((new_top, row_total, weighted), None)

    start_top = jnp.full((flat_rows,), MASKED, jnp.float32)
    start_carry = (
        start_top,
        jnp.zeros((flat_rows,), jnp.float32),
        jnp.zeros((flat_rows, head_dim), jnp.float32),
    )
    (row_top, row_total, weighted), unused = lax.scan(running_total, start_carry, key_blocks)
    log_total = row_top + jnp.log(row_total)
    attn_out = weighted / row_total[:, None]
    row_delta = jnp.sum(flat_grad.astype(jnp.float32) * attn_out, axis=1)

    def grad_step(summed, current):
        pair_rows, key_pos, key_doc = current
        scores, visible = block_scores(
            flat_query, pair_rows[:, :head_dim], flat_pos, flat_doc, key_pos, key_doc, score_scale
        )
        attn_prob = jnp.where(visible, jnp.exp(scores - log_total[:, None]), 0.0)
        prob_grad = contract_cols(flat_grad, pair_rows[:, head_dim:])
        score_grad = (score_scale * attn_prob * (prob_grad - row_delta[:, None])).astype(
            jnp.bfloat16
        )
        summed = summed + jnp.dot(
            score_grad, pair_rows[:, :head_dim], preferred_element_type=jnp.float32
        )
        key_term = contract_rows(score_grad, flat_query)
        value_term = contract_rows(attn_prob.astype(jnp.bfloat16), flat_grad)
        return (summed, jnp.concatenate([key_term, value_term], axis=1))

    query_grad_rot, key_terms = lax.scan(
        grad_step, jnp.zeros((flat_rows, head_dim), jnp.float32), key_blocks
    )
    own_positions = first_row + jnp.arange(local_rows, dtype=jnp.int32)
    query_grad = (
        unrotate(query_grad_rot, flat_pos)
        .reshape(local_rows, group * head_dim)
        .astype(jnp.bfloat16)
    )
    next_query_grad = passed_along_2(query_grad, "pipe", -1)
    if side == len(RING_OFFSETS):
        keyval_grad = ring_scatter_sum(key_terms.reshape(seq_len, 2 * head_dim), device, side)
    else:
        keyval_grad = summed_rows(
            key_terms.reshape(seq_len, 2 * head_dim).astype(jnp.bfloat16), "ctx"
        )
    key_grad = unrotate(keyval_grad[:, :head_dim], own_positions).astype(jnp.bfloat16)
    value_grad = keyval_grad[:, head_dim:].astype(jnp.bfloat16)
    next_keyval_grad = passed_along_2(
        jnp.concatenate([key_grad, value_grad], axis=1), "pipe", -1
    )
    next_qkv_grad = jnp.concatenate([next_query_grad, next_keyval_grad], axis=1)
    passed = projected_sum(next_qkv_grad, next_weight, next_grad_in)
    return passed[None]


def solution(mesh):
    return jax.shard_map(
        body,
        mesh=mesh,
        in_specs=(
            P("pipe", "ctx", None),
            P("pipe", "ctx", None),
            P("pipe", "ctx", None),
            P("pipe", "ctx", None),
            P("pipe", "ctx", None),
            P("pipe", None),
            P("pipe", None),
        ),
        out_specs=P("pipe", "ctx", None),
        check_vma=False,
    )
```

```python
import math

import jax
import jax.numpy as jnp
from jax import lax
from jax.experimental import pallas as pl
from jax.sharding import PartitionSpec as P

BLOCK = 128


ROPE_BASE = 500000.0
MASKED = -1e30


def passed_along(value, axis, steps):
    count = lax.axis_size(axis)
    pairs = [(source, (source + steps) % count) for source in range(count)]
    return lax.ppermute(value, axis, pairs)


def passed_along_2(value, axis, by):
    size = lax.axis_size(axis)
    pairs = [(i, i + by) for i in range(size) if 0 <= i + by < size]
    return lax.ppermute(value, axis, pairs)


def gathered_rows(value, axis):
    count = lax.axis_size(axis)
    spread = jnp.broadcast_to(value[None], (count,) + value.shape)
    return lax.all_to_all(spread, axis, 0, 0, tiled=False).reshape((-1,) + value.shape[1:])


def summed_rows(value, axis):
    count = lax.axis_size(axis)
    pieces = lax.all_to_all(value.reshape((count, -1) + value.shape[1:]), axis, 0, 0, tiled=False)
    return jnp.sum(pieces.astype(jnp.float32), axis=0)


def projection_kernel(grad_ref, weight_ref, base_ref, out_ref):
    product = lax.dot_general(
        grad_ref[...], weight_ref[...], (((1,), (1,)), ((), ())), preferred_element_type=jnp.float32
    )
    out_ref[...] = (base_ref[...].astype(jnp.float32) + product).astype(out_ref.dtype)


def projected_sum(grad_rows, weight, base, first_column, out_dtype, tile=4096):
    rows, inner = grad_rows.shape
    width = weight.shape[0]
    column_block = first_column // inner
    return pl.pallas_call(
        projection_kernel,
        grid=(width // tile,),
        in_specs=[
            pl.BlockSpec((rows, inner), lambda j: (0, 0)),
            pl.BlockSpec((tile, inner), lambda j: (j, column_block)),
            pl.BlockSpec((rows, tile), lambda j: (0, j)),
        ],
        out_specs=pl.BlockSpec((rows, tile), lambda j: (0, j)),
        out_shape=jax.ShapeDtypeStruct((rows, width), out_dtype),
        cost_estimate=pl.CostEstimate(
            flops=2 * rows * inner * width,
            bytes_accessed=2 * (rows * inner + width * inner) + 6 * rows * width,
            transcendentals=0,
        ),
    )(grad_rows, weight, base)


RING_OFFSETS = (0, -1, 1, -2)
RING_INDEX_OF_DELTA = (0, 2, 3, 1)


def ring_shift(value, phase, step, side):
    pairs = []
    for source in range(side * side):
        row, col = divmod(source, side)
        if phase == 0:
            target = row * side + (col + step) % side
        else:
            target = ((row + step) % side) * side + col
        pairs.append((source, target))
    return lax.ppermute(value, "ctx", pairs)


def ring_four(value, phase, side):
    from_left = ring_shift(value, phase, 1, side)
    from_right = ring_shift(value, phase, -1, side)
    from_far = ring_shift(from_left, phase, 1, side)
    return jnp.stack([value, from_left, from_right, from_far])


def ring_gather(value, first_phase, side):
    inner = ring_four(value, first_phase, side)
    return ring_four(inner, 1 - first_phase, side).reshape((side * side,) + value.shape)


def ring_reduce(chunks, phase, device, side):
    me = device % side if phase == 0 else device // side
    rel = lax.dynamic_slice_in_dim(jnp.concatenate([chunks, chunks]), me, side, axis=0)
    from_far = ring_shift(rel[2].astype(jnp.bfloat16), phase, 1, side)
    from_right = ring_shift(rel[3].astype(jnp.bfloat16), phase, -1, side)
    carried = (rel[1] + from_far.astype(jnp.float32)).astype(jnp.bfloat16)
    from_left = ring_shift(carried, phase, 1, side)
    return rel[0] + from_right.astype(jnp.float32) + from_left.astype(jnp.float32)


def ring_scatter_sum(rows, device, side):
    region = rows.shape[0] // (side * side)
    width = rows.shape[1]
    tiles = rows.reshape(side, side, region, width)
    half = width // 2
    first = ring_reduce(jnp.moveaxis(tiles[..., :half], 1, 0), 0, device, side)
    first = ring_reduce(first, 1, device, side)
    second = ring_reduce(tiles[..., half:], 1, device, side)
    second = ring_reduce(second, 0, device, side)
    return jnp.concatenate([first, second], axis=1)


def ring_position(device, source, first_phase, side):
    index_of_delta = jnp.asarray(RING_INDEX_OF_DELTA, jnp.int32)
    row_delta = index_of_delta[(source // side - device // side) % side]
    col_delta = index_of_delta[(source % side - device % side) % side]
    if first_phase == 0:
        return row_delta * side + col_delta
    return col_delta * side + row_delta


def rope_tables(positions, head_dim):
    half_width = head_dim // 2
    inv_freq = ROPE_BASE ** (-(jnp.arange(half_width, dtype=jnp.float32) * 2.0 / head_dim))
    angles = positions.astype(jnp.float32)[:, None] * inv_freq[None, :]
    angles = jnp.concatenate([angles, angles], axis=1)
    return (jnp.cos(angles), jnp.sin(angles))


def unrotate(gradient, positions):
    cosine, sine_table = rope_tables(positions, gradient.shape[1])
    half_width = gradient.shape[1] // 2
    turned = jnp.concatenate([-gradient[:, half_width:], gradient[:, :half_width]], axis=1)
    return gradient * cosine - turned * sine_table


def doc_ids(positions, lengths):
    doc_ends = jnp.cumsum(lengths)[:-1]
    return jnp.sum((positions[:, None] >= doc_ends[None, :]).astype(jnp.int32), axis=1)


def seq_to_stored(rows, block_order, device, ctx_size, per_device):
    width = rows.shape[1]
    first_block = device * per_device
    blocks = rows.reshape(per_device, BLOCK, width)
    pieces = []
    for slot_k in range(per_device):
        offset = slot_k * ctx_size // per_device
        slot_at = (device - offset) % ctx_size * per_device + slot_k
        local_index = block_order[slot_at] - first_block
        chosen = lax.dynamic_index_in_dim(blocks, local_index, 0, keepdims=False)
        if slot_k > 0:
            chosen = passed_along(chosen, "ctx", -offset)
        pieces.append(chosen)
    return jnp.concatenate(pieces, axis=0)


def stored_to_seq(rows, block_order, device, ctx_size, per_device):
    width = rows.shape[1]
    first_block = device * per_device
    blocks = rows.reshape(per_device, BLOCK, width)
    pieces = []
    local_ids = []
    for slot_k in range(per_device):
        offset = slot_k * ctx_size // per_device
        piece = blocks[slot_k]
        if slot_k > 0:
            piece = passed_along(piece, "ctx", offset)
        pieces.append(piece)
        sender_slot = (device - offset) % ctx_size * per_device + slot_k
        local_ids.append(block_order[sender_slot] - first_block)
    stacked = jnp.stack(pieces)
    index_list = jnp.stack(local_ids)
    choose = (jnp.arange(per_device, dtype=jnp.int32)[:, None] == index_list[None, :]).astype(
        rows.dtype
    )
    placed = jnp.einsum("pk,kbw->pbw", choose, stacked, preferred_element_type=jnp.float32)
    return placed.astype(rows.dtype).reshape(-1, width)


def contract_rows(left_rows, right_rows):
    return lax.dot_general(
        left_rows, right_rows, (((0,), (0,)), ((), ())), preferred_element_type=jnp.float32
    )


def contract_cols(left_rows, right_rows):
    return lax.dot_general(
        left_rows, right_rows, (((1,), (1,)), ((), ())), preferred_element_type=jnp.float32
    )


def block_scores(query_rows, key_rows, query_pos, query_doc, key_pos, key_doc, score_scale):
    scores = contract_cols(query_rows, key_rows) * score_scale
    visible = (query_doc[:, None] == key_doc[None, :]) & (key_pos[None, :] <= query_pos[:, None])
    return (scores, visible)


def body(grad_in, query, keyval, w_qkv, w_out, doc_lengths, order):
    section_grad_in = grad_in[0]
    stored_query = query[0]
    stored_keyval = keyval[0]
    in_weight = w_qkv[0]
    out_weight = w_out[0]
    lengths = doc_lengths[0]
    block_order = order[0]
    ctx_size = lax.axis_size("ctx")
    device = lax.axis_index("ctx")
    local_rows = section_grad_in.shape[0]
    head_dim = stored_keyval.shape[1] // 2
    group = stored_query.shape[1] // head_dim
    per_device = local_rows // BLOCK
    block_count = block_order.shape[0]
    seq_len = local_rows * ctx_size
    first_row = device * local_rows
    score_scale = 1.0 / math.sqrt(head_dim)
    key_block = math.gcd(seq_len, 512)
    key_steps = seq_len // key_block
    within = jnp.arange(BLOCK, dtype=jnp.int32)
    next_weight = lax.all_gather(passed_along_2(in_weight, "pipe", -1), "ctx", axis=0, tiled=True)
    out_grad = jnp.dot(
        section_grad_in,
        lax.all_gather(out_weight, "ctx", axis=0, tiled=True),
        preferred_element_type=jnp.float32,
    ).astype(jnp.bfloat16)
    local_out_grad = out_grad
    seq_query = stored_to_seq(stored_query, block_order, device, ctx_size, per_device)
    side = math.isqrt(ctx_size)
    slot_ids = jnp.arange(block_count, dtype=jnp.int32)
    if side == len(RING_OFFSETS) and per_device == 2:
        gathered = jnp.concatenate(
            [
                ring_gather(stored_keyval[:BLOCK], 0, side),
                ring_gather(stored_keyval[BLOCK:], 1, side),
            ]
        ).reshape(seq_len, 2 * head_dim)
        holder = slot_ids // per_device
        slot_place = jnp.where(
            slot_ids % per_device == 0,
            ring_position(device, holder, 0, side),
            ctx_size + ring_position(device, holder, 1, side),
        )
    else:
        gathered = gathered_rows(stored_keyval, "ctx")
        slot_place = slot_ids
    gathered, grad_source = lax.optimization_barrier((gathered, section_grad_in))
    next_grad_in = passed_along_2(grad_source, "pipe", -1)
    inverse = jnp.sum(
        jnp.where(block_order[None, :] == slot_ids[:, None], slot_place[None, :], 0), axis=1
    )
    all_keyval = gathered.reshape(block_count, BLOCK, 2 * head_dim)[inverse].reshape(
        seq_len, 2 * head_dim
    )
    key_positions = jnp.arange(seq_len, dtype=jnp.int32)
    key_docs = doc_ids(key_positions, lengths)
    query_pos = first_row + jnp.arange(local_rows, dtype=jnp.int32)
    query_doc = doc_ids(query_pos, lengths)
    flat_rows = local_rows * group
    flat_query = seq_query.reshape(flat_rows, head_dim)
    flat_grad = local_out_grad.reshape(flat_rows, head_dim)
    flat_pos = jnp.repeat(query_pos, group)
    flat_doc = jnp.repeat(query_doc, group)
    key_blocks = (
        all_keyval.reshape(key_steps, key_block, 2 * head_dim),
        key_positions.reshape(key_steps, key_block),
        key_docs.reshape(key_steps, key_block),
    )

    def running_total(carried, current):
        row_top, row_total, weighted = carried
        pair_rows, key_pos, key_doc = current
        scores, visible = block_scores(
            flat_query, pair_rows[:, :head_dim], flat_pos, flat_doc, key_pos, key_doc, score_scale
        )
        new_top = jnp.maximum(row_top, jnp.max(jnp.where(visible, scores, MASKED), axis=1))
        rescale = jnp.exp(row_top - new_top)
        weights = jnp.where(visible, jnp.exp(scores - new_top[:, None]), 0.0)
        row_total = row_total * rescale + jnp.sum(weights, axis=1)
        value_wide = pair_rows[:, head_dim:].astype(jnp.float32)
        weighted = weighted * rescale[:, None] + jnp.dot(
            weights, value_wide, precision=lax.Precision.DEFAULT
        )
        return ((new_top, row_total, weighted), None)

    start_top = jnp.full((flat_rows,), MASKED, jnp.float32)
    start_carry = (
        start_top,
        jnp.zeros((flat_rows,), jnp.float32),
        jnp.zeros((flat_rows, head_dim), jnp.float32),
    )
    (row_top, row_total, weighted), unused = lax.scan(running_total, start_carry, key_blocks)
    log_total = row_top + jnp.log(row_total)
    attn_out = weighted / row_total[:, None]
    row_delta = jnp.sum(flat_grad.astype(jnp.float32) * attn_out, axis=1)

    def grad_step(summed, current):
        pair_rows, key_pos, key_doc = current
        scores, visible = block_scores(
            flat_query, pair_rows[:, :head_dim], flat_pos, flat_doc, key_pos, key_doc, score_scale
        )
        attn_prob = jnp.where(visible, jnp.exp(scores - log_total[:, None]), 0.0)
        prob_grad = contract_cols(flat_grad, pair_rows[:, head_dim:])
        score_grad = (score_scale * attn_prob * (prob_grad - row_delta[:, None])).astype(
            jnp.bfloat16
        )
        summed = summed + jnp.dot(
            score_grad, pair_rows[:, :head_dim], preferred_element_type=jnp.float32
        )
        key_term = contract_rows(score_grad, flat_query)
        value_term = contract_rows(attn_prob.astype(jnp.bfloat16), flat_grad)
        return (summed, jnp.concatenate([key_term, value_term], axis=1))

    query_grad_rot, key_terms = lax.scan(
        grad_step, jnp.zeros((flat_rows, head_dim), jnp.float32), key_blocks
    )
    own_positions = first_row + jnp.arange(local_rows, dtype=jnp.int32)
    query_grad = (
        unrotate(query_grad_rot, flat_pos)
        .reshape(local_rows, group * head_dim)
        .astype(jnp.bfloat16)
    )
    next_query_grad = passed_along_2(query_grad, "pipe", -1)
    if side == len(RING_OFFSETS):
        keyval_grad = ring_scatter_sum(key_terms.reshape(seq_len, 2 * head_dim), device, side)
    else:
        keyval_grad = summed_rows(
            key_terms.reshape(seq_len, 2 * head_dim).astype(jnp.bfloat16), "ctx"
        )
    key_grad = unrotate(keyval_grad[:, :head_dim], own_positions).astype(jnp.bfloat16)
    value_grad = keyval_grad[:, head_dim:].astype(jnp.bfloat16)
    next_keyval_grad = passed_along_2(
        jnp.concatenate([key_grad, value_grad], axis=1), "pipe", -1
    )
    query_width = next_query_grad.shape[1]
    partial = projected_sum(next_query_grad, next_weight, next_grad_in, 0, jnp.float32)
    passed = projected_sum(next_keyval_grad, next_weight, partial, query_width, jnp.bfloat16)
    return passed[None]


def solution(mesh):
    return jax.shard_map(
        body,
        mesh=mesh,
        in_specs=(
            P("pipe", "ctx", None),
            P("pipe", "ctx", None),
            P("pipe", "ctx", None),
            P("pipe", "ctx", None),
            P("pipe", "ctx", None),
            P("pipe", None),
            P("pipe", None),
        ),
        out_specs=P("pipe", "ctx", None),
        check_vma=False,
    )
```

```python
import math

import jax
import jax.numpy as jnp
from jax import lax
from jax.experimental import pallas as pl
from jax.sharding import PartitionSpec as P

BLOCK = 128


ROPE_BASE = 500000.0
MASKED = -1e30


def passed_along(value, axis, steps):
    count = lax.axis_size(axis)
    pairs = [(source, (source + steps) % count) for source in range(count)]
    return lax.ppermute(value, axis, pairs)


def passed_along_2(value, axis, by):
    size = lax.axis_size(axis)
    pairs = [(i, i + by) for i in range(size) if 0 <= i + by < size]
    return lax.ppermute(value, axis, pairs)


def gathered_rows(value, axis):
    count = lax.axis_size(axis)
    spread = jnp.broadcast_to(value[None], (count,) + value.shape)
    return lax.all_to_all(spread, axis, 0, 0, tiled=False).reshape((-1,) + value.shape[1:])


def summed_rows(value, axis):
    count = lax.axis_size(axis)
    pieces = lax.all_to_all(value.reshape((count, -1) + value.shape[1:]), axis, 0, 0, tiled=False)
    return jnp.sum(pieces.astype(jnp.float32), axis=0)


def projection_kernel(grad_ref, weight_ref, base_ref, out_ref):
    product = lax.dot_general(
        grad_ref[...], weight_ref[...], (((1,), (1,)), ((), ())), preferred_element_type=jnp.float32
    )
    out_ref[...] = (base_ref[...].astype(jnp.float32) + product).astype(out_ref.dtype)


def projected_sum(grad_rows, weight, base, tile=4096):
    rows, inner = grad_rows.shape
    width = weight.shape[0]
    return pl.pallas_call(
        projection_kernel,
        grid=(width // tile,),
        in_specs=[
            pl.BlockSpec((rows, inner), lambda j: (0, 0)),
            pl.BlockSpec((tile, inner), lambda j: (j, 0)),
            pl.BlockSpec((rows, tile), lambda j: (0, j)),
        ],
        out_specs=pl.BlockSpec((rows, tile), lambda j: (0, j)),
        out_shape=jax.ShapeDtypeStruct((rows, width), base.dtype),
        cost_estimate=pl.CostEstimate(
            flops=2 * rows * inner * width,
            bytes_accessed=2 * (rows * inner + width * inner + 2 * rows * width),
            transcendentals=0,
        ),
    )(grad_rows, weight, base)


RING_OFFSETS = (0, -1, 1, -2)
RING_INDEX_OF_DELTA = (0, 2, 3, 1)


def ring_shift(value, phase, step, side):
    pairs = []
    for source in range(side * side):
        row, col = divmod(source, side)
        if phase == 0:
            target = row * side + (col + step) % side
        else:
            target = ((row + step) % side) * side + col
        pairs.append((source, target))
    return lax.ppermute(value, "ctx", pairs)


def ring_four(value, phase, side):
    from_left = ring_shift(value, phase, 1, side)
    from_right = ring_shift(value, phase, -1, side)
    from_far = ring_shift(from_left, phase, 1, side)
    return jnp.stack([value, from_left, from_right, from_far])


def ring_gather(value, first_phase, side):
    inner = ring_four(value, first_phase, side)
    return ring_four(inner, 1 - first_phase, side).reshape((side * side,) + value.shape)


def ring_reduce(chunks, phase, device, side):
    me = device % side if phase == 0 else device // side
    rel = lax.dynamic_slice_in_dim(jnp.concatenate([chunks, chunks]), me, side, axis=0)
    from_far = ring_shift(rel[2].astype(jnp.bfloat16), phase, 1, side)
    from_right = ring_shift(rel[3].astype(jnp.bfloat16), phase, -1, side)
    carried = (rel[1] + from_far.astype(jnp.float32)).astype(jnp.bfloat16)
    from_left = ring_shift(carried, phase, 1, side)
    return rel[0] + from_right.astype(jnp.float32) + from_left.astype(jnp.float32)


def ring_scatter_sum(rows, device, side):
    region = rows.shape[0] // (side * side)
    width = rows.shape[1]
    tiles = rows.reshape(side, side, region, width)
    half = width // 2
    first = ring_reduce(jnp.moveaxis(tiles[..., :half], 1, 0), 0, device, side)
    first = ring_reduce(first, 1, device, side)
    second = summed_rows(rows[:, half:].astype(jnp.bfloat16), "ctx")
    return jnp.concatenate([first, second], axis=1)


def ring_position(device, source, first_phase, side):
    index_of_delta = jnp.asarray(RING_INDEX_OF_DELTA, jnp.int32)
    row_delta = index_of_delta[(source // side - device // side) % side]
    col_delta = index_of_delta[(source % side - device % side) % side]
    if first_phase == 0:
        return row_delta * side + col_delta
    return col_delta * side + row_delta


def rope_tables(positions, head_dim):
    half_width = head_dim // 2
    inv_freq = ROPE_BASE ** (-(jnp.arange(half_width, dtype=jnp.float32) * 2.0 / head_dim))
    angles = positions.astype(jnp.float32)[:, None] * inv_freq[None, :]
    angles = jnp.concatenate([angles, angles], axis=1)
    return (jnp.cos(angles), jnp.sin(angles))


def unrotate(gradient, positions):
    cosine, sine_table = rope_tables(positions, gradient.shape[1])
    half_width = gradient.shape[1] // 2
    turned = jnp.concatenate([-gradient[:, half_width:], gradient[:, :half_width]], axis=1)
    return gradient * cosine - turned * sine_table


def doc_ids(positions, lengths):
    doc_ends = jnp.cumsum(lengths)[:-1]
    return jnp.sum((positions[:, None] >= doc_ends[None, :]).astype(jnp.int32), axis=1)


def seq_to_stored(rows, block_order, device, ctx_size, per_device):
    width = rows.shape[1]
    first_block = device * per_device
    blocks = rows.reshape(per_device, BLOCK, width)
    pieces = []
    for slot_k in range(per_device):
        offset = slot_k * ctx_size // per_device
        slot_at = (device - offset) % ctx_size * per_device + slot_k
        local_index = block_order[slot_at] - first_block
        chosen = lax.dynamic_index_in_dim(blocks, local_index, 0, keepdims=False)
        if slot_k > 0:
            chosen = passed_along(chosen, "ctx", -offset)
        pieces.append(chosen)
    return jnp.concatenate(pieces, axis=0)


def stored_to_seq(rows, block_order, device, ctx_size, per_device):
    width = rows.shape[1]
    first_block = device * per_device
    blocks = rows.reshape(per_device, BLOCK, width)
    pieces = []
    local_ids = []
    for slot_k in range(per_device):
        offset = slot_k * ctx_size // per_device
        piece = blocks[slot_k]
        if slot_k > 0:
            piece = passed_along(piece, "ctx", offset)
        pieces.append(piece)
        sender_slot = (device - offset) % ctx_size * per_device + slot_k
        local_ids.append(block_order[sender_slot] - first_block)
    stacked = jnp.stack(pieces)
    index_list = jnp.stack(local_ids)
    choose = (jnp.arange(per_device, dtype=jnp.int32)[:, None] == index_list[None, :]).astype(
        rows.dtype
    )
    placed = jnp.einsum("pk,kbw->pbw", choose, stacked, preferred_element_type=jnp.float32)
    return placed.astype(rows.dtype).reshape(-1, width)


def contract_rows(left_rows, right_rows):
    return lax.dot_general(
        left_rows, right_rows, (((0,), (0,)), ((), ())), preferred_element_type=jnp.float32
    )


def contract_cols(left_rows, right_rows):
    return lax.dot_general(
        left_rows, right_rows, (((1,), (1,)), ((), ())), preferred_element_type=jnp.float32
    )


def block_scores(query_rows, key_rows, query_pos, query_doc, key_pos, key_doc, score_scale):
    scores = contract_cols(query_rows, key_rows) * score_scale
    visible = (query_doc[:, None] == key_doc[None, :]) & (key_pos[None, :] <= query_pos[:, None])
    return (scores, visible)


def body(grad_in, query, keyval, w_qkv, w_out, doc_lengths, order):
    section_grad_in = grad_in[0]
    stored_query = query[0]
    stored_keyval = keyval[0]
    in_weight = w_qkv[0]
    out_weight = w_out[0]
    lengths = doc_lengths[0]
    block_order = order[0]
    ctx_size = lax.axis_size("ctx")
    device = lax.axis_index("ctx")
    local_rows = section_grad_in.shape[0]
    head_dim = stored_keyval.shape[1] // 2
    group = stored_query.shape[1] // head_dim
    per_device = local_rows // BLOCK
    block_count = block_order.shape[0]
    seq_len = local_rows * ctx_size
    first_row = device * local_rows
    score_scale = 1.0 / math.sqrt(head_dim)
    key_block = math.gcd(seq_len, 512)
    key_steps = seq_len // key_block
    within = jnp.arange(BLOCK, dtype=jnp.int32)
    next_weight = lax.all_gather(passed_along_2(in_weight, "pipe", -1), "ctx", axis=0, tiled=True)
    out_grad = jnp.dot(
        section_grad_in,
        lax.all_gather(out_weight, "ctx", axis=0, tiled=True),
        preferred_element_type=jnp.float32,
    ).astype(jnp.bfloat16)
    local_out_grad = out_grad
    seq_query = stored_to_seq(stored_query, block_order, device, ctx_size, per_device)
    side = math.isqrt(ctx_size)
    slot_ids = jnp.arange(block_count, dtype=jnp.int32)
    if side == len(RING_OFFSETS) and per_device == 2:
        gathered = jnp.concatenate(
            [
                ring_gather(stored_keyval[:BLOCK], 0, side),
                ring_gather(stored_keyval[BLOCK:], 1, side),
            ]
        ).reshape(seq_len, 2 * head_dim)
        holder = slot_ids // per_device
        slot_place = jnp.where(
            slot_ids % per_device == 0,
            ring_position(device, holder, 0, side),
            ctx_size + ring_position(device, holder, 1, side),
        )
    else:
        gathered = gathered_rows(stored_keyval, "ctx")
        slot_place = slot_ids
    gathered, grad_source = lax.optimization_barrier((gathered, section_grad_in))
    next_grad_in = passed_along_2(grad_source, "pipe", -1)
    inverse = jnp.sum(
        jnp.where(block_order[None, :] == slot_ids[:, None], slot_place[None, :], 0), axis=1
    )
    all_keyval = gathered.reshape(block_count, BLOCK, 2 * head_dim)[inverse].reshape(
        seq_len, 2 * head_dim
    )
    key_positions = jnp.arange(seq_len, dtype=jnp.int32)
    key_docs = doc_ids(key_positions, lengths)
    query_pos = first_row + jnp.arange(local_rows, dtype=jnp.int32)
    query_doc = doc_ids(query_pos, lengths)
    flat_rows = local_rows * group
    flat_query = seq_query.reshape(flat_rows, head_dim)
    flat_grad = local_out_grad.reshape(flat_rows, head_dim)
    flat_pos = jnp.repeat(query_pos, group)
    flat_doc = jnp.repeat(query_doc, group)
    key_blocks = (
        all_keyval.reshape(key_steps, key_block, 2 * head_dim),
        key_positions.reshape(key_steps, key_block),
        key_docs.reshape(key_steps, key_block),
    )

    def running_total(carried, current):
        row_top, row_total, weighted = carried
        pair_rows, key_pos, key_doc = current
        scores, visible = block_scores(
            flat_query, pair_rows[:, :head_dim], flat_pos, flat_doc, key_pos, key_doc, score_scale
        )
        new_top = jnp.maximum(row_top, jnp.max(jnp.where(visible, scores, MASKED), axis=1))
        rescale = jnp.exp(row_top - new_top)
        weights = jnp.where(visible, jnp.exp(scores - new_top[:, None]), 0.0)
        row_total = row_total * rescale + jnp.sum(weights, axis=1)
        value_wide = pair_rows[:, head_dim:].astype(jnp.float32)
        weighted = weighted * rescale[:, None] + jnp.dot(
            weights, value_wide, precision=lax.Precision.DEFAULT
        )
        return ((new_top, row_total, weighted), None)

    start_top = jnp.full((flat_rows,), MASKED, jnp.float32)
    start_carry = (
        start_top,
        jnp.zeros((flat_rows,), jnp.float32),
        jnp.zeros((flat_rows, head_dim), jnp.float32),
    )
    (row_top, row_total, weighted), unused = lax.scan(running_total, start_carry, key_blocks)
    log_total = row_top + jnp.log(row_total)
    attn_out = weighted / row_total[:, None]
    row_delta = jnp.sum(flat_grad.astype(jnp.float32) * attn_out, axis=1)

    def grad_step(summed, current):
        pair_rows, key_pos, key_doc = current
        scores, visible = block_scores(
            flat_query, pair_rows[:, :head_dim], flat_pos, flat_doc, key_pos, key_doc, score_scale
        )
        attn_prob = jnp.where(visible, jnp.exp(scores - log_total[:, None]), 0.0)
        prob_grad = contract_cols(flat_grad, pair_rows[:, head_dim:])
        score_grad = (score_scale * attn_prob * (prob_grad - row_delta[:, None])).astype(
            jnp.bfloat16
        )
        summed = summed + jnp.dot(
            score_grad, pair_rows[:, :head_dim], preferred_element_type=jnp.float32
        )
        key_term = contract_rows(score_grad, flat_query)
        value_term = contract_rows(attn_prob.astype(jnp.bfloat16), flat_grad)
        return (summed, jnp.concatenate([key_term, value_term], axis=1))

    query_grad_rot, key_terms = lax.scan(
        grad_step, jnp.zeros((flat_rows, head_dim), jnp.float32), key_blocks
    )
    own_positions = first_row + jnp.arange(local_rows, dtype=jnp.int32)
    query_grad = (
        unrotate(query_grad_rot, flat_pos)
        .reshape(local_rows, group * head_dim)
        .astype(jnp.bfloat16)
    )
    next_query_grad = passed_along_2(query_grad, "pipe", -1)
    if side == len(RING_OFFSETS):
        keyval_grad = ring_scatter_sum(key_terms.reshape(seq_len, 2 * head_dim), device, side)
    else:
        keyval_grad = summed_rows(
            key_terms.reshape(seq_len, 2 * head_dim).astype(jnp.bfloat16), "ctx"
        )
    key_grad = unrotate(keyval_grad[:, :head_dim], own_positions).astype(jnp.bfloat16)
    value_grad = keyval_grad[:, head_dim:].astype(jnp.bfloat16)
    next_keyval_grad = passed_along_2(
        jnp.concatenate([key_grad, value_grad], axis=1), "pipe", -1
    )
    next_qkv_grad = jnp.concatenate([next_query_grad, next_keyval_grad], axis=1)
    passed = projected_sum(next_qkv_grad, next_weight, next_grad_in)
    return passed[None]


def solution(mesh):
    return jax.shard_map(
        body,
        mesh=mesh,
        in_specs=(
            P("pipe", "ctx", None),
            P("pipe", "ctx", None),
            P("pipe", "ctx", None),
            P("pipe", "ctx", None),
            P("pipe", "ctx", None),
            P("pipe", None),
            P("pipe", None),
        ),
        out_specs=P("pipe", "ctx", None),
        check_vma=False,
    )
```
